32 devices in a mesh: dp: 4 (over z), ctx: 8 (over y, x, core).
Axes of the slice: x: 2, y: 2, z: 4, core: 2. Of those that a mesh axis runs over, the one named last changes fastest.
Arguments:
- mixed: bfloat16 [4, 1024, 4096], P('dp', 'ctx'), may hold values from -6 to 6
- conv_weight: float32 [4, 4096], replicated, may hold values from -3 to 3
- log_decay: float32 [4, 1024, 16], P('dp', 'ctx'), may hold values from -1 to 0
- write_rate: float32 [4, 1024, 16], P('dp', 'ctx'), may hold values from 0.1 to 0.95
- segment_ids: int32 [4, 1024], P('dp', 'ctx'), may hold values from 0 to 3, never falling along the last dimension, each value on 1 to 512 neighbouring positions
- cotangent: bfloat16 [4, 1024, 2048], P('dp', 'ctx'), may hold values from -6 to 6
Outputs:
- core_out: bfloat16 [4, 1024, 2048], P('dp', 'ctx')
- grad_mixed: bfloat16 [4, 1024, 4096], P('dp', 'ctx')
- grad_decay: float32 [4, 1024, 16], P('dp', 'ctx')
- grad_rate: float32 [4, 1024, 16], P('dp', 'ctx')
- grad_conv: float32 [4, 4096], replicated
The draws below stay inside these ranges and needn't reach their ends.
Inputs may be any that keep to these rules, and one draw needn't show every extreme that they name: `segment_ids`: per sequence, segment numbers never fall along the positions; every number of 0 to 3 occurs, each on at most 512 positions.
All inputs are finite; a program needn't handle non-finite values.
Results may differ from the reference program's by a relative error of at most 0.00105.
Values may be sent and summed in bfloat16 or wider, within the bound.
No kernel may reach another device: no remote copies, remote signals or barrier semaphores. Data moves between devices by JAX's collectives and lax.ppermute only.
A program may use at most 320 MiB of HBM per device.

```python
import math
import jax
import jax.numpy as jnp
import numpy as np
from jax import lax

HK = 8
HV = 16
DK = 128
DV = 128
CONV = 4
BLOCK = 64
DOCS = 4
TOK_DEV = 128
SEQUENCE_COUNT = 4
SEQUENCE_LENGTH = 1024
CH = 4096


def draw_log_decay(key, part):
    key_rows = jax.random.split(key, 7)
    fast_share = 0.5
    fast_heads = jax.random.uniform(key_rows[0], (SEQUENCE_COUNT, 1, HV)) < fast_share
    fast_rate = jnp.exp(jax.random.uniform(key_rows[1], (SEQUENCE_COUNT, 1, HV), minval=math.log(1.0 / 50.0), maxval=math.log(1.0 / 30.0)))
    slow_rate = jnp.exp(jax.random.uniform(key_rows[2], (SEQUENCE_COUNT, 1, HV), minval=math.log(0.1), maxval=math.log(0.6))) / SEQUENCE_LENGTH
    baseline_rate = jnp.where(fast_heads, fast_rate, slow_rate)
    device_multiplier = jnp.exp(jax.random.uniform(key_rows[3], (SEQUENCE_COUNT, SEQUENCE_LENGTH // TOK_DEV, HV), minval=-0.5, maxval=0.5))
    device_multiplier = jnp.repeat(device_multiplier, TOK_DEV, axis=1)
    token_multiplier = jnp.exp(jax.random.uniform(key_rows[4], (SEQUENCE_COUNT, SEQUENCE_LENGTH, HV), minval=-0.4, maxval=0.4))
    spike_locations = jax.random.randint(key_rows[5], (SEQUENCE_COUNT, 2), 0, SEQUENCE_LENGTH)
    token_position = jnp.arange(SEQUENCE_LENGTH)
    spike_mask = jnp.any(token_position[None, :, None] == spike_locations[:, None, :], axis=2).astype(jnp.float32)
    spike_loss = jnp.log(jax.random.uniform(key_rows[6], (SEQUENCE_COUNT, SEQUENCE_LENGTH, 1), minval=0.5, maxval=0.8))
    value_output = -baseline_rate * device_multiplier * token_multiplier + spike_mask[:, :, None] * spike_loss
    return value_output.astype(jnp.float32)


def steps_of(key, shape, cuts, least, top_value):
    factor_of, own = 1.0, jax.random.fold_in(key, 6)
    for dim, shards_of in cuts:
        heights = jnp.exp(jax.random.uniform(jax.random.fold_in(own, dim), (shards_of,), jnp.float32, least / len(cuts), top_value / len(cuts)))
        factor_of = factor_of * jnp.repeat(heights, shape[dim] // shards_of).reshape([-1 if axis == dim else 1 for axis in range(len(shape))])
    return factor_of


def split_up(number_of, total, reach, skew):
    loads = [(1 << 20) // math.isqrt(rank ** skew) + 1 for rank in range(2, number_of + 1)]
    surplus, holding = total - reach - (number_of - 1), [1] * (number_of - 1)
    while surplus > 0:
        movable = [i for i in range(number_of - 1) if holding[i] < reach]
        pool, remaining = sum([loads[i] for i in movable]), surplus
        for i in movable:
            more = min(reach - holding[i], max(1, remaining * loads[i] // pool), surplus)
            holding[i] = holding[i] + more
            surplus = surplus - more
    return np.array([reach] + holding)


def ragged_sizes(key, count, total, bound, slope):
    if count == 2:
        one = jax.random.randint(key, (), max(1, total - bound), min(bound, total - 1) + 1)
        return jnp.stack([one, total - one])
    sizes = jnp.asarray(split_up(count, total, bound, slope), jnp.int32)
    pairs = (count - 1) // 2
    source_of, receiver = sizes[1:1 + 2 * pairs:2], sizes[2:2 + 2 * pairs:2]
    room = jnp.minimum(source_of - 1, bound - receiver)
    moved = jax.random.randint(jax.random.fold_in(key, 1), (pairs,), 0, 1 << 20) % (room + 1)
    sizes = sizes.at[1:1 + 2 * pairs:2].set(source_of - moved).at[2:2 + 2 * pairs:2].set(receiver + moved)
    return sizes[jax.random.permutation(jax.random.fold_in(key, 2), count)]


def centred(own_key, dims, scale, limit, cuts=(), kind=jnp.bfloat16):
    values = scale * jax.random.normal(own_key, dims, jnp.float32)
    if cuts:
        values = values * steps_of(own_key, dims, cuts, -0.22, 0.18)
    return jnp.clip(values, -limit, limit).astype(kind)


def setup_inputs(seed: int = 0) -> dict:
    arg_keys = jax.random.split(jax.random.key(seed), 7)
    mixed = centred(arg_keys[0], (SEQUENCE_COUNT, SEQUENCE_LENGTH, CH), 1.0, 6.0, ((0, 4), (1, 8)))
    conv_weight = centred(arg_keys[1], (CONV, CH), CONV ** -0.5, 3.0, (), jnp.float32)
    log_decay = draw_log_decay(jax.random.fold_in(arg_keys[6], 71), 0)
    write_rate = jnp.clip(0.1 + 0.84999999 * jax.random.uniform(arg_keys[3], (SEQUENCE_COUNT, SEQUENCE_LENGTH, HV), jnp.float32) ** steps_of(arg_keys[3], (SEQUENCE_COUNT, SEQUENCE_LENGTH, HV), ((0, 4), (1, 8)), -0.2, 0.2), 0.1, 0.95)
    segment_ids = jax.vmap(lambda own: jnp.searchsorted(jnp.cumsum(ragged_sizes(own, DOCS, SEQUENCE_LENGTH, SEQUENCE_LENGTH // 2, 1)), jnp.arange(SEQUENCE_LENGTH), side="right"))(jax.random.split(arg_keys[4], SEQUENCE_COUNT)).reshape((SEQUENCE_COUNT, SEQUENCE_LENGTH)).astype(jnp.int32)
    cotangent = centred(arg_keys[5], (SEQUENCE_COUNT, SEQUENCE_LENGTH, HV * DV), 1.0, 6.0, ((0, 4), (1, 8)))
    return {"mixed": mixed, "conv_weight": conv_weight, "log_decay": log_decay, "write_rate": write_rate, "segment_ids": segment_ids, "cotangent": cotangent}


HIGHEST = lax.Precision.HIGHEST

def prepare(mix_ext, seg_ext, conv_weight):
    margin = conv_weight.shape[0] - 1
    positions = mix_ext.shape[0] - margin
    current = seg_ext[margin:]
    summed = jnp.zeros((positions, mix_ext.shape[1]), jnp.float32)
    for tap_index in range(margin + 1):
        same_doc = (seg_ext[tap_index:tap_index + positions] == current).astype(jnp.float32)
        summed = summed + conv_weight[tap_index][None, :] * mix_ext[tap_index:tap_index + positions] * same_doc[:, None]
    activated = jax.nn.silu(summed)
    split_at = HK * DK
    queries = activated[:, :split_at].reshape(positions, HK, DK)
    keyset = activated[:, split_at:2 * split_at].reshape(positions, HK, DK)
    values = activated[:, 2 * split_at:].reshape(positions, HV, DV)
    queries = queries / jnp.sqrt(lax.optimization_barrier(jnp.sum(queries * queries, axis=-1, keepdims=True)) + 1e-06) / math.sqrt(DK)
    keyset = keyset / jnp.sqrt(lax.optimization_barrier(jnp.sum(keyset * keyset, axis=-1, keepdims=True)) + 1e-06)
    repeats = HV // HK
    return (jnp.repeat(queries, repeats, axis=1), jnp.repeat(keyset, repeats, axis=1), values)

def solve_lower(matrix, target):
    return jax.scipy.linalg.solve_triangular(matrix, target, lower=True, unit_diagonal=True)

def block_parts(queries, keyset, values, log_decay, write_rate, segments, seg_before):
    positions = queries.shape[0]
    cumulative = jnp.cumsum(log_decay, axis=0)
    keep_state = (segments == seg_before).astype(jnp.float32)
    entering = jnp.exp(cumulative) * keep_state[:, None]
    token_position = lax.iota(jnp.int32, positions)
    same_doc = segments[:, None] == segments[None, :]
    strict = same_doc & (token_position[:, None] > token_position[None, :])
    causal = same_doc & (token_position[:, None] >= token_position[None, :])
    spread = cumulative.T[:, :, None] - cumulative.T[:, None, :]
    strict_decay = jnp.where(strict[None], jnp.exp(jnp.where(strict[None], spread, 0.0)), 0.0)
    causal_decay = jnp.where(causal[None], jnp.exp(jnp.where(causal[None], spread, 0.0)), 0.0)
    key_inner = jnp.einsum('ihd,jhd->hij', keyset, keyset, precision=HIGHEST)
    system = jnp.eye(positions, dtype=jnp.float32)[None] + write_rate.T[:, :, None] * key_inner * strict_decay
    targets = jnp.concatenate([keyset * (write_rate * entering)[:, :, None], values * write_rate[:, :, None]], axis=2)
    solved = jax.vmap(solve_lower)(system, targets.transpose(1, 0, 2))
    write_keys = solved[:, :, :DK]
    write_values = solved[:, :, DK:]
    scores = jnp.einsum('ihd,jhd->hij', queries, keyset, precision=HIGHEST) * causal_decay
    final_sum = cumulative[-1]
    tail_decay = jnp.exp(final_sum[None, :] - cumulative) * (segments == segments[-1]).astype(jnp.float32)[:, None]
    carried = jnp.exp(final_sum) * keep_state[-1]
    tail_keys = (keyset * tail_decay[:, :, None]).transpose(1, 0, 2)
    queried = (queries * entering[:, :, None]).transpose(1, 0, 2)
    return (write_keys, write_values, scores, tail_keys, queried, carried)

def block_apply(block_data, state_in):
    write_keys, write_values, scores, tail_keys, queried, carried = block_data
    fresh_values = write_values - jnp.einsum('hcd,hde->hce', write_keys, state_in, precision=HIGHEST)
    output = jnp.einsum('hcd,hde->hce', queried, state_in, precision=HIGHEST)
    output = output + jnp.einsum('hij,hje->hie', scores, fresh_values, precision=HIGHEST)
    state_next = carried[:, None, None] * state_in + jnp.einsum('hcd,hce->hde', tail_keys, fresh_values, precision=HIGHEST)
    return (output, state_next)

def section_one(mix_ext, conv_weight, log_decay, write_rate, seg_ext):
    queries, keyset, values = prepare(mix_ext, seg_ext, conv_weight)
    margin = conv_weight.shape[0] - 1
    positions = log_decay.shape[0]
    blocks = positions // BLOCK
    segments = seg_ext[margin:]
    before = seg_ext[margin - 1:margin - 1 + positions:BLOCK]

    def blocked(tensor):
        return tensor.reshape((blocks, BLOCK) + tensor.shape[1:])
    return jax.vmap(block_parts)(blocked(queries), blocked(keyset), blocked(values), blocked(log_decay), blocked(write_rate), blocked(segments), before)

def section_two(parts, state_in):

    def step_block(state_now, block_data):
        output, state_next = block_apply(block_data, state_now)
        return (state_next, output)
    state_out, outputs = lax.scan(step_block, state_in, parts)
    blocks = outputs.shape[0]
    return (outputs.transpose(0, 2, 1, 3).reshape(blocks * BLOCK, HV * DV), state_out)

def reference(mixed, conv_weight, log_decay, write_rate, segment_ids, cotangent):
    margin = conv_weight.shape[0] - 1
    outputs_all = []
    mixed_grads = []
    decay_grads = []
    rate_grads = []
    conv_total = jnp.zeros(conv_weight.shape, jnp.float32)
    for sequence in range(SEQUENCE_COUNT):
        seg_ext = jnp.concatenate([jnp.full((margin,), -1, jnp.int32), segment_ids[sequence].astype(jnp.int32)])

        def forward(mix_in, weight_in, decay_in, rate_in):
            mix_ext = jnp.concatenate([jnp.zeros((margin, CH), jnp.float32), mix_in], axis=0)
            parts = section_one(mix_ext, weight_in, decay_in, rate_in, seg_ext)
            outputs, state_out = section_two(parts, jnp.zeros((HV, DK, DV), jnp.float32))
            return outputs
        outputs, pullback = jax.vjp(forward, mixed[sequence].astype(jnp.float32), conv_weight, log_decay[sequence], write_rate[sequence])
        grads = pullback(cotangent[sequence].astype(jnp.float32))
        outputs_all.append(outputs.astype(jnp.bfloat16))
        mixed_grads.append(grads[0].astype(jnp.bfloat16))
        conv_total = conv_total + grads[1]
        decay_grads.append(grads[2])
        rate_grads.append(grads[3])
    scale = 1.0 / math.sqrt(SEQUENCE_COUNT * SEQUENCE_LENGTH)
    return (jnp.stack(outputs_all), jnp.stack(mixed_grads), jnp.stack(decay_grads), jnp.stack(rate_grads), conv_total * scale)
```

```python
import math

import jax
import jax.numpy as jnp
from jax import lax
from jax.sharding import PartitionSpec as P

HK = 8
HV = 16
DK = 128
DV = 128
BLOCK = 64


HIGHEST = lax.Precision.HIGHEST


def from_behind(x, axis, by):
    size = lax.axis_size(axis)
    pairs = [(i, i + by) for i in range(size) if 0 <= i + by < size]
    return lax.ppermute(x, axis, pairs)


def prefix(value, axis, join, neutral, backward):
    count, mine = (lax.axis_size(axis), lax.axis_index(axis))
    pieces = jax.tree.map(lambda part: lax.all_gather(part, axis), value)
    if backward:
        pieces = jax.tree.map(lambda part: part[::-1], pieces)
        mine = count - 1 - mine
    total = jax.tree.map(
        lambda part, zero: jnp.full_like(part, 0) + jnp.asarray(zero, part.dtype), value, neutral
    )

    def hop(position, total):
        longer = join(total, jax.tree.map(lambda part: part[position], pieces))
        return jax.tree.map(lambda new, old: jnp.where(position < mine, new, old), longer, total)

    return lax.fori_loop(0, count - 1, hop, total)


def prepare(mix_ext, seg_ext, conv_weight):
    margin = conv_weight.shape[0] - 1
    positions = mix_ext.shape[0] - margin
    current = seg_ext[margin:]
    summed = jnp.zeros((positions, mix_ext.shape[1]), jnp.float32)
    for tap_index in range(margin + 1):
        same_doc = (seg_ext[tap_index : tap_index + positions] == current).astype(jnp.float32)
        summed = (
            summed
            + conv_weight[tap_index][None, :]
            * mix_ext[tap_index : tap_index + positions]
            * same_doc[:, None]
        )
    activated = jax.nn.silu(summed)
    split_at = HK * DK
    queries = activated[:, :split_at].reshape(positions, HK, DK)
    keyset = activated[:, split_at : 2 * split_at].reshape(positions, HK, DK)
    values = activated[:, 2 * split_at :].reshape(positions, HV, DV)
    queries = (
        queries
        / jnp.sqrt(jnp.sum(queries * queries, axis=-1, keepdims=True) + 1e-06)
        / math.sqrt(DK)
    )
    keyset = keyset / jnp.sqrt(jnp.sum(keyset * keyset, axis=-1, keepdims=True) + 1e-06)
    repeats = HV // HK
    return (jnp.repeat(queries, repeats, axis=1), jnp.repeat(keyset, repeats, axis=1), values)


def unit_lower_inverse(strict_part):
    positions = strict_part.shape[-1]
    identity_matrix = jnp.eye(positions, dtype=jnp.float32)[None]
    result = identity_matrix - strict_part
    power = strict_part
    reach = 2
    while reach < positions:
        power = jnp.einsum("hij,hjk->hik", power, power, precision=HIGHEST)
        result = jnp.einsum("hij,hjk->hik", result, identity_matrix + power, precision=HIGHEST)
        reach = reach * 2
    return result


def block_parts(queries, keyset, values, log_decay, write_rate, segments, seg_before):
    positions = queries.shape[0]
    cumulative = jnp.cumsum(log_decay, axis=0)
    keep_state = (segments == seg_before).astype(jnp.float32)
    entering = jnp.exp(cumulative) * keep_state[:, None]
    token_position = lax.iota(jnp.int32, positions)
    same_doc = segments[:, None] == segments[None, :]
    strict = same_doc & (token_position[:, None] > token_position[None, :])
    causal = same_doc & (token_position[:, None] >= token_position[None, :])
    spread = cumulative.T[:, :, None] - cumulative.T[:, None, :]
    strict_decay = jnp.where(strict[None], jnp.exp(jnp.where(strict[None], spread, 0.0)), 0.0)
    causal_decay = jnp.where(causal[None], jnp.exp(jnp.where(causal[None], spread, 0.0)), 0.0)
    key_inner = jnp.einsum("ihd,jhd->hij", keyset, keyset, precision=HIGHEST)
    inverse = unit_lower_inverse(write_rate.T[:, :, None] * key_inner * strict_decay)
    targets = jnp.concatenate(
        [keyset * (write_rate * entering)[:, :, None], values * write_rate[:, :, None]], axis=2
    )
    solved = jnp.einsum("hij,hjd->hid", inverse, targets.transpose(1, 0, 2), precision=HIGHEST)
    write_keys = solved[:, :, :DK]
    write_values = solved[:, :, DK:]
    scores = jnp.einsum("ihd,jhd->hij", queries, keyset, precision=HIGHEST) * causal_decay
    final_sum = cumulative[-1]
    tail_decay = (
        jnp.exp(final_sum[None, :] - cumulative)
        * (segments == segments[-1]).astype(jnp.float32)[:, None]
    )
    carried = jnp.exp(final_sum) * keep_state[-1]
    tail_keys = (keyset * tail_decay[:, :, None]).transpose(1, 0, 2)
    queried = (queries * entering[:, :, None]).transpose(1, 0, 2)
    return (write_keys, write_values, scores, tail_keys, queried, carried)


def block_map(block_data):
    write_keys, write_values, scores, tail_keys, queried, carried = block_data
    identity_matrix = jnp.eye(DK, dtype=jnp.float32)
    transform = carried[:, None, None] * identity_matrix[None] - jnp.einsum(
        "hcd,hce->hde", tail_keys, write_keys, precision=HIGHEST
    )
    shift_term = jnp.einsum("hcd,hce->hde", tail_keys, write_values, precision=HIGHEST)
    return (transform, shift_term)


def block_apply(block_data, state_in):
    write_keys, write_values, scores, tail_keys, queried, carried = block_data
    fresh_values = write_values - jnp.einsum(
        "hcd,hde->hce", write_keys, state_in, precision=HIGHEST
    )
    output = jnp.einsum("hcd,hde->hce", queried, state_in, precision=HIGHEST)
    output = output + jnp.einsum("hij,hje->hie", scores, fresh_values, precision=HIGHEST)
    state_next = carried[:, None, None] * state_in + jnp.einsum(
        "hcd,hce->hde", tail_keys, fresh_values, precision=HIGHEST
    )
    return (output, state_next)


def section_one(mix_ext, conv_weight, log_decay, write_rate, seg_ext):
    queries, keyset, values = prepare(mix_ext, seg_ext, conv_weight)
    margin = conv_weight.shape[0] - 1
    positions = log_decay.shape[0]
    blocks = positions // BLOCK
    segments = seg_ext[margin:]
    before = seg_ext[margin - 1 : margin - 1 + positions : BLOCK]

    def blocked(tensor):
        return tensor.reshape((blocks, BLOCK) + tensor.shape[1:])

    return jax.vmap(block_parts)(
        blocked(queries),
        blocked(keyset),
        blocked(values),
        blocked(log_decay),
        blocked(write_rate),
        blocked(segments),
        before,
    )


def section_two(parts, state_in):

    def step_block(state_now, block_data):
        output, state_next = block_apply(block_data, state_now)
        return (state_next, output)

    state_out, outputs = lax.scan(step_block, state_in, parts)
    blocks = outputs.shape[0]
    return (outputs.transpose(0, 2, 1, 3).reshape(blocks * BLOCK, HV * DV), state_out)


def summarize(parts):
    identity_matrix = jnp.eye(DK, dtype=jnp.float32)
    initial = (
        jnp.broadcast_to(identity_matrix, (HV, DK, DK)),
        jnp.zeros((HV, DK, DV), jnp.float32),
    )

    def fold_block(carried_map, block_data):
        transform, shift_term = block_map(block_data)
        merged = jnp.einsum("hij,hjk->hik", transform, carried_map[0], precision=HIGHEST)
        moved = (
            jnp.einsum("hij,hjk->hik", transform, carried_map[1], precision=HIGHEST) + shift_term
        )
        return ((merged, moved), None)

    result, unused = lax.scan(fold_block, initial, parts)
    return result


def compose(earlier_map, later_map):
    merged = jnp.einsum("shij,shjk->shik", later_map[0], earlier_map[0], precision=HIGHEST)
    moved = (
        jnp.einsum("shij,shjk->shik", later_map[0], earlier_map[1], precision=HIGHEST)
        + later_map[1]
    )
    return (merged, moved)


def local(mixed, conv_weight, log_decay, write_rate, segment_ids, cotangent):
    margin = conv_weight.shape[0] - 1
    shifted_rows, shifted_segs = from_behind(
        (mixed[:, -margin:, :], segment_ids[:, -margin:].astype(jnp.bfloat16)), "ctx", 1
    )
    mix_ext = jnp.concatenate([shifted_rows, mixed], axis=1).astype(jnp.float32)
    seg_ext = jnp.concatenate([shifted_segs.astype(jnp.int32), segment_ids], axis=1)

    def first_section(mix_in, weight_in, decay_in, rate_in):
        return jax.vmap(section_one, in_axes=(0, None, 0, 0, 0))(
            mix_in, weight_in, decay_in, rate_in, seg_ext
        )

    parts, first_pull = jax.vjp(first_section, mix_ext, conv_weight, log_decay, write_rate)
    transform, shift_term = jax.vmap(summarize)(parts)
    identity_pair = (
        jnp.broadcast_to(jnp.eye(transform.shape[-1], dtype=jnp.float32), transform.shape),
        jnp.zeros_like(shift_term),
    )
    incoming = prefix((transform, shift_term), "ctx", compose, identity_pair, False)[1]
    (outputs, leaving), second_pull = jax.vjp(jax.vmap(section_two), parts, incoming)
    part_grads, local_term = second_pull((cotangent.astype(jnp.float32), jnp.zeros_like(leaving)))
    flipped = jnp.swapaxes(transform, -1, -2)
    departing = prefix((flipped, local_term), "ctx", compose, identity_pair, True)[1]
    more_grads, unused_grad = second_pull((jnp.zeros_like(outputs), departing))
    total_parts = jax.tree.map(jnp.add, part_grads, more_grads)
    grad_mix, grad_weight, grad_decay, grad_rate = first_pull(total_parts)
    returned = from_behind(grad_mix[:, :margin, :].astype(jnp.bfloat16), "ctx", -1).astype(
        jnp.float32
    )
    own_grad = grad_mix[:, margin:, :]
    own_grad = jnp.concatenate(
        [own_grad[:, :-margin, :], own_grad[:, -margin:, :] + returned], axis=1
    )
    total_conv = lax.psum(grad_weight, ("dp", "ctx"))
    tokens_all = mixed.shape[0] * lax.axis_size("dp") * mixed.shape[1] * lax.axis_size("ctx")
    return (
        outputs.astype(jnp.bfloat16),
        own_grad.astype(jnp.bfloat16),
        grad_decay,
        grad_rate,
        total_conv / math.sqrt(tokens_all),
    )


def tree_sum(value, axis):
    count = lax.axis_size(axis)
    if count & (count - 1):
        return lax.psum(value, axis)
    step = 1
    while step < count:
        value = value + lax.ppermute(value, axis, [(i, i ^ step) for i in range(count)])
        step = step * 2
    return value


def prepare_heads(mix_ext, seg_ext, conv_weight, key_heads, value_heads):
    margin = conv_weight.shape[0] - 1
    positions = mix_ext.shape[0] - margin
    current = seg_ext[margin:]
    summed = jnp.zeros((positions, mix_ext.shape[1]), jnp.float32)
    for tap_index in range(margin + 1):
        same_doc = (seg_ext[tap_index : tap_index + positions] == current).astype(jnp.float32)
        summed = (
            summed
            + conv_weight[tap_index][None, :]
            * mix_ext[tap_index : tap_index + positions]
            * same_doc[:, None]
        )
    activated = jax.nn.silu(summed)
    split_at = key_heads * DK
    queries = activated[:, :split_at].reshape(positions, key_heads, DK)
    keyset = activated[:, split_at : 2 * split_at].reshape(positions, key_heads, DK)
    values = activated[:, 2 * split_at :].reshape(positions, value_heads, DV)
    queries = (
        queries
        / jnp.sqrt(jnp.sum(queries * queries, axis=-1, keepdims=True) + 1e-06)
        / math.sqrt(DK)
    )
    keyset = keyset / jnp.sqrt(jnp.sum(keyset * keyset, axis=-1, keepdims=True) + 1e-06)
    repeats = value_heads // key_heads
    return (jnp.repeat(queries, repeats, axis=1), jnp.repeat(keyset, repeats, axis=1), values)


def combine_maps(earlier, later):
    merged = jnp.einsum("...ij,...jk->...ik", later[0], earlier[0], precision=HIGHEST)
    moved = jnp.einsum("...ij,...jk->...ik", later[0], earlier[1], precision=HIGHEST) + later[1]
    return (merged, moved)


def heads_forward(mix_in, weight_in, decay_in, rate_in, seg_ext, key_heads, value_heads):
    margin = weight_in.shape[0] - 1
    positions = decay_in.shape[0]
    blocks = positions // BLOCK
    mix_ext = jnp.concatenate([jnp.zeros((margin, mix_in.shape[1]), jnp.float32), mix_in], axis=0)
    queries, keyset, values = prepare_heads(mix_ext, seg_ext, weight_in, key_heads, value_heads)
    segments = seg_ext[margin:]
    before = seg_ext[margin - 1 : margin - 1 + positions : BLOCK]

    def blocked(tensor):
        return tensor.reshape((blocks, BLOCK) + tensor.shape[1:])

    parts = jax.vmap(block_parts)(
        blocked(queries),
        blocked(keyset),
        blocked(values),
        blocked(decay_in),
        blocked(rate_in),
        blocked(segments),
        before,
    )
    transform, shift_term = jax.vmap(block_map)(parts)
    inclusive = lax.associative_scan(combine_maps, (transform, shift_term))[1]
    incoming = jnp.concatenate([jnp.zeros_like(inclusive[:1]), inclusive[:-1]], axis=0)
    outputs, unused = jax.vmap(block_apply)(parts, incoming)
    return outputs.transpose(0, 2, 1, 3).reshape(positions, value_heads * DV)


def heads_local(mixed, conv_weight, log_decay, write_rate, segment_ids, cotangent):
    if mixed.shape[0] != 1:
        return local(mixed, conv_weight, log_decay, write_rate, segment_ids, cotangent)
    count = lax.axis_size("ctx")
    mine = lax.axis_index("ctx")
    value_heads = HV // count
    key_heads = value_heads * HK // HV
    margin = conv_weight.shape[0] - 1
    rows = mixed.shape[1]
    length = rows * count
    qk_width = key_heads * DK
    v_width = value_heads * DV

    def to_heads(array, width):
        grouped = array.reshape(rows, count, width)
        return lax.all_to_all(grouped, "ctx", 1, 0, tiled=True).reshape(length, width)

    def to_rows(array, width):
        grouped = array.reshape(count, rows, 1, width)
        return lax.all_to_all(grouped, "ctx", 0, 2, tiled=True).reshape(rows, count, width)

    own = mixed[0]
    packed = jnp.concatenate(
        [
            own[:, : HK * DK].reshape(rows, count, qk_width),
            own[:, HK * DK : 2 * HK * DK].reshape(rows, count, qk_width),
            own[:, 2 * HK * DK :].reshape(rows, count, v_width),
        ],
        axis=-1,
    )
    width = 2 * qk_width + v_width
    mix_heads = to_heads(packed, width).astype(jnp.float32)
    decay_heads = to_heads(log_decay[0], value_heads)
    rate_heads = to_heads(write_rate[0], value_heads)
    cot_heads = to_heads(cotangent[0], v_width).astype(jnp.float32)
    segments = lax.all_gather(segment_ids[0], "ctx", tiled=True)
    seg_ext = jnp.concatenate([jnp.full((margin,), -1, jnp.int32), segments.astype(jnp.int32)])

    weight_q = conv_weight[:, : HK * DK].reshape(-1, count, qk_width)[:, mine]
    weight_k = conv_weight[:, HK * DK : 2 * HK * DK].reshape(-1, count, qk_width)[:, mine]
    weight_v = conv_weight[:, 2 * HK * DK :].reshape(-1, count, v_width)[:, mine]
    weight_heads = jnp.concatenate([weight_q, weight_k, weight_v], axis=-1)

    def forward(mix_in, weight_in, decay_in, rate_in):
        return heads_forward(
            mix_in, weight_in, decay_in, rate_in, seg_ext, key_heads, value_heads
        )

    outputs, pullback = jax.vjp(forward, mix_heads, weight_heads, decay_heads, rate_heads)
    grad_mix, grad_weight, grad_decay, grad_rate = pullback(cot_heads)

    core = to_rows(outputs.astype(jnp.bfloat16), v_width).reshape(1, rows, HV * DV)
    back = to_rows(grad_mix.astype(jnp.bfloat16), width)
    grad_rows = jnp.concatenate(
        [
            back[:, :, :qk_width].reshape(rows, HK * DK),
            back[:, :, qk_width : 2 * qk_width].reshape(rows, HK * DK),
            back[:, :, 2 * qk_width :].reshape(rows, HV * DV),
        ],
        axis=-1,
    )[None]
    decay_rows = to_rows(grad_decay, value_heads).reshape(1, rows, HV)
    rate_rows = to_rows(grad_rate, value_heads).reshape(1, rows, HV)

    taps = conv_weight.shape[0]

    def place(part, total_width, part_width):
        slots = jnp.zeros((taps, count, part_width), jnp.float32)
        slots = lax.dynamic_update_slice(slots, part[:, None, :], (0, mine, 0))
        return slots.reshape(taps, total_width)

    placed = jnp.concatenate(
        [
            place(grad_weight[:, :qk_width], HK * DK, qk_width),
            place(grad_weight[:, qk_width : 2 * qk_width], HK * DK, qk_width),
            place(grad_weight[:, 2 * qk_width :], HV * DV, v_width),
        ],
        axis=-1,
    )
    total_conv = tree_sum(tree_sum(placed, "ctx"), "dp")
    tokens_all = mixed.shape[0] * lax.axis_size("dp") * length
    return (core, grad_rows, decay_rows, rate_rows, total_conv / math.sqrt(tokens_all))


def solution(mesh):
    in_specs = (
        P("dp", "ctx", None),
        P(),
        P("dp", "ctx", None),
        P("dp", "ctx", None),
        P("dp", "ctx"),
        P("dp", "ctx", None),
    )
    out_specs = (
        P("dp", "ctx", None),
        P("dp", "ctx", None),
        P("dp", "ctx", None),
        P("dp", "ctx", None),
        P(),
    )
    count = mesh.shape["ctx"]
    per_device = HV // count if HV % count == 0 else 0
    chosen = heads_local if per_device and (per_device * HK) % HV == 0 else local
    return jax.shard_map(chosen, mesh=mesh, in_specs=in_specs, out_specs=out_specs, check_vma=False)
```

```python
import math

import jax
import jax.numpy as jnp
from jax import lax
from jax.sharding import PartitionSpec as P

HK = 8
HV = 16
DK = 128
DV = 128
BLOCK = 64


HIGHEST = lax.Precision.HIGHEST


def from_behind(x, axis, by):
    size = lax.axis_size(axis)
    pairs = [(i, i + by) for i in range(size) if 0 <= i + by < size]
    return lax.ppermute(x, axis, pairs)


def prefix(value, axis, join, neutral, backward):
    count, mine = (lax.axis_size(axis), lax.axis_index(axis))
    pieces = jax.tree.map(lambda part: lax.all_gather(part, axis), value)
    if backward:
        pieces = jax.tree.map(lambda part: part[::-1], pieces)
        mine = count - 1 - mine
    total = jax.tree.map(
        lambda part, zero: jnp.full_like(part, 0) + jnp.asarray(zero, part.dtype), value, neutral
    )

    def hop(position, total):
        longer = join(total, jax.tree.map(lambda part: part[position], pieces))
        return jax.tree.map(lambda new, old: jnp.where(position < mine, new, old), longer, total)

    return lax.fori_loop(0, count - 1, hop, total)


def prepare(mix_ext, seg_ext, conv_weight):
    margin = conv_weight.shape[0] - 1
    positions = mix_ext.shape[0] - margin
    current = seg_ext[margin:]
    summed = jnp.zeros((positions, mix_ext.shape[1]), jnp.float32)
    for tap_index in range(margin + 1):
        same_doc = (seg_ext[tap_index : tap_index + positions] == current).astype(jnp.float32)
        summed = (
            summed
            + conv_weight[tap_index][None, :]
            * mix_ext[tap_index : tap_index + positions]
            * same_doc[:, None]
        )
    activated = jax.nn.silu(summed)
    split_at = HK * DK
    queries = activated[:, :split_at].reshape(positions, HK, DK)
    keyset = activated[:, split_at : 2 * split_at].reshape(positions, HK, DK)
    values = activated[:, 2 * split_at :].reshape(positions, HV, DV)
    queries = (
        queries
        / jnp.sqrt(jnp.sum(queries * queries, axis=-1, keepdims=True) + 1e-06)
        / math.sqrt(DK)
    )
    keyset = keyset / jnp.sqrt(jnp.sum(keyset * keyset, axis=-1, keepdims=True) + 1e-06)
    repeats = HV // HK
    return (jnp.repeat(queries, repeats, axis=1), jnp.repeat(keyset, repeats, axis=1), values)


def unit_lower_inverse(strict_part):
    positions = strict_part.shape[-1]
    identity_matrix = jnp.eye(positions, dtype=jnp.float32)[None]
    result = identity_matrix - strict_part
    power = strict_part
    reach = 2
    while reach < positions:
        power = jnp.einsum("hij,hjk->hik", power, power, precision=HIGHEST)
        result = jnp.einsum("hij,hjk->hik", result, identity_matrix + power, precision=HIGHEST)
        reach = reach * 2
    return result


def block_parts(queries, keyset, values, log_decay, write_rate, segments, seg_before):
    positions = queries.shape[0]
    cumulative = jnp.cumsum(log_decay, axis=0)
    keep_state = (segments == seg_before).astype(jnp.float32)
    entering = jnp.exp(cumulative) * keep_state[:, None]
    token_position = lax.iota(jnp.int32, positions)
    same_doc = segments[:, None] == segments[None, :]
    strict = same_doc & (token_position[:, None] > token_position[None, :])
    causal = same_doc & (token_position[:, None] >= token_position[None, :])
    spread = cumulative.T[:, :, None] - cumulative.T[:, None, :]
    strict_decay = jnp.where(strict[None], jnp.exp(jnp.where(strict[None], spread, 0.0)), 0.0)
    causal_decay = jnp.where(causal[None], jnp.exp(jnp.where(causal[None], spread, 0.0)), 0.0)
    key_inner = jnp.einsum("ihd,jhd->hij", keyset, keyset, precision=HIGHEST)
    inverse = unit_lower_inverse(write_rate.T[:, :, None] * key_inner * strict_decay)
    targets = jnp.concatenate(
        [keyset * (write_rate * entering)[:, :, None], values * write_rate[:, :, None]], axis=2
    )
    solved = jnp.einsum("hij,hjd->hid", inverse, targets.transpose(1, 0, 2), precision=HIGHEST)
    write_keys = solved[:, :, :DK]
    write_values = solved[:, :, DK:]
    scores = jnp.einsum("ihd,jhd->hij", queries, keyset, precision=HIGHEST) * causal_decay
    final_sum = cumulative[-1]
    tail_decay = (
        jnp.exp(final_sum[None, :] - cumulative)
        * (segments == segments[-1]).astype(jnp.float32)[:, None]
    )
    carried = jnp.exp(final_sum) * keep_state[-1]
    tail_keys = (keyset * tail_decay[:, :, None]).transpose(1, 0, 2)
    queried = (queries * entering[:, :, None]).transpose(1, 0, 2)
    return (write_keys, write_values, scores, tail_keys, queried, carried)


def block_map(block_data):
    write_keys, write_values, scores, tail_keys, queried, carried = block_data
    identity_matrix = jnp.eye(DK, dtype=jnp.float32)
    transform = carried[:, None, None] * identity_matrix[None] - jnp.einsum(
        "hcd,hce->hde", tail_keys, write_keys, precision=HIGHEST
    )
    shift_term = jnp.einsum("hcd,hce->hde", tail_keys, write_values, precision=HIGHEST)
    return (transform, shift_term)


def block_apply(block_data, state_in):
    write_keys, write_values, scores, tail_keys, queried, carried = block_data
    fresh_values = write_values - jnp.einsum(
        "hcd,hde->hce", write_keys, state_in, precision=HIGHEST
    )
    output = jnp.einsum("hcd,hde->hce", queried, state_in, precision=HIGHEST)
    output = output + jnp.einsum("hij,hje->hie", scores, fresh_values, precision=HIGHEST)
    state_next = carried[:, None, None] * state_in + jnp.einsum(
        "hcd,hce->hde", tail_keys, fresh_values, precision=HIGHEST
    )
    return (output, state_next)


def section_one(mix_ext, conv_weight, log_decay, write_rate, seg_ext):
    queries, keyset, values = prepare(mix_ext, seg_ext, conv_weight)
    margin = conv_weight.shape[0] - 1
    positions = log_decay.shape[0]
    blocks = positions // BLOCK
    segments = seg_ext[margin:]
    before = seg_ext[margin - 1 : margin - 1 + positions : BLOCK]

    def blocked(tensor):
        return tensor.reshape((blocks, BLOCK) + tensor.shape[1:])

    return jax.vmap(block_parts)(
        blocked(queries),
        blocked(keyset),
        blocked(values),
        blocked(log_decay),
        blocked(write_rate),
        blocked(segments),
        before,
    )


def section_two(parts, state_in):

    def step_block(state_now, block_data):
        output, state_next = block_apply(block_data, state_now)
        return (state_next, output)

    state_out, outputs = lax.scan(step_block, state_in, parts)
    blocks = outputs.shape[0]
    return (outputs.transpose(0, 2, 1, 3).reshape(blocks * BLOCK, HV * DV), state_out)


def summarize(parts):
    identity_matrix = jnp.eye(DK, dtype=jnp.float32)
    initial = (
        jnp.broadcast_to(identity_matrix, (HV, DK, DK)),
        jnp.zeros((HV, DK, DV), jnp.float32),
    )

    def fold_block(carried_map, block_data):
        transform, shift_term = block_map(block_data)
        merged = jnp.einsum("hij,hjk->hik", transform, carried_map[0], precision=HIGHEST)
        moved = (
            jnp.einsum("hij,hjk->hik", transform, carried_map[1], precision=HIGHEST) + shift_term
        )
        return ((merged, moved), None)

    result, unused = lax.scan(fold_block, initial, parts)
    return result


def compose(earlier_map, later_map):
    merged = jnp.einsum("shij,shjk->shik", later_map[0], earlier_map[0], precision=HIGHEST)
    moved = (
        jnp.einsum("shij,shjk->shik", later_map[0], earlier_map[1], precision=HIGHEST)
        + later_map[1]
    )
    return (merged, moved)


def local(mixed, conv_weight, log_decay, write_rate, segment_ids, cotangent):
    margin = conv_weight.shape[0] - 1
    shifted_rows, shifted_segs = from_behind(
        (mixed[:, -margin:, :], segment_ids[:, -margin:].astype(jnp.bfloat16)), "ctx", 1
    )
    mix_ext = jnp.concatenate([shifted_rows, mixed], axis=1).astype(jnp.float32)
    seg_ext = jnp.concatenate([shifted_segs.astype(jnp.int32), segment_ids], axis=1)

    def first_section(mix_in, weight_in, decay_in, rate_in):
        return jax.vmap(section_one, in_axes=(0, None, 0, 0, 0))(
            mix_in, weight_in, decay_in, rate_in, seg_ext
        )

    parts, first_pull = jax.vjp(first_section, mix_ext, conv_weight, log_decay, write_rate)
    transform, shift_term = jax.vmap(summarize)(parts)
    identity_pair = (
        jnp.broadcast_to(jnp.eye(transform.shape[-1], dtype=jnp.float32), transform.shape),
        jnp.zeros_like(shift_term),
    )
    incoming = prefix((transform, shift_term), "ctx", compose, identity_pair, False)[1]
    (outputs, leaving), second_pull = jax.vjp(jax.vmap(section_two), parts, incoming)
    part_grads, local_term = second_pull((cotangent.astype(jnp.float32), jnp.zeros_like(leaving)))
    flipped = jnp.swapaxes(transform, -1, -2)
    departing = prefix((flipped, local_term), "ctx", compose, identity_pair, True)[1]
    more_grads, unused_grad = second_pull((jnp.zeros_like(outputs), departing))
    total_parts = jax.tree.map(jnp.add, part_grads, more_grads)
    grad_mix, grad_weight, grad_decay, grad_rate = first_pull(total_parts)
    returned = from_behind(grad_mix[:, :margin, :].astype(jnp.bfloat16), "ctx", -1).astype(
        jnp.float32
    )
    own_grad = grad_mix[:, margin:, :]
    own_grad = jnp.concatenate(
        [own_grad[:, :-margin, :], own_grad[:, -margin:, :] + returned], axis=1
    )
    total_conv = lax.psum(grad_weight, ("dp", "ctx"))
    tokens_all = mixed.shape[0] * lax.axis_size("dp") * mixed.shape[1] * lax.axis_size("ctx")
    return (
        outputs.astype(jnp.bfloat16),
        own_grad.astype(jnp.bfloat16),
        grad_decay,
        grad_rate,
        total_conv / math.sqrt(tokens_all),
    )


def tree_sum(value, axis):
    count = lax.axis_size(axis)
    if count & (count - 1):
        return lax.psum(value, axis)
    step = 1
    while step < count:
        value = value + lax.ppermute(value, axis, [(i, i ^ step) for i in range(count)])
        step = step * 2
    return value


def prepare_heads(mix_ext, seg_ext, conv_weight, key_heads, value_heads):
    margin = conv_weight.shape[0] - 1
    positions = mix_ext.shape[0] - margin
    current = seg_ext[margin:]
    summed = jnp.zeros((positions, mix_ext.shape[1]), jnp.float32)
    for tap_index in range(margin + 1):
        same_doc = (seg_ext[tap_index : tap_index + positions] == current).astype(jnp.float32)
        summed = (
            summed
            + conv_weight[tap_index][None, :]
            * mix_ext[tap_index : tap_index + positions]
            * same_doc[:, None]
        )
    activated = jax.nn.silu(summed)
    split_at = key_heads * DK
    queries = activated[:, :split_at].reshape(positions, key_heads, DK)
    keyset = activated[:, split_at : 2 * split_at].reshape(positions, key_heads, DK)
    values = activated[:, 2 * split_at :].reshape(positions, value_heads, DV)
    queries = (
        queries
        / jnp.sqrt(jnp.sum(queries * queries, axis=-1, keepdims=True) + 1e-06)
        / math.sqrt(DK)
    )
    keyset = keyset / jnp.sqrt(jnp.sum(keyset * keyset, axis=-1, keepdims=True) + 1e-06)
    repeats = value_heads // key_heads
    return (jnp.repeat(queries, repeats, axis=1), jnp.repeat(keyset, repeats, axis=1), values)


def combine_maps(earlier, later):
    merged = jnp.einsum("...ij,...jk->...ik", later[0], earlier[0], precision=HIGHEST)
    moved = jnp.einsum("...ij,...jk->...ik", later[0], earlier[1], precision=HIGHEST) + later[1]
    return (merged, moved)


def inclusive_states(transform, shift_term):
    blocks = transform.shape[0]
    reach = 1
    while reach < blocks:
        moved = jnp.einsum(
            "bhij,bhjk->bhik", transform[reach:], shift_term[:-reach], precision=HIGHEST
        )
        shift_term = jnp.concatenate([shift_term[:reach], shift_term[reach:] + moved], axis=0)
        if 2 * reach < blocks:
            merged = jnp.einsum(
                "bhij,bhjk->bhik", transform[reach:], transform[:-reach], precision=HIGHEST
            )
            transform = jnp.concatenate([transform[:reach], merged], axis=0)
        reach = reach * 2
    return shift_term


@jax.custom_vjp
def entering_states(transform, shift_term):
    return entering_forward(transform, shift_term)[0]


def entering_forward(transform, shift_term):
    eye = jnp.broadcast_to(jnp.eye(transform.shape[-1], dtype=transform.dtype), transform[:1].shape)
    shifted_maps = jnp.concatenate([eye, transform[:-1]], axis=0)
    shifted_terms = jnp.concatenate([jnp.zeros_like(shift_term[:1]), shift_term[:-1]], axis=0)
    states = inclusive_states(shifted_maps, shifted_terms)
    return states, (transform, states)


def entering_backward(saved, grad_states):
    transform, states = saved
    flipped = jnp.swapaxes(transform, -1, -2)[::-1]
    total = inclusive_states(flipped, grad_states[::-1])[::-1]
    later = total[1:]
    grad_shift = jnp.concatenate([later, jnp.zeros_like(later[:1])], axis=0)
    grad_map = jnp.einsum("bhik,bhjk->bhij", later, states[:-1], precision=HIGHEST)
    grad_transform = jnp.concatenate([grad_map, jnp.zeros_like(transform[:1])], axis=0)
    return (grad_transform, grad_shift)


entering_states.defvjp(entering_forward, entering_backward)


def heads_forward(mix_in, weight_in, decay_in, rate_in, seg_ext, key_heads, value_heads):
    margin = weight_in.shape[0] - 1
    positions = decay_in.shape[0]
    blocks = positions // BLOCK
    mix_ext = jnp.concatenate([jnp.zeros((margin, mix_in.shape[1]), jnp.float32), mix_in], axis=0)
    queries, keyset, values = prepare_heads(mix_ext, seg_ext, weight_in, key_heads, value_heads)
    segments = seg_ext[margin:]
    before = seg_ext[margin - 1 : margin - 1 + positions : BLOCK]

    def blocked(tensor):
        return tensor.reshape((blocks, BLOCK) + tensor.shape[1:])

    parts = jax.vmap(block_parts)(
        blocked(queries),
        blocked(keyset),
        blocked(values),
        blocked(decay_in),
        blocked(rate_in),
        blocked(segments),
        before,
    )
    transform, shift_term = jax.vmap(block_map)(parts)
    incoming = entering_states(transform, shift_term)
    outputs, unused = jax.vmap(block_apply)(parts, incoming)
    return outputs.transpose(0, 2, 1, 3).reshape(positions, value_heads * DV)


def heads_local(mixed, conv_weight, log_decay, write_rate, segment_ids, cotangent):
    if mixed.shape[0] != 1:
        return local(mixed, conv_weight, log_decay, write_rate, segment_ids, cotangent)
    count = lax.axis_size("ctx")
    mine = lax.axis_index("ctx")
    value_heads = HV // count
    key_heads = value_heads * HK // HV
    margin = conv_weight.shape[0] - 1
    rows = mixed.shape[1]
    length = rows * count
    qk_width = key_heads * DK
    v_width = value_heads * DV

    def to_heads(array, width):
        grouped = array.reshape(rows, count, width)
        return lax.all_to_all(grouped, "ctx", 1, 0, tiled=True).reshape(length, width)

    def to_rows(array, width):
        grouped = array.reshape(count, rows, 1, width)
        return lax.all_to_all(grouped, "ctx", 0, 2, tiled=True).reshape(rows, count, width)

    own = mixed[0]
    packed = jnp.concatenate(
        [
            own[:, : HK * DK].reshape(rows, count, qk_width),
            own[:, HK * DK : 2 * HK * DK].reshape(rows, count, qk_width),
            own[:, 2 * HK * DK :].reshape(rows, count, v_width),
        ],
        axis=-1,
    )
    width = 2 * qk_width + v_width
    mix_heads = to_heads(packed, width).astype(jnp.float32)
    decay_heads = to_heads(log_decay[0], value_heads)
    rate_heads = to_heads(write_rate[0], value_heads)
    cot_heads = to_heads(cotangent[0], v_width).astype(jnp.float32)
    segments = lax.all_gather(segment_ids[0], "ctx", tiled=True)
    seg_ext = jnp.concatenate([jnp.full((margin,), -1, jnp.int32), segments.astype(jnp.int32)])

    weight_q = conv_weight[:, : HK * DK].reshape(-1, count, qk_width)[:, mine]
    weight_k = conv_weight[:, HK * DK : 2 * HK * DK].reshape(-1, count, qk_width)[:, mine]
    weight_v = conv_weight[:, 2 * HK * DK :].reshape(-1, count, v_width)[:, mine]
    weight_heads = jnp.concatenate([weight_q, weight_k, weight_v], axis=-1)

    def forward(mix_in, weight_in, decay_in, rate_in):
        return heads_forward(
            mix_in, weight_in, decay_in, rate_in, seg_ext, key_heads, value_heads
        )

    outputs, pullback = jax.vjp(forward, mix_heads, weight_heads, decay_heads, rate_heads)
    grad_mix, grad_weight, grad_decay, grad_rate = pullback(cot_heads)

    core = to_rows(outputs.astype(jnp.bfloat16), v_width).reshape(1, rows, HV * DV)
    back = to_rows(grad_mix.astype(jnp.bfloat16), width)
    grad_rows = jnp.concatenate(
        [
            back[:, :, :qk_width].reshape(rows, HK * DK),
            back[:, :, qk_width : 2 * qk_width].reshape(rows, HK * DK),
            back[:, :, 2 * qk_width :].reshape(rows, HV * DV),
        ],
        axis=-1,
    )[None]
    decay_rows = to_rows(grad_decay, value_heads).reshape(1, rows, HV)
    rate_rows = to_rows(grad_rate, value_heads).reshape(1, rows, HV)

    taps = conv_weight.shape[0]

    def place(part, total_width, part_width):
        slots = jnp.zeros((taps, count, part_width), jnp.float32)
        slots = lax.dynamic_update_slice(slots, part[:, None, :], (0, mine, 0))
        return slots.reshape(taps, total_width)

    placed = jnp.concatenate(
        [
            place(grad_weight[:, :qk_width], HK * DK, qk_width),
            place(grad_weight[:, qk_width : 2 * qk_width], HK * DK, qk_width),
            place(grad_weight[:, 2 * qk_width :], HV * DV, v_width),
        ],
        axis=-1,
    )
    total_conv = tree_sum(tree_sum(placed, "ctx"), "dp")
    tokens_all = mixed.shape[0] * lax.axis_size("dp") * length
    return (core, grad_rows, decay_rows, rate_rows, total_conv / math.sqrt(tokens_all))


def solution(mesh):
    in_specs = (
        P("dp", "ctx", None),
        P(),
        P("dp", "ctx", None),
        P("dp", "ctx", None),
        P("dp", "ctx"),
        P("dp", "ctx", None),
    )
    out_specs = (
        P("dp", "ctx", None),
        P("dp", "ctx", None),
        P("dp", "ctx", None),
        P("dp", "ctx", None),
        P(),
    )
    count = mesh.shape["ctx"]
    per_device = HV // count if HV % count == 0 else 0
    chosen = heads_local if per_device and (per_device * HK) % HV == 0 else local
    return jax.shard_map(chosen, mesh=mesh, in_specs=in_specs, out_specs=out_specs, check_vma=False)
```

```python
import math

import jax
import jax.numpy as jnp
from jax import lax
from jax.sharding import PartitionSpec as P

HK = 8
HV = 16
DK = 128
DV = 128
BLOCK = 64


HIGHEST = lax.Precision.HIGHEST


def from_behind(x, axis, by):
    size = lax.axis_size(axis)
    pairs = [(i, i + by) for i in range(size) if 0 <= i + by < size]
    return lax.ppermute(x, axis, pairs)


def prefix(value, axis, join, neutral, backward):
    count, mine = (lax.axis_size(axis), lax.axis_index(axis))
    pieces = jax.tree.map(lambda part: lax.all_gather(part, axis), value)
    if backward:
        pieces = jax.tree.map(lambda part: part[::-1], pieces)
        mine = count - 1 - mine
    total = jax.tree.map(
        lambda part, zero: jnp.full_like(part, 0) + jnp.asarray(zero, part.dtype), value, neutral
    )

    def hop(position, total):
        longer = join(total, jax.tree.map(lambda part: part[position], pieces))
        return jax.tree.map(lambda new, old: jnp.where(position < mine, new, old), longer, total)

    return lax.fori_loop(0, count - 1, hop, total)


def prepare(mix_ext, seg_ext, conv_weight):
    margin = conv_weight.shape[0] - 1
    positions = mix_ext.shape[0] - margin
    current = seg_ext[margin:]
    summed = jnp.zeros((positions, mix_ext.shape[1]), jnp.float32)
    for tap_index in range(margin + 1):
        same_doc = (seg_ext[tap_index : tap_index + positions] == current).astype(jnp.float32)
        summed = (
            summed
            + conv_weight[tap_index][None, :]
            * mix_ext[tap_index : tap_index + positions]
            * same_doc[:, None]
        )
    activated = jax.nn.silu(summed)
    split_at = HK * DK
    queries = activated[:, :split_at].reshape(positions, HK, DK)
    keyset = activated[:, split_at : 2 * split_at].reshape(positions, HK, DK)
    values = activated[:, 2 * split_at :].reshape(positions, HV, DV)
    queries = (
        queries
        / jnp.sqrt(jnp.sum(queries * queries, axis=-1, keepdims=True) + 1e-06)
        / math.sqrt(DK)
    )
    keyset = keyset / jnp.sqrt(jnp.sum(keyset * keyset, axis=-1, keepdims=True) + 1e-06)
    repeats = HV // HK
    return (jnp.repeat(queries, repeats, axis=1), jnp.repeat(keyset, repeats, axis=1), values)


def unit_lower_inverse(strict_part):
    positions = strict_part.shape[-1]
    identity_matrix = jnp.eye(positions, dtype=jnp.float32)[None]
    result = identity_matrix - strict_part
    power = strict_part
    reach = 2
    while reach < positions:
        power = jnp.einsum("hij,hjk->hik", power, power, precision=HIGHEST)
        result = jnp.einsum("hij,hjk->hik", result, identity_matrix + power, precision=HIGHEST)
        reach = reach * 2
    return result


def block_parts(queries, keyset, values, log_decay, write_rate, segments, seg_before):
    positions = queries.shape[0]
    cumulative = jnp.cumsum(log_decay, axis=0)
    keep_state = (segments == seg_before).astype(jnp.float32)
    entering = jnp.exp(cumulative) * keep_state[:, None]
    token_position = lax.iota(jnp.int32, positions)
    same_doc = segments[:, None] == segments[None, :]
    strict = same_doc & (token_position[:, None] > token_position[None, :])
    causal = same_doc & (token_position[:, None] >= token_position[None, :])
    spread = cumulative.T[:, :, None] - cumulative.T[:, None, :]
    strict_decay = jnp.where(strict[None], jnp.exp(jnp.where(strict[None], spread, 0.0)), 0.0)
    causal_decay = jnp.where(causal[None], jnp.exp(jnp.where(causal[None], spread, 0.0)), 0.0)
    key_inner = jnp.einsum("ihd,jhd->hij", keyset, keyset, precision=HIGHEST)
    inverse = unit_lower_inverse(write_rate.T[:, :, None] * key_inner * strict_decay)
    targets = jnp.concatenate(
        [keyset * (write_rate * entering)[:, :, None], values * write_rate[:, :, None]], axis=2
    )
    solved = jnp.einsum("hij,hjd->hid", inverse, targets.transpose(1, 0, 2), precision=HIGHEST)
    write_keys = solved[:, :, :DK]
    write_values = solved[:, :, DK:]
    scores = jnp.einsum("ihd,jhd->hij", queries, keyset, precision=HIGHEST) * causal_decay
    final_sum = cumulative[-1]
    tail_decay = (
        jnp.exp(final_sum[None, :] - cumulative)
        * (segments == segments[-1]).astype(jnp.float32)[:, None]
    )
    carried = jnp.exp(final_sum) * keep_state[-1]
    tail_keys = (keyset * tail_decay[:, :, None]).transpose(1, 0, 2)
    queried = (queries * entering[:, :, None]).transpose(1, 0, 2)
    return (write_keys, write_values, scores, tail_keys, queried, carried)


def block_map(block_data):
    write_keys, write_values, scores, tail_keys, queried, carried = block_data
    identity_matrix = jnp.eye(DK, dtype=jnp.float32)
    transform = carried[:, None, None] * identity_matrix[None] - jnp.einsum(
        "hcd,hce->hde", tail_keys, write_keys, precision=HIGHEST
    )
    shift_term = jnp.einsum("hcd,hce->hde", tail_keys, write_values, precision=HIGHEST)
    return (transform, shift_term)


def block_apply(block_data, state_in):
    write_keys, write_values, scores, tail_keys, queried, carried = block_data
    fresh_values = write_values - jnp.einsum(
        "hcd,hde->hce", write_keys, state_in, precision=HIGHEST
    )
    output = jnp.einsum("hcd,hde->hce", queried, state_in, precision=HIGHEST)
    output = output + jnp.einsum("hij,hje->hie", scores, fresh_values, precision=HIGHEST)
    state_next = carried[:, None, None] * state_in + jnp.einsum(
        "hcd,hce->hde", tail_keys, fresh_values, precision=HIGHEST
    )
    return (output, state_next)


def section_one(mix_ext, conv_weight, log_decay, write_rate, seg_ext):
    queries, keyset, values = prepare(mix_ext, seg_ext, conv_weight)
    margin = conv_weight.shape[0] - 1
    positions = log_decay.shape[0]
    blocks = positions // BLOCK
    segments = seg_ext[margin:]
    before = seg_ext[margin - 1 : margin - 1 + positions : BLOCK]

    def blocked(tensor):
        return tensor.reshape((blocks, BLOCK) + tensor.shape[1:])

    return jax.vmap(block_parts)(
        blocked(queries),
        blocked(keyset),
        blocked(values),
        blocked(log_decay),
        blocked(write_rate),
        blocked(segments),
        before,
    )


def section_two(parts, state_in):

    def step_block(state_now, block_data):
        output, state_next = block_apply(block_data, state_now)
        return (state_next, output)

    state_out, outputs = lax.scan(step_block, state_in, parts)
    blocks = outputs.shape[0]
    return (outputs.transpose(0, 2, 1, 3).reshape(blocks * BLOCK, HV * DV), state_out)


def summarize(parts):
    identity_matrix = jnp.eye(DK, dtype=jnp.float32)
    initial = (
        jnp.broadcast_to(identity_matrix, (HV, DK, DK)),
        jnp.zeros((HV, DK, DV), jnp.float32),
    )

    def fold_block(carried_map, block_data):
        transform, shift_term = block_map(block_data)
        merged = jnp.einsum("hij,hjk->hik", transform, carried_map[0], precision=HIGHEST)
        moved = (
            jnp.einsum("hij,hjk->hik", transform, carried_map[1], precision=HIGHEST) + shift_term
        )
        return ((merged, moved), None)

    result, unused = lax.scan(fold_block, initial, parts)
    return result


def compose(earlier_map, later_map):
    merged = jnp.einsum("shij,shjk->shik", later_map[0], earlier_map[0], precision=HIGHEST)
    moved = (
        jnp.einsum("shij,shjk->shik", later_map[0], earlier_map[1], precision=HIGHEST)
        + later_map[1]
    )
    return (merged, moved)


def local(mixed, conv_weight, log_decay, write_rate, segment_ids, cotangent):
    margin = conv_weight.shape[0] - 1
    shifted_rows, shifted_segs = from_behind(
        (mixed[:, -margin:, :], segment_ids[:, -margin:].astype(jnp.bfloat16)), "ctx", 1
    )
    mix_ext = jnp.concatenate([shifted_rows, mixed], axis=1).astype(jnp.float32)
    seg_ext = jnp.concatenate([shifted_segs.astype(jnp.int32), segment_ids], axis=1)

    def first_section(mix_in, weight_in, decay_in, rate_in):
        return jax.vmap(section_one, in_axes=(0, None, 0, 0, 0))(
            mix_in, weight_in, decay_in, rate_in, seg_ext
        )

    parts, first_pull = jax.vjp(first_section, mix_ext, conv_weight, log_decay, write_rate)
    transform, shift_term = jax.vmap(summarize)(parts)
    identity_pair = (
        jnp.broadcast_to(jnp.eye(transform.shape[-1], dtype=jnp.float32), transform.shape),
        jnp.zeros_like(shift_term),
    )
    incoming = prefix((transform, shift_term), "ctx", compose, identity_pair, False)[1]
    (outputs, leaving), second_pull = jax.vjp(jax.vmap(section_two), parts, incoming)
    part_grads, local_term = second_pull((cotangent.astype(jnp.float32), jnp.zeros_like(leaving)))
    flipped = jnp.swapaxes(transform, -1, -2)
    departing = prefix((flipped, local_term), "ctx", compose, identity_pair, True)[1]
    more_grads, unused_grad = second_pull((jnp.zeros_like(outputs), departing))
    total_parts = jax.tree.map(jnp.add, part_grads, more_grads)
    grad_mix, grad_weight, grad_decay, grad_rate = first_pull(total_parts)
    returned = from_behind(grad_mix[:, :margin, :].astype(jnp.bfloat16), "ctx", -1).astype(
        jnp.float32
    )
    own_grad = grad_mix[:, margin:, :]
    own_grad = jnp.concatenate(
        [own_grad[:, :-margin, :], own_grad[:, -margin:, :] + returned], axis=1
    )
    total_conv = lax.psum(grad_weight, ("dp", "ctx"))
    tokens_all = mixed.shape[0] * lax.axis_size("dp") * mixed.shape[1] * lax.axis_size("ctx")
    return (
        outputs.astype(jnp.bfloat16),
        own_grad.astype(jnp.bfloat16),
        grad_decay,
        grad_rate,
        total_conv / math.sqrt(tokens_all),
    )


def tree_sum(value, axis):
    count = lax.axis_size(axis)
    if count & (count - 1):
        return lax.psum(value, axis)
    step = 1
    while step < count:
        value = value + lax.ppermute(value, axis, [(i, i ^ step) for i in range(count)])
        step = step * 2
    return value


def prepare_heads(mix_ext, seg_ext, conv_weight, key_heads, value_heads):
    margin = conv_weight.shape[0] - 1
    positions = mix_ext.shape[0] - margin
    current = seg_ext[margin:]
    summed = jnp.zeros((positions, mix_ext.shape[1]), jnp.float32)
    for tap_index in range(margin + 1):
        same_doc = (seg_ext[tap_index : tap_index + positions] == current).astype(jnp.float32)
        summed = (
            summed
            + conv_weight[tap_index][None, :]
            * mix_ext[tap_index : tap_index + positions]
            * same_doc[:, None]
        )
    activated = jax.nn.silu(summed)
    split_at = key_heads * DK
    queries = activated[:, :split_at].reshape(positions, key_heads, DK)
    keyset = activated[:, split_at : 2 * split_at].reshape(positions, key_heads, DK)
    values = activated[:, 2 * split_at :].reshape(positions, value_heads, DV)
    queries = (
        queries
        / jnp.sqrt(jnp.sum(queries * queries, axis=-1, keepdims=True) + 1e-06)
        / math.sqrt(DK)
    )
    keyset = keyset / jnp.sqrt(jnp.sum(keyset * keyset, axis=-1, keepdims=True) + 1e-06)
    repeats = value_heads // key_heads
    return (jnp.repeat(queries, repeats, axis=1), jnp.repeat(keyset, repeats, axis=1), values)


def combine_maps(earlier, later):
    merged = jnp.einsum("...ij,...jk->...ik", later[0], earlier[0], precision=HIGHEST)
    moved = jnp.einsum("...ij,...jk->...ik", later[0], earlier[1], precision=HIGHEST) + later[1]
    return (merged, moved)


def inclusive_states(transform, shift_term):
    blocks = transform.shape[0]
    reach = 1
    while reach < blocks:
        moved = jnp.einsum(
            "bhij,bhjk->bhik", transform[reach:], shift_term[:-reach], precision=HIGHEST
        )
        shift_term = jnp.concatenate([shift_term[:reach], shift_term[reach:] + moved], axis=0)
        if 2 * reach < blocks:
            merged = jnp.einsum(
                "bhij,bhjk->bhik", transform[reach:], transform[:-reach], precision=HIGHEST
            )
            transform = jnp.concatenate([transform[:reach], merged], axis=0)
        reach = reach * 2
    return shift_term


@jax.custom_vjp
def entering_states(transform, shift_term):
    return entering_forward(transform, shift_term)[0]


def entering_forward(transform, shift_term):
    eye = jnp.broadcast_to(jnp.eye(transform.shape[-1], dtype=transform.dtype), transform[:1].shape)
    shifted_maps = jnp.concatenate([eye, transform[:-1]], axis=0)
    shifted_terms = jnp.concatenate([jnp.zeros_like(shift_term[:1]), shift_term[:-1]], axis=0)
    states = inclusive_states(shifted_maps, shifted_terms)
    return states, (transform, states)


def entering_backward(saved, grad_states):
    transform, states = saved
    flipped = jnp.swapaxes(transform, -1, -2)[::-1]
    total = inclusive_states(flipped, grad_states[::-1])[::-1]
    later = total[1:]
    grad_shift = jnp.concatenate([later, jnp.zeros_like(later[:1])], axis=0)
    grad_map = jnp.einsum("bhik,bhjk->bhij", later, states[:-1], precision=HIGHEST)
    grad_transform = jnp.concatenate([grad_map, jnp.zeros_like(transform[:1])], axis=0)
    return (grad_transform, grad_shift)


entering_states.defvjp(entering_forward, entering_backward)


def heads_forward(mix_in, weight_in, decay_in, rate_in, seg_ext, key_heads, value_heads):
    margin = weight_in.shape[0] - 1
    positions = decay_in.shape[0]
    blocks = positions // BLOCK
    mix_ext = jnp.concatenate([jnp.zeros((margin, mix_in.shape[1]), jnp.float32), mix_in], axis=0)
    queries, keyset, values = prepare_heads(mix_ext, seg_ext, weight_in, key_heads, value_heads)
    segments = seg_ext[margin:]
    before = seg_ext[margin - 1 : margin - 1 + positions : BLOCK]

    def blocked(tensor):
        return tensor.reshape((blocks, BLOCK) + tensor.shape[1:])

    parts = jax.vmap(block_parts)(
        blocked(queries),
        blocked(keyset),
        blocked(values),
        blocked(decay_in),
        blocked(rate_in),
        blocked(segments),
        before,
    )
    transform, shift_term = jax.vmap(block_map)(parts)
    incoming = entering_states(transform, shift_term)
    outputs, unused = jax.vmap(block_apply)(parts, incoming)
    return outputs.transpose(0, 2, 1, 3).reshape(positions, value_heads * DV)


def heads_local(mixed, conv_weight, log_decay, write_rate, segment_ids, cotangent):
    if mixed.shape[0] != 1:
        return local(mixed, conv_weight, log_decay, write_rate, segment_ids, cotangent)
    count = lax.axis_size("ctx")
    mine = lax.axis_index("ctx")
    value_heads = HV // count
    key_heads = value_heads * HK // HV
    margin = conv_weight.shape[0] - 1
    rows = mixed.shape[1]
    length = rows * count
    qk_width = key_heads * DK
    v_width = value_heads * DV

    def to_heads(array, width):
        grouped = array.reshape(rows, count, width)
        return lax.all_to_all(grouped, "ctx", 1, 0, tiled=True).reshape(length, width)

    def to_rows(array, width):
        grouped = array.reshape(count, rows, 1, width)
        return lax.all_to_all(grouped, "ctx", 0, 2, tiled=True).reshape(rows, count, width)

    own = mixed[0]
    width = 2 * qk_width + v_width
    packed = jnp.concatenate(
        [
            own[:, : HK * DK].reshape(rows, count, qk_width),
            own[:, HK * DK : 2 * HK * DK].reshape(rows, count, qk_width),
            own[:, 2 * HK * DK :].reshape(rows, count, v_width),
            cotangent[0].reshape(rows, count, v_width),
        ],
        axis=-1,
    )
    wide = to_heads(packed, width + v_width)
    mix_heads = wide[:, :width].astype(jnp.float32)
    cot_heads = wide[:, width:].astype(jnp.float32)
    seg_columns = jnp.broadcast_to(
        segment_ids[0].astype(jnp.float32)[:, None, None], (rows, count, 1)
    )
    small = jnp.concatenate(
        [
            log_decay[0].reshape(rows, count, value_heads),
            write_rate[0].reshape(rows, count, value_heads),
            seg_columns,
        ],
        axis=-1,
    )
    narrow = to_heads(small, 2 * value_heads + 1)
    decay_heads = narrow[:, :value_heads]
    rate_heads = narrow[:, value_heads : 2 * value_heads]
    segments = narrow[:, 2 * value_heads].astype(jnp.int32)
    seg_ext = jnp.concatenate([jnp.full((margin,), -1, jnp.int32), segments])

    weight_q = conv_weight[:, : HK * DK].reshape(-1, count, qk_width)[:, mine]
    weight_k = conv_weight[:, HK * DK : 2 * HK * DK].reshape(-1, count, qk_width)[:, mine]
    weight_v = conv_weight[:, 2 * HK * DK :].reshape(-1, count, v_width)[:, mine]
    weight_heads = jnp.concatenate([weight_q, weight_k, weight_v], axis=-1)

    def forward(mix_in, weight_in, decay_in, rate_in):
        return heads_forward(
            mix_in, weight_in, decay_in, rate_in, seg_ext, key_heads, value_heads
        )

    outputs, pullback = jax.vjp(forward, mix_heads, weight_heads, decay_heads, rate_heads)
    grad_mix, grad_weight, grad_decay, grad_rate = pullback(cot_heads)

    joined = jnp.concatenate([outputs.astype(jnp.bfloat16), grad_mix.astype(jnp.bfloat16)], axis=-1)
    back = to_rows(joined, v_width + width)
    core = back[:, :, :v_width].reshape(1, rows, HV * DV)
    grad_rows = jnp.concatenate(
        [
            back[:, :, v_width : v_width + qk_width].reshape(rows, HK * DK),
            back[:, :, v_width + qk_width : v_width + 2 * qk_width].reshape(rows, HK * DK),
            back[:, :, v_width + 2 * qk_width :].reshape(rows, HV * DV),
        ],
        axis=-1,
    )[None]
    grads_small = to_rows(jnp.concatenate([grad_decay, grad_rate], axis=-1), 2 * value_heads)
    decay_rows = grads_small[:, :, :value_heads].reshape(1, rows, HV)
    rate_rows = grads_small[:, :, value_heads:].reshape(1, rows, HV)

    taps = conv_weight.shape[0]

    def place(part, total_width, part_width):
        slots = jnp.zeros((taps, count, part_width), jnp.float32)
        slots = lax.dynamic_update_slice(slots, part[:, None, :], (0, mine, 0))
        return slots.reshape(taps, total_width)

    placed = jnp.concatenate(
        [
            place(grad_weight[:, :qk_width], HK * DK, qk_width),
            place(grad_weight[:, qk_width : 2 * qk_width], HK * DK, qk_width),
            place(grad_weight[:, 2 * qk_width :], HV * DV, v_width),
        ],
        axis=-1,
    )
    total_conv = tree_sum(tree_sum(placed, "ctx"), "dp")
    tokens_all = mixed.shape[0] * lax.axis_size("dp") * length
    return (core, grad_rows, decay_rows, rate_rows, total_conv / math.sqrt(tokens_all))


def solution(mesh):
    in_specs = (
        P("dp", "ctx", None),
        P(),
        P("dp", "ctx", None),
        P("dp", "ctx", None),
        P("dp", "ctx"),
        P("dp", "ctx", None),
    )
    out_specs = (
        P("dp", "ctx", None),
        P("dp", "ctx", None),
        P("dp", "ctx", None),
        P("dp", "ctx", None),
        P(),
    )
    count = mesh.shape["ctx"]
    per_device = HV // count if HV % count == 0 else 0
    chosen = heads_local if per_device and (per_device * HK) % HV == 0 else local
    return jax.shard_map(chosen, mesh=mesh, in_specs=in_specs, out_specs=out_specs, check_vma=False)
```

```python
import math

import jax
import jax.numpy as jnp
from jax import lax
from jax.sharding import PartitionSpec as P

HK = 8
HV = 16
DK = 128
DV = 128
BLOCK = 64


HIGHEST = lax.Precision.HIGHEST


def from_behind(x, axis, by):
    size = lax.axis_size(axis)
    pairs = [(i, i + by) for i in range(size) if 0 <= i + by < size]
    return lax.ppermute(x, axis, pairs)


def prefix(value, axis, join, neutral, backward):
    count, mine = (lax.axis_size(axis), lax.axis_index(axis))
    pieces = jax.tree.map(lambda part: lax.all_gather(part, axis), value)
    if backward:
        pieces = jax.tree.map(lambda part: part[::-1], pieces)
        mine = count - 1 - mine
    total = jax.tree.map(
        lambda part, zero: jnp.full_like(part, 0) + jnp.asarray(zero, part.dtype), value, neutral
    )

    def hop(position, total):
        longer = join(total, jax.tree.map(lambda part: part[position], pieces))
        return jax.tree.map(lambda new, old: jnp.where(position < mine, new, old), longer, total)

    return lax.fori_loop(0, count - 1, hop, total)


def prepare(mix_ext, seg_ext, conv_weight):
    margin = conv_weight.shape[0] - 1
    positions = mix_ext.shape[0] - margin
    current = seg_ext[margin:]
    summed = jnp.zeros((positions, mix_ext.shape[1]), jnp.float32)
    for tap_index in range(margin + 1):
        same_doc = (seg_ext[tap_index : tap_index + positions] == current).astype(jnp.float32)
        summed = (
            summed
            + conv_weight[tap_index][None, :]
            * mix_ext[tap_index : tap_index + positions]
            * same_doc[:, None]
        )
    activated = jax.nn.silu(summed)
    split_at = HK * DK
    queries = activated[:, :split_at].reshape(positions, HK, DK)
    keyset = activated[:, split_at : 2 * split_at].reshape(positions, HK, DK)
    values = activated[:, 2 * split_at :].reshape(positions, HV, DV)
    queries = (
        queries
        / jnp.sqrt(jnp.sum(queries * queries, axis=-1, keepdims=True) + 1e-06)
        / math.sqrt(DK)
    )
    keyset = keyset / jnp.sqrt(jnp.sum(keyset * keyset, axis=-1, keepdims=True) + 1e-06)
    repeats = HV // HK
    return (jnp.repeat(queries, repeats, axis=1), jnp.repeat(keyset, repeats, axis=1), values)


def unit_lower_inverse(strict_part):
    positions = strict_part.shape[-1]
    identity_matrix = jnp.eye(positions, dtype=jnp.float32)[None]
    result = identity_matrix - strict_part
    power = strict_part
    reach = 2
    while reach < positions:
        power = jnp.einsum("hij,hjk->hik", power, power, precision=HIGHEST)
        result = jnp.einsum("hij,hjk->hik", result, identity_matrix + power, precision=HIGHEST)
        reach = reach * 2
    return result


def block_parts(queries, keyset, values, log_decay, write_rate, segments, seg_before):
    positions = queries.shape[0]
    cumulative = jnp.cumsum(log_decay, axis=0)
    keep_state = (segments == seg_before).astype(jnp.float32)
    entering = jnp.exp(cumulative) * keep_state[:, None]
    token_position = lax.iota(jnp.int32, positions)
    same_doc = segments[:, None] == segments[None, :]
    strict = same_doc & (token_position[:, None] > token_position[None, :])
    causal = same_doc & (token_position[:, None] >= token_position[None, :])
    spread = cumulative.T[:, :, None] - cumulative.T[:, None, :]
    strict_decay = jnp.where(strict[None], jnp.exp(jnp.where(strict[None], spread, 0.0)), 0.0)
    causal_decay = jnp.where(causal[None], jnp.exp(jnp.where(causal[None], spread, 0.0)), 0.0)
    key_inner = jnp.einsum("ihd,jhd->hij", keyset, keyset, precision=HIGHEST)
    inverse = unit_lower_inverse(write_rate.T[:, :, None] * key_inner * strict_decay)
    targets = jnp.concatenate(
        [keyset * (write_rate * entering)[:, :, None], values * write_rate[:, :, None]], axis=2
    )
    solved = jnp.einsum("hij,hjd->hid", inverse, targets.transpose(1, 0, 2), precision=HIGHEST)
    write_keys = solved[:, :, :DK]
    write_values = solved[:, :, DK:]
    scores = jnp.einsum("ihd,jhd->hij", queries, keyset, precision=HIGHEST) * causal_decay
    final_sum = cumulative[-1]
    tail_decay = (
        jnp.exp(final_sum[None, :] - cumulative)
        * (segments == segments[-1]).astype(jnp.float32)[:, None]
    )
    carried = jnp.exp(final_sum) * keep_state[-1]
    tail_keys = (keyset * tail_decay[:, :, None]).transpose(1, 0, 2)
    queried = (queries * entering[:, :, None]).transpose(1, 0, 2)
    return (write_keys, write_values, scores, tail_keys, queried, carried)


def block_map(block_data):
    write_keys, write_values, scores, tail_keys, queried, carried = block_data
    identity_matrix = jnp.eye(DK, dtype=jnp.float32)
    transform = carried[:, None, None] * identity_matrix[None] - jnp.einsum(
        "hcd,hce->hde", tail_keys, write_keys, precision=HIGHEST
    )
    shift_term = jnp.einsum("hcd,hce->hde", tail_keys, write_values, precision=HIGHEST)
    return (transform, shift_term)


def block_apply(block_data, state_in):
    write_keys, write_values, scores, tail_keys, queried, carried = block_data
    fresh_values = write_values - jnp.einsum(
        "hcd,hde->hce", write_keys, state_in, precision=HIGHEST
    )
    output = jnp.einsum("hcd,hde->hce", queried, state_in, precision=HIGHEST)
    output = output + jnp.einsum("hij,hje->hie", scores, fresh_values, precision=HIGHEST)
    state_next = carried[:, None, None] * state_in + jnp.einsum(
        "hcd,hce->hde", tail_keys, fresh_values, precision=HIGHEST
    )
    return (output, state_next)


def section_one(mix_ext, conv_weight, log_decay, write_rate, seg_ext):
    queries, keyset, values = prepare(mix_ext, seg_ext, conv_weight)
    margin = conv_weight.shape[0] - 1
    positions = log_decay.shape[0]
    blocks = positions // BLOCK
    segments = seg_ext[margin:]
    before = seg_ext[margin - 1 : margin - 1 + positions : BLOCK]

    def blocked(tensor):
        return tensor.reshape((blocks, BLOCK) + tensor.shape[1:])

    return jax.vmap(block_parts)(
        blocked(queries),
        blocked(keyset),
        blocked(values),
        blocked(log_decay),
        blocked(write_rate),
        blocked(segments),
        before,
    )


def section_two(parts, state_in):

    def step_block(state_now, block_data):
        output, state_next = block_apply(block_data, state_now)
        return (state_next, output)

    state_out, outputs = lax.scan(step_block, state_in, parts)
    blocks = outputs.shape[0]
    return (outputs.transpose(0, 2, 1, 3).reshape(blocks * BLOCK, HV * DV), state_out)


def summarize(parts):
    identity_matrix = jnp.eye(DK, dtype=jnp.float32)
    initial = (
        jnp.broadcast_to(identity_matrix, (HV, DK, DK)),
        jnp.zeros((HV, DK, DV), jnp.float32),
    )

    def fold_block(carried_map, block_data):
        transform, shift_term = block_map(block_data)
        merged = jnp.einsum("hij,hjk->hik", transform, carried_map[0], precision=HIGHEST)
        moved = (
            jnp.einsum("hij,hjk->hik", transform, carried_map[1], precision=HIGHEST) + shift_term
        )
        return ((merged, moved), None)

    result, unused = lax.scan(fold_block, initial, parts)
    return result


def compose(earlier_map, later_map):
    merged = jnp.einsum("shij,shjk->shik", later_map[0], earlier_map[0], precision=HIGHEST)
    moved = (
        jnp.einsum("shij,shjk->shik", later_map[0], earlier_map[1], precision=HIGHEST)
        + later_map[1]
    )
    return (merged, moved)


def local(mixed, conv_weight, log_decay, write_rate, segment_ids, cotangent):
    margin = conv_weight.shape[0] - 1
    shifted_rows, shifted_segs = from_behind(
        (mixed[:, -margin:, :], segment_ids[:, -margin:].astype(jnp.bfloat16)), "ctx", 1
    )
    mix_ext = jnp.concatenate([shifted_rows, mixed], axis=1).astype(jnp.float32)
    seg_ext = jnp.concatenate([shifted_segs.astype(jnp.int32), segment_ids], axis=1)

    def first_section(mix_in, weight_in, decay_in, rate_in):
        return jax.vmap(section_one, in_axes=(0, None, 0, 0, 0))(
            mix_in, weight_in, decay_in, rate_in, seg_ext
        )

    parts, first_pull = jax.vjp(first_section, mix_ext, conv_weight, log_decay, write_rate)
    transform, shift_term = jax.vmap(summarize)(parts)
    identity_pair = (
        jnp.broadcast_to(jnp.eye(transform.shape[-1], dtype=jnp.float32), transform.shape),
        jnp.zeros_like(shift_term),
    )
    incoming = prefix((transform, shift_term), "ctx", compose, identity_pair, False)[1]
    (outputs, leaving), second_pull = jax.vjp(jax.vmap(section_two), parts, incoming)
    part_grads, local_term = second_pull((cotangent.astype(jnp.float32), jnp.zeros_like(leaving)))
    flipped = jnp.swapaxes(transform, -1, -2)
    departing = prefix((flipped, local_term), "ctx", compose, identity_pair, True)[1]
    more_grads, unused_grad = second_pull((jnp.zeros_like(outputs), departing))
    total_parts = jax.tree.map(jnp.add, part_grads, more_grads)
    grad_mix, grad_weight, grad_decay, grad_rate = first_pull(total_parts)
    returned = from_behind(grad_mix[:, :margin, :].astype(jnp.bfloat16), "ctx", -1).astype(
        jnp.float32
    )
    own_grad = grad_mix[:, margin:, :]
    own_grad = jnp.concatenate(
        [own_grad[:, :-margin, :], own_grad[:, -margin:, :] + returned], axis=1
    )
    total_conv = lax.psum(grad_weight, ("dp", "ctx"))
    tokens_all = mixed.shape[0] * lax.axis_size("dp") * mixed.shape[1] * lax.axis_size("ctx")
    return (
        outputs.astype(jnp.bfloat16),
        own_grad.astype(jnp.bfloat16),
        grad_decay,
        grad_rate,
        total_conv / math.sqrt(tokens_all),
    )


def tree_sum(value, axis):
    count = lax.axis_size(axis)
    if count & (count - 1):
        return lax.psum(value, axis)
    step = 1
    while step < count:
        value = value + lax.ppermute(value, axis, [(i, i ^ step) for i in range(count)])
        step = step * 2
    return value


def prepare_heads(mix_ext, seg_ext, conv_weight, key_heads, value_heads):
    margin = conv_weight.shape[0] - 1
    positions = mix_ext.shape[0] - margin
    current = seg_ext[margin:]
    summed = jnp.zeros((positions, mix_ext.shape[1]), jnp.float32)
    for tap_index in range(margin + 1):
        same_doc = (seg_ext[tap_index : tap_index + positions] == current).astype(jnp.float32)
        summed = (
            summed
            + conv_weight[tap_index][None, :]
            * mix_ext[tap_index : tap_index + positions]
            * same_doc[:, None]
        )
    activated = jax.nn.silu(summed)
    split_at = key_heads * DK
    queries = activated[:, :split_at].reshape(positions, key_heads, DK)
    keyset = activated[:, split_at : 2 * split_at].reshape(positions, key_heads, DK)
    values = activated[:, 2 * split_at :].reshape(positions, value_heads, DV)
    queries = (
        queries
        / jnp.sqrt(jnp.sum(queries * queries, axis=-1, keepdims=True) + 1e-06)
        / math.sqrt(DK)
    )
    keyset = keyset / jnp.sqrt(jnp.sum(keyset * keyset, axis=-1, keepdims=True) + 1e-06)
    repeats = value_heads // key_heads
    return (jnp.repeat(queries, repeats, axis=1), jnp.repeat(keyset, repeats, axis=1), values)


def combine_maps(earlier, later):
    merged = jnp.einsum("...ij,...jk->...ik", later[0], earlier[0], precision=HIGHEST)
    moved = jnp.einsum("...ij,...jk->...ik", later[0], earlier[1], precision=HIGHEST) + later[1]
    return (merged, moved)


def inclusive_states(transform, shift_term):
    blocks = transform.shape[0]
    reach = 1
    while reach < blocks:
        moved = jnp.einsum(
            "bhij,bhjk->bhik", transform[reach:], shift_term[:-reach], precision=HIGHEST
        )
        shift_term = jnp.concatenate([shift_term[:reach], shift_term[reach:] + moved], axis=0)
        if 2 * reach < blocks:
            merged = jnp.einsum(
                "bhij,bhjk->bhik", transform[reach:], transform[:-reach], precision=HIGHEST
            )
            transform = jnp.concatenate([transform[:reach], merged], axis=0)
        reach = reach * 2
    return shift_term


@jax.custom_vjp
def entering_states(transform, shift_term):
    return entering_forward(transform, shift_term)[0]


def entering_forward(transform, shift_term):
    eye = jnp.broadcast_to(jnp.eye(transform.shape[-1], dtype=transform.dtype), transform[:1].shape)
    shifted_maps = jnp.concatenate([eye, transform[:-1]], axis=0)
    shifted_terms = jnp.concatenate([jnp.zeros_like(shift_term[:1]), shift_term[:-1]], axis=0)
    states = inclusive_states(shifted_maps, shifted_terms)
    return states, (transform, states)


def entering_backward(saved, grad_states):
    transform, states = saved
    flipped = jnp.swapaxes(transform, -1, -2)[::-1]
    total = inclusive_states(flipped, grad_states[::-1])[::-1]
    later = total[1:]
    grad_shift = jnp.concatenate([later, jnp.zeros_like(later[:1])], axis=0)
    grad_map = jnp.einsum("bhik,bhjk->bhij", later, states[:-1], precision=HIGHEST)
    grad_transform = jnp.concatenate([grad_map, jnp.zeros_like(transform[:1])], axis=0)
    return (grad_transform, grad_shift)


entering_states.defvjp(entering_forward, entering_backward)


def heads_forward(mix_in, weight_in, decay_in, rate_in, seg_ext, key_heads, value_heads):
    margin = weight_in.shape[0] - 1
    positions = decay_in.shape[0]
    blocks = positions // BLOCK
    mix_ext = jnp.concatenate([jnp.zeros((margin, mix_in.shape[1]), jnp.float32), mix_in], axis=0)
    queries, keyset, values = prepare_heads(mix_ext, seg_ext, weight_in, key_heads, value_heads)
    segments = seg_ext[margin:]
    before = seg_ext[margin - 1 : margin - 1 + positions : BLOCK]

    def blocked(tensor):
        return tensor.reshape((blocks, BLOCK) + tensor.shape[1:])

    parts = jax.vmap(block_parts)(
        blocked(queries),
        blocked(keyset),
        blocked(values),
        blocked(decay_in),
        blocked(rate_in),
        blocked(segments),
        before,
    )
    transform, shift_term = jax.vmap(block_map)(parts)
    incoming = entering_states(transform, shift_term)
    outputs, unused = jax.vmap(block_apply)(parts, incoming)
    return outputs.transpose(0, 2, 1, 3).reshape(positions, value_heads * DV)


def heads_local(mixed, conv_weight, log_decay, write_rate, segment_ids, cotangent):
    if mixed.shape[0] != 1:
        return local(mixed, conv_weight, log_decay, write_rate, segment_ids, cotangent)
    count = lax.axis_size("ctx")
    mine = lax.axis_index("ctx")
    value_heads = HV // count
    key_heads = value_heads * HK // HV
    margin = conv_weight.shape[0] - 1
    rows = mixed.shape[1]
    length = rows * count
    qk_width = key_heads * DK
    v_width = value_heads * DV

    def to_heads(array, width):
        grouped = array.reshape(rows, count, width)
        return lax.all_to_all(grouped, "ctx", 1, 0, tiled=True).reshape(length, width)

    def to_rows(array, width):
        grouped = array.reshape(count, rows, 1, width)
        return lax.all_to_all(grouped, "ctx", 0, 2, tiled=True).reshape(rows, count, width)

    own = mixed[0]
    width = 2 * qk_width + v_width
    packed = jnp.concatenate(
        [
            own[:, : HK * DK].reshape(rows, count, qk_width),
            own[:, HK * DK : 2 * HK * DK].reshape(rows, count, qk_width),
            own[:, 2 * HK * DK :].reshape(rows, count, v_width),
            cotangent[0].reshape(rows, count, v_width),
        ],
        axis=-1,
    )
    wide = to_heads(packed, width + v_width)
    mix_heads = wide[:, :width].astype(jnp.float32)
    cot_heads = wide[:, width:].astype(jnp.float32)
    seg_columns = jnp.broadcast_to(
        segment_ids[0].astype(jnp.float32)[:, None, None], (rows, count, 1)
    )
    small = jnp.concatenate(
        [
            log_decay[0].reshape(rows, count, value_heads),
            write_rate[0].reshape(rows, count, value_heads),
            seg_columns,
        ],
        axis=-1,
    )
    narrow = to_heads(small, 2 * value_heads + 1)
    decay_heads = narrow[:, :value_heads]
    rate_heads = narrow[:, value_heads : 2 * value_heads]
    segments = narrow[:, 2 * value_heads].astype(jnp.int32)
    seg_ext = jnp.concatenate([jnp.full((margin,), -1, jnp.int32), segments])

    weight_q = conv_weight[:, : HK * DK].reshape(-1, count, qk_width)[:, mine]
    weight_k = conv_weight[:, HK * DK : 2 * HK * DK].reshape(-1, count, qk_width)[:, mine]
    weight_v = conv_weight[:, 2 * HK * DK :].reshape(-1, count, v_width)[:, mine]
    weight_heads = jnp.concatenate([weight_q, weight_k, weight_v], axis=-1)

    def forward(mix_in, weight_in, decay_in, rate_in):
        return heads_forward(
            mix_in, weight_in, decay_in, rate_in, seg_ext, key_heads, value_heads
        )

    outputs, pullback = jax.vjp(forward, mix_heads, weight_heads, decay_heads, rate_heads)
    grad_mix, grad_weight, grad_decay, grad_rate = pullback(cot_heads)

    joined = jnp.concatenate([outputs.astype(jnp.bfloat16), grad_mix.astype(jnp.bfloat16)], axis=-1)
    back = to_rows(joined, v_width + width)
    core = back[:, :, :v_width].reshape(1, rows, HV * DV)
    grad_rows = jnp.concatenate(
        [
            back[:, :, v_width : v_width + qk_width].reshape(rows, HK * DK),
            back[:, :, v_width + qk_width : v_width + 2 * qk_width].reshape(rows, HK * DK),
            back[:, :, v_width + 2 * qk_width :].reshape(rows, HV * DV),
        ],
        axis=-1,
    )[None]
    taps = conv_weight.shape[0]
    sequences = lax.axis_size("dp")
    spread = jnp.broadcast_to(grad_weight[None], (sequences,) + grad_weight.shape)
    gathered = lax.all_to_all(spread, "dp", 0, 0, tiled=True)
    weight_sum = gathered[0]
    for index in range(1, sequences):
        weight_sum = weight_sum + gathered[index]
    pieces = jnp.concatenate(
        [
            jnp.concatenate([grad_decay, grad_rate], axis=-1).reshape(count, rows * 2 * value_heads),
            jnp.broadcast_to(weight_sum.reshape(1, taps * width), (count, taps * width)),
        ],
        axis=-1,
    )
    returned = lax.all_to_all(pieces[:, None], "ctx", 0, 1, tiled=True)[0]
    grads_small = returned[:, : rows * 2 * value_heads].reshape(count, rows, 2 * value_heads)
    grads_small = grads_small.transpose(1, 0, 2)
    decay_rows = grads_small[:, :, :value_heads].reshape(1, rows, HV)
    rate_rows = grads_small[:, :, value_heads:].reshape(1, rows, HV)
    conv_parts = returned[:, rows * 2 * value_heads :].reshape(count, taps, width).transpose(1, 0, 2)
    total_conv = jnp.concatenate(
        [
            conv_parts[:, :, :qk_width].reshape(taps, HK * DK),
            conv_parts[:, :, qk_width : 2 * qk_width].reshape(taps, HK * DK),
            conv_parts[:, :, 2 * qk_width :].reshape(taps, HV * DV),
        ],
        axis=-1,
    )
    tokens_all = mixed.shape[0] * sequences * length
    return (core, grad_rows, decay_rows, rate_rows, total_conv / math.sqrt(tokens_all))


def solution(mesh):
    in_specs = (
        P("dp", "ctx", None),
        P(),
        P("dp", "ctx", None),
        P("dp", "ctx", None),
        P("dp", "ctx"),
        P("dp", "ctx", None),
    )
    out_specs = (
        P("dp", "ctx", None),
        P("dp", "ctx", None),
        P("dp", "ctx", None),
        P("dp", "ctx", None),
        P(),
    )
    count = mesh.shape["ctx"]
    per_device = HV // count if HV % count == 0 else 0
    chosen = heads_local if per_device and (per_device * HK) % HV == 0 else local
    return jax.shard_map(chosen, mesh=mesh, in_specs=in_specs, out_specs=out_specs, check_vma=False)
```

```python
import math

import jax
import jax.numpy as jnp
from jax import lax
from jax.sharding import PartitionSpec as P

HK = 8
HV = 16
DK = 128
DV = 128
BLOCK = 64


HIGHEST = lax.Precision.HIGHEST


def from_behind(x, axis, by):
    size = lax.axis_size(axis)
    pairs = [(i, i + by) for i in range(size) if 0 <= i + by < size]
    return lax.ppermute(x, axis, pairs)


def prefix(value, axis, join, neutral, backward):
    count, mine = (lax.axis_size(axis), lax.axis_index(axis))
    pieces = jax.tree.map(lambda part: lax.all_gather(part, axis), value)
    if backward:
        pieces = jax.tree.map(lambda part: part[::-1], pieces)
        mine = count - 1 - mine
    total = jax.tree.map(
        lambda part, zero: jnp.full_like(part, 0) + jnp.asarray(zero, part.dtype), value, neutral
    )

    def hop(position, total):
        longer = join(total, jax.tree.map(lambda part: part[position], pieces))
        return jax.tree.map(lambda new, old: jnp.where(position < mine, new, old), longer, total)

    return lax.fori_loop(0, count - 1, hop, total)


def prepare(mix_ext, seg_ext, conv_weight):
    margin = conv_weight.shape[0] - 1
    positions = mix_ext.shape[0] - margin
    current = seg_ext[margin:]
    summed = jnp.zeros((positions, mix_ext.shape[1]), jnp.float32)
    for tap_index in range(margin + 1):
        same_doc = (seg_ext[tap_index : tap_index + positions] == current).astype(jnp.float32)
        summed = (
            summed
            + conv_weight[tap_index][None, :]
            * mix_ext[tap_index : tap_index + positions]
            * same_doc[:, None]
        )
    activated = jax.nn.silu(summed)
    split_at = HK * DK
    queries = activated[:, :split_at].reshape(positions, HK, DK)
    keyset = activated[:, split_at : 2 * split_at].reshape(positions, HK, DK)
    values = activated[:, 2 * split_at :].reshape(positions, HV, DV)
    queries = (
        queries
        / jnp.sqrt(jnp.sum(queries * queries, axis=-1, keepdims=True) + 1e-06)
        / math.sqrt(DK)
    )
    keyset = keyset / jnp.sqrt(jnp.sum(keyset * keyset, axis=-1, keepdims=True) + 1e-06)
    repeats = HV // HK
    return (jnp.repeat(queries, repeats, axis=1), jnp.repeat(keyset, repeats, axis=1), values)


def unit_lower_inverse(strict_part):
    positions = strict_part.shape[-1]
    identity_matrix = jnp.eye(positions, dtype=jnp.float32)[None]
    result = identity_matrix - strict_part
    power = strict_part
    reach = 2
    while reach < positions:
        power = jnp.einsum("hij,hjk->hik", power, power, precision=HIGHEST)
        result = jnp.einsum("hij,hjk->hik", result, identity_matrix + power, precision=HIGHEST)
        reach = reach * 2
    return result


def block_parts(queries, keyset, values, log_decay, write_rate, segments, seg_before):
    positions = queries.shape[0]
    cumulative = jnp.cumsum(log_decay, axis=0)
    keep_state = (segments == seg_before).astype(jnp.float32)
    entering = jnp.exp(cumulative) * keep_state[:, None]
    token_position = lax.iota(jnp.int32, positions)
    same_doc = segments[:, None] == segments[None, :]
    strict = same_doc & (token_position[:, None] > token_position[None, :])
    causal = same_doc & (token_position[:, None] >= token_position[None, :])
    spread = cumulative.T[:, :, None] - cumulative.T[:, None, :]
    strict_decay = jnp.where(strict[None], jnp.exp(jnp.where(strict[None], spread, 0.0)), 0.0)
    causal_decay = jnp.where(causal[None], jnp.exp(jnp.where(causal[None], spread, 0.0)), 0.0)
    key_inner = jnp.einsum("ihd,jhd->hij", keyset, keyset, precision=HIGHEST)
    inverse = unit_lower_inverse(write_rate.T[:, :, None] * key_inner * strict_decay)
    targets = jnp.concatenate(
        [keyset * (write_rate * entering)[:, :, None], values * write_rate[:, :, None]], axis=2
    )
    solved = jnp.einsum("hij,hjd->hid", inverse, targets.transpose(1, 0, 2), precision=HIGHEST)
    write_keys = solved[:, :, :DK]
    write_values = solved[:, :, DK:]
    scores = jnp.einsum("ihd,jhd->hij", queries, keyset, precision=HIGHEST) * causal_decay
    final_sum = cumulative[-1]
    tail_decay = (
        jnp.exp(final_sum[None, :] - cumulative)
        * (segments == segments[-1]).astype(jnp.float32)[:, None]
    )
    carried = jnp.exp(final_sum) * keep_state[-1]
    tail_keys = (keyset * tail_decay[:, :, None]).transpose(1, 0, 2)
    queried = (queries * entering[:, :, None]).transpose(1, 0, 2)
    return (write_keys, write_values, scores, tail_keys, queried, carried)


@jax.custom_vjp
def lower_inverse(strict_part):
    return unit_lower_inverse(strict_part)


def lower_inverse_forward(strict_part):
    inverse = unit_lower_inverse(strict_part)
    return inverse, inverse


def lower_inverse_backward(inverse, grad_inverse):
    flipped = jnp.swapaxes(inverse, -1, -2)
    inner = jnp.einsum("hij,hjk->hik", flipped, grad_inverse, precision=HIGHEST)
    return (-jnp.einsum("hij,hjk->hik", inner, flipped, precision=HIGHEST),)


lower_inverse.defvjp(lower_inverse_forward, lower_inverse_backward)


def block_parts_heads(queries, keyset, values, log_decay, write_rate, segments, seg_before):
    positions = queries.shape[0]
    cumulative = jnp.cumsum(log_decay, axis=0)
    keep_state = (segments == seg_before).astype(jnp.float32)
    entering = jnp.exp(cumulative) * keep_state[:, None]
    token_position = lax.iota(jnp.int32, positions)
    same_doc = segments[:, None] == segments[None, :]
    strict = same_doc & (token_position[:, None] > token_position[None, :])
    causal = same_doc & (token_position[:, None] >= token_position[None, :])
    spread = cumulative.T[:, :, None] - cumulative.T[:, None, :]
    strict_decay = jnp.where(strict[None], jnp.exp(jnp.where(strict[None], spread, 0.0)), 0.0)
    causal_decay = jnp.where(causal[None], jnp.exp(jnp.where(causal[None], spread, 0.0)), 0.0)
    key_inner = jnp.einsum("ihd,jhd->hij", keyset, keyset, precision=HIGHEST)
    inverse = lower_inverse(write_rate.T[:, :, None] * key_inner * strict_decay)
    targets = jnp.concatenate(
        [keyset * (write_rate * entering)[:, :, None], values * write_rate[:, :, None]], axis=2
    )
    solved = jnp.einsum("hij,hjd->hid", inverse, targets.transpose(1, 0, 2), precision=HIGHEST)
    write_keys = solved[:, :, :DK]
    write_values = solved[:, :, DK:]
    scores = jnp.einsum("ihd,jhd->hij", queries, keyset, precision=HIGHEST) * causal_decay
    final_sum = cumulative[-1]
    tail_decay = (
        jnp.exp(final_sum[None, :] - cumulative)
        * (segments == segments[-1]).astype(jnp.float32)[:, None]
    )
    carried = jnp.exp(final_sum) * keep_state[-1]
    tail_keys = (keyset * tail_decay[:, :, None]).transpose(1, 0, 2)
    queried = (queries * entering[:, :, None]).transpose(1, 0, 2)
    return (write_keys, write_values, scores, tail_keys, queried, carried)


def block_map(block_data):
    write_keys, write_values, scores, tail_keys, queried, carried = block_data
    identity_matrix = jnp.eye(DK, dtype=jnp.float32)
    transform = carried[:, None, None] * identity_matrix[None] - jnp.einsum(
        "hcd,hce->hde", tail_keys, write_keys, precision=HIGHEST
    )
    shift_term = jnp.einsum("hcd,hce->hde", tail_keys, write_values, precision=HIGHEST)
    return (transform, shift_term)


def block_apply(block_data, state_in):
    write_keys, write_values, scores, tail_keys, queried, carried = block_data
    fresh_values = write_values - jnp.einsum(
        "hcd,hde->hce", write_keys, state_in, precision=HIGHEST
    )
    output = jnp.einsum("hcd,hde->hce", queried, state_in, precision=HIGHEST)
    output = output + jnp.einsum("hij,hje->hie", scores, fresh_values, precision=HIGHEST)
    state_next = carried[:, None, None] * state_in + jnp.einsum(
        "hcd,hce->hde", tail_keys, fresh_values, precision=HIGHEST
    )
    return (output, state_next)


def section_one(mix_ext, conv_weight, log_decay, write_rate, seg_ext):
    queries, keyset, values = prepare(mix_ext, seg_ext, conv_weight)
    margin = conv_weight.shape[0] - 1
    positions = log_decay.shape[0]
    blocks = positions // BLOCK
    segments = seg_ext[margin:]
    before = seg_ext[margin - 1 : margin - 1 + positions : BLOCK]

    def blocked(tensor):
        return tensor.reshape((blocks, BLOCK) + tensor.shape[1:])

    return jax.vmap(block_parts)(
        blocked(queries),
        blocked(keyset),
        blocked(values),
        blocked(log_decay),
        blocked(write_rate),
        blocked(segments),
        before,
    )


def section_two(parts, state_in):

    def step_block(state_now, block_data):
        output, state_next = block_apply(block_data, state_now)
        return (state_next, output)

    state_out, outputs = lax.scan(step_block, state_in, parts)
    blocks = outputs.shape[0]
    return (outputs.transpose(0, 2, 1, 3).reshape(blocks * BLOCK, HV * DV), state_out)


def summarize(parts):
    identity_matrix = jnp.eye(DK, dtype=jnp.float32)
    initial = (
        jnp.broadcast_to(identity_matrix, (HV, DK, DK)),
        jnp.zeros((HV, DK, DV), jnp.float32),
    )

    def fold_block(carried_map, block_data):
        transform, shift_term = block_map(block_data)
        merged = jnp.einsum("hij,hjk->hik", transform, carried_map[0], precision=HIGHEST)
        moved = (
            jnp.einsum("hij,hjk->hik", transform, carried_map[1], precision=HIGHEST) + shift_term
        )
        return ((merged, moved), None)

    result, unused = lax.scan(fold_block, initial, parts)
    return result


def compose(earlier_map, later_map):
    merged = jnp.einsum("shij,shjk->shik", later_map[0], earlier_map[0], precision=HIGHEST)
    moved = (
        jnp.einsum("shij,shjk->shik", later_map[0], earlier_map[1], precision=HIGHEST)
        + later_map[1]
    )
    return (merged, moved)


def local(mixed, conv_weight, log_decay, write_rate, segment_ids, cotangent):
    margin = conv_weight.shape[0] - 1
    shifted_rows, shifted_segs = from_behind(
        (mixed[:, -margin:, :], segment_ids[:, -margin:].astype(jnp.bfloat16)), "ctx", 1
    )
    mix_ext = jnp.concatenate([shifted_rows, mixed], axis=1).astype(jnp.float32)
    seg_ext = jnp.concatenate([shifted_segs.astype(jnp.int32), segment_ids], axis=1)

    def first_section(mix_in, weight_in, decay_in, rate_in):
        return jax.vmap(section_one, in_axes=(0, None, 0, 0, 0))(
            mix_in, weight_in, decay_in, rate_in, seg_ext
        )

    parts, first_pull = jax.vjp(first_section, mix_ext, conv_weight, log_decay, write_rate)
    transform, shift_term = jax.vmap(summarize)(parts)
    identity_pair = (
        jnp.broadcast_to(jnp.eye(transform.shape[-1], dtype=jnp.float32), transform.shape),
        jnp.zeros_like(shift_term),
    )
    incoming = prefix((transform, shift_term), "ctx", compose, identity_pair, False)[1]
    (outputs, leaving), second_pull = jax.vjp(jax.vmap(section_two), parts, incoming)
    part_grads, local_term = second_pull((cotangent.astype(jnp.float32), jnp.zeros_like(leaving)))
    flipped = jnp.swapaxes(transform, -1, -2)
    departing = prefix((flipped, local_term), "ctx", compose, identity_pair, True)[1]
    more_grads, unused_grad = second_pull((jnp.zeros_like(outputs), departing))
    total_parts = jax.tree.map(jnp.add, part_grads, more_grads)
    grad_mix, grad_weight, grad_decay, grad_rate = first_pull(total_parts)
    returned = from_behind(grad_mix[:, :margin, :].astype(jnp.bfloat16), "ctx", -1).astype(
        jnp.float32
    )
    own_grad = grad_mix[:, margin:, :]
    own_grad = jnp.concatenate(
        [own_grad[:, :-margin, :], own_grad[:, -margin:, :] + returned], axis=1
    )
    total_conv = lax.psum(grad_weight, ("dp", "ctx"))
    tokens_all = mixed.shape[0] * lax.axis_size("dp") * mixed.shape[1] * lax.axis_size("ctx")
    return (
        outputs.astype(jnp.bfloat16),
        own_grad.astype(jnp.bfloat16),
        grad_decay,
        grad_rate,
        total_conv / math.sqrt(tokens_all),
    )


def tree_sum(value, axis):
    count = lax.axis_size(axis)
    if count & (count - 1):
        return lax.psum(value, axis)
    step = 1
    while step < count:
        value = value + lax.ppermute(value, axis, [(i, i ^ step) for i in range(count)])
        step = step * 2
    return value


def prepare_heads(mix_ext, seg_ext, conv_weight, key_heads, value_heads):
    margin = conv_weight.shape[0] - 1
    positions = mix_ext.shape[0] - margin
    current = seg_ext[margin:]
    summed = jnp.zeros((positions, mix_ext.shape[1]), jnp.float32)
    for tap_index in range(margin + 1):
        same_doc = (seg_ext[tap_index : tap_index + positions] == current).astype(jnp.float32)
        summed = (
            summed
            + conv_weight[tap_index][None, :]
            * mix_ext[tap_index : tap_index + positions]
            * same_doc[:, None]
        )
    activated = jax.nn.silu(summed)
    split_at = key_heads * DK
    queries = activated[:, :split_at].reshape(positions, key_heads, DK)
    keyset = activated[:, split_at : 2 * split_at].reshape(positions, key_heads, DK)
    values = activated[:, 2 * split_at :].reshape(positions, value_heads, DV)
    queries = (
        queries
        / jnp.sqrt(jnp.sum(queries * queries, axis=-1, keepdims=True) + 1e-06)
        / math.sqrt(DK)
    )
    keyset = keyset / jnp.sqrt(jnp.sum(keyset * keyset, axis=-1, keepdims=True) + 1e-06)
    repeats = value_heads // key_heads
    return (jnp.repeat(queries, repeats, axis=1), jnp.repeat(keyset, repeats, axis=1), values)


def combine_maps(earlier, later):
    merged = jnp.einsum("...ij,...jk->...ik", later[0], earlier[0], precision=HIGHEST)
    moved = jnp.einsum("...ij,...jk->...ik", later[0], earlier[1], precision=HIGHEST) + later[1]
    return (merged, moved)


def inclusive_states(transform, shift_term):
    blocks = transform.shape[0]
    reach = 1
    while reach < blocks:
        moved = jnp.einsum(
            "bhij,bhjk->bhik", transform[reach:], shift_term[:-reach], precision=HIGHEST
        )
        shift_term = jnp.concatenate([shift_term[:reach], shift_term[reach:] + moved], axis=0)
        if 2 * reach < blocks:
            merged = jnp.einsum(
                "bhij,bhjk->bhik", transform[reach:], transform[:-reach], precision=HIGHEST
            )
            transform = jnp.concatenate([transform[:reach], merged], axis=0)
        reach = reach * 2
    return shift_term


@jax.custom_vjp
def entering_states(transform, shift_term):
    return entering_forward(transform, shift_term)[0]


def entering_forward(transform, shift_term):
    eye = jnp.broadcast_to(jnp.eye(transform.shape[-1], dtype=transform.dtype), transform[:1].shape)
    shifted_maps = jnp.concatenate([eye, transform[:-1]], axis=0)
    shifted_terms = jnp.concatenate([jnp.zeros_like(shift_term[:1]), shift_term[:-1]], axis=0)
    states = inclusive_states(shifted_maps, shifted_terms)
    return states, (transform, states)


def entering_backward(saved, grad_states):
    transform, states = saved
    flipped = jnp.swapaxes(transform, -1, -2)[::-1]
    total = inclusive_states(flipped, grad_states[::-1])[::-1]
    later = total[1:]
    grad_shift = jnp.concatenate([later, jnp.zeros_like(later[:1])], axis=0)
    grad_map = jnp.einsum("bhik,bhjk->bhij", later, states[:-1], precision=HIGHEST)
    grad_transform = jnp.concatenate([grad_map, jnp.zeros_like(transform[:1])], axis=0)
    return (grad_transform, grad_shift)


entering_states.defvjp(entering_forward, entering_backward)


def heads_forward(mix_in, weight_in, decay_in, rate_in, seg_ext, key_heads, value_heads):
    margin = weight_in.shape[0] - 1
    positions = decay_in.shape[0]
    blocks = positions // BLOCK
    mix_ext = jnp.concatenate([jnp.zeros((margin, mix_in.shape[1]), jnp.float32), mix_in], axis=0)
    queries, keyset, values = prepare_heads(mix_ext, seg_ext, weight_in, key_heads, value_heads)
    segments = seg_ext[margin:]
    before = seg_ext[margin - 1 : margin - 1 + positions : BLOCK]

    def blocked(tensor):
        return tensor.reshape((blocks, BLOCK) + tensor.shape[1:])

    parts = jax.vmap(block_parts_heads)(
        blocked(queries),
        blocked(keyset),
        blocked(values),
        blocked(decay_in),
        blocked(rate_in),
        blocked(segments),
        before,
    )
    transform, shift_term = jax.vmap(block_map)(parts)
    incoming = entering_states(transform, shift_term)
    outputs, unused = jax.vmap(block_apply)(parts, incoming)
    return outputs.transpose(0, 2, 1, 3).reshape(positions, value_heads * DV)


def heads_local(mixed, conv_weight, log_decay, write_rate, segment_ids, cotangent):
    if mixed.shape[0] != 1:
        return local(mixed, conv_weight, log_decay, write_rate, segment_ids, cotangent)
    count = lax.axis_size("ctx")
    mine = lax.axis_index("ctx")
    value_heads = HV // count
    key_heads = value_heads * HK // HV
    margin = conv_weight.shape[0] - 1
    rows = mixed.shape[1]
    length = rows * count
    qk_width = key_heads * DK
    v_width = value_heads * DV

    def to_heads(array, width):
        grouped = array.reshape(rows, count, width)
        return lax.all_to_all(grouped, "ctx", 1, 0, tiled=True).reshape(length, width)

    def to_rows(array, width):
        grouped = array.reshape(count, rows, 1, width)
        return lax.all_to_all(grouped, "ctx", 0, 2, tiled=True).reshape(rows, count, width)

    own = mixed[0]
    width = 2 * qk_width + v_width
    packed = jnp.concatenate(
        [
            own[:, : HK * DK].reshape(rows, count, qk_width),
            own[:, HK * DK : 2 * HK * DK].reshape(rows, count, qk_width),
            own[:, 2 * HK * DK :].reshape(rows, count, v_width),
            cotangent[0].reshape(rows, count, v_width),
        ],
        axis=-1,
    )
    wide = to_heads(packed, width + v_width)
    mix_heads = wide[:, :width].astype(jnp.float32)
    cot_heads = wide[:, width:].astype(jnp.float32)
    seg_columns = jnp.broadcast_to(
        segment_ids[0].astype(jnp.float32)[:, None, None], (rows, count, 1)
    )
    small = jnp.concatenate(
        [
            log_decay[0].reshape(rows, count, value_heads),
            write_rate[0].reshape(rows, count, value_heads),
            seg_columns,
        ],
        axis=-1,
    )
    narrow = to_heads(small, 2 * value_heads + 1)
    decay_heads = narrow[:, :value_heads]
    rate_heads = narrow[:, value_heads : 2 * value_heads]
    segments = narrow[:, 2 * value_heads].astype(jnp.int32)
    seg_ext = jnp.concatenate([jnp.full((margin,), -1, jnp.int32), segments])

    weight_q = conv_weight[:, : HK * DK].reshape(-1, count, qk_width)[:, mine]
    weight_k = conv_weight[:, HK * DK : 2 * HK * DK].reshape(-1, count, qk_width)[:, mine]
    weight_v = conv_weight[:, 2 * HK * DK :].reshape(-1, count, v_width)[:, mine]
    weight_heads = jnp.concatenate([weight_q, weight_k, weight_v], axis=-1)

    def forward(mix_in, weight_in, decay_in, rate_in):
        return heads_forward(
            mix_in, weight_in, decay_in, rate_in, seg_ext, key_heads, value_heads
        )

    outputs, pullback = jax.vjp(forward, mix_heads, weight_heads, decay_heads, rate_heads)
    grad_mix, grad_weight, grad_decay, grad_rate = pullback(cot_heads)

    joined = jnp.concatenate([outputs.astype(jnp.bfloat16), grad_mix.astype(jnp.bfloat16)], axis=-1)
    back = to_rows(joined, v_width + width)
    core = back[:, :, :v_width].reshape(1, rows, HV * DV)
    grad_rows = jnp.concatenate(
        [
            back[:, :, v_width : v_width + qk_width].reshape(rows, HK * DK),
            back[:, :, v_width + qk_width : v_width + 2 * qk_width].reshape(rows, HK * DK),
            back[:, :, v_width + 2 * qk_width :].reshape(rows, HV * DV),
        ],
        axis=-1,
    )[None]
    taps = conv_weight.shape[0]
    sequences = lax.axis_size("dp")
    spread = jnp.broadcast_to(grad_weight[None], (sequences,) + grad_weight.shape)
    gathered = lax.all_to_all(spread, "dp", 0, 0, tiled=True)
    weight_sum = gathered[0]
    for index in range(1, sequences):
        weight_sum = weight_sum + gathered[index]
    pieces = jnp.concatenate(
        [
            jnp.concatenate([grad_decay, grad_rate], axis=-1).reshape(count, rows * 2 * value_heads),
            jnp.broadcast_to(weight_sum.reshape(1, taps * width), (count, taps * width)),
        ],
        axis=-1,
    )
    returned = lax.all_to_all(pieces[:, None], "ctx", 0, 1, tiled=True)[0]
    grads_small = returned[:, : rows * 2 * value_heads].reshape(count, rows, 2 * value_heads)
    grads_small = grads_small.transpose(1, 0, 2)
    decay_rows = grads_small[:, :, :value_heads].reshape(1, rows, HV)
    rate_rows = grads_small[:, :, value_heads:].reshape(1, rows, HV)
    conv_parts = returned[:, rows * 2 * value_heads :].reshape(count, taps, width).transpose(1, 0, 2)
    total_conv = jnp.concatenate(
        [
            conv_parts[:, :, :qk_width].reshape(taps, HK * DK),
            conv_parts[:, :, qk_width : 2 * qk_width].reshape(taps, HK * DK),
            conv_parts[:, :, 2 * qk_width :].reshape(taps, HV * DV),
        ],
        axis=-1,
    )
    tokens_all = mixed.shape[0] * sequences * length
    return (core, grad_rows, decay_rows, rate_rows, total_conv / math.sqrt(tokens_all))


def solution(mesh):
    in_specs = (
        P("dp", "ctx", None),
        P(),
        P("dp", "ctx", None),
        P("dp", "ctx", None),
        P("dp", "ctx"),
        P("dp", "ctx", None),
    )
    out_specs = (
        P("dp", "ctx", None),
        P("dp", "ctx", None),
        P("dp", "ctx", None),
        P("dp", "ctx", None),
        P(),
    )
    count = mesh.shape["ctx"]
    per_device = HV // count if HV % count == 0 else 0
    chosen = heads_local if per_device and (per_device * HK) % HV == 0 else local
    return jax.shard_map(chosen, mesh=mesh, in_specs=in_specs, out_specs=out_specs, check_vma=False)
```

```python
import math

import jax
import jax.numpy as jnp
from jax import lax
from jax.sharding import PartitionSpec as P

HK = 8
HV = 16
DK = 128
DV = 128
BLOCK = 64


HIGHEST = lax.Precision.HIGHEST


def from_behind(x, axis, by):
    size = lax.axis_size(axis)
    pairs = [(i, i + by) for i in range(size) if 0 <= i + by < size]
    return lax.ppermute(x, axis, pairs)


def prefix(value, axis, join, neutral, backward):
    count, mine = (lax.axis_size(axis), lax.axis_index(axis))
    pieces = jax.tree.map(lambda part: lax.all_gather(part, axis), value)
    if backward:
        pieces = jax.tree.map(lambda part: part[::-1], pieces)
        mine = count - 1 - mine
    total = jax.tree.map(
        lambda part, zero: jnp.full_like(part, 0) + jnp.asarray(zero, part.dtype), value, neutral
    )

    def hop(position, total):
        longer = join(total, jax.tree.map(lambda part: part[position], pieces))
        return jax.tree.map(lambda new, old: jnp.where(position < mine, new, old), longer, total)

    return lax.fori_loop(0, count - 1, hop, total)


def prepare(mix_ext, seg_ext, conv_weight):
    margin = conv_weight.shape[0] - 1
    positions = mix_ext.shape[0] - margin
    current = seg_ext[margin:]
    summed = jnp.zeros((positions, mix_ext.shape[1]), jnp.float32)
    for tap_index in range(margin + 1):
        same_doc = (seg_ext[tap_index : tap_index + positions] == current).astype(jnp.float32)
        summed = (
            summed
            + conv_weight[tap_index][None, :]
            * mix_ext[tap_index : tap_index + positions]
            * same_doc[:, None]
        )
    activated = jax.nn.silu(summed)
    split_at = HK * DK
    queries = activated[:, :split_at].reshape(positions, HK, DK)
    keyset = activated[:, split_at : 2 * split_at].reshape(positions, HK, DK)
    values = activated[:, 2 * split_at :].reshape(positions, HV, DV)
    queries = (
        queries
        / jnp.sqrt(jnp.sum(queries * queries, axis=-1, keepdims=True) + 1e-06)
        / math.sqrt(DK)
    )
    keyset = keyset / jnp.sqrt(jnp.sum(keyset * keyset, axis=-1, keepdims=True) + 1e-06)
    repeats = HV // HK
    return (jnp.repeat(queries, repeats, axis=1), jnp.repeat(keyset, repeats, axis=1), values)


def unit_lower_inverse(strict_part):
    positions = strict_part.shape[-1]
    identity_matrix = jnp.eye(positions, dtype=jnp.float32)[None]
    result = identity_matrix - strict_part
    power = strict_part
    reach = 2
    while reach < positions:
        power = jnp.einsum("hij,hjk->hik", power, power, precision=HIGHEST)
        result = jnp.einsum("hij,hjk->hik", result, identity_matrix + power, precision=HIGHEST)
        reach = reach * 2
    return result


def block_parts(queries, keyset, values, log_decay, write_rate, segments, seg_before):
    positions = queries.shape[0]
    cumulative = jnp.cumsum(log_decay, axis=0)
    keep_state = (segments == seg_before).astype(jnp.float32)
    entering = jnp.exp(cumulative) * keep_state[:, None]
    token_position = lax.iota(jnp.int32, positions)
    same_doc = segments[:, None] == segments[None, :]
    strict = same_doc & (token_position[:, None] > token_position[None, :])
    causal = same_doc & (token_position[:, None] >= token_position[None, :])
    spread = cumulative.T[:, :, None] - cumulative.T[:, None, :]
    strict_decay = jnp.where(strict[None], jnp.exp(jnp.where(strict[None], spread, 0.0)), 0.0)
    causal_decay = jnp.where(causal[None], jnp.exp(jnp.where(causal[None], spread, 0.0)), 0.0)
    key_inner = jnp.einsum("ihd,jhd->hij", keyset, keyset, precision=HIGHEST)
    inverse = unit_lower_inverse(write_rate.T[:, :, None] * key_inner * strict_decay)
    targets = jnp.concatenate(
        [keyset * (write_rate * entering)[:, :, None], values * write_rate[:, :, None]], axis=2
    )
    solved = jnp.einsum("hij,hjd->hid", inverse, targets.transpose(1, 0, 2), precision=HIGHEST)
    write_keys = solved[:, :, :DK]
    write_values = solved[:, :, DK:]
    scores = jnp.einsum("ihd,jhd->hij", queries, keyset, precision=HIGHEST) * causal_decay
    final_sum = cumulative[-1]
    tail_decay = (
        jnp.exp(final_sum[None, :] - cumulative)
        * (segments == segments[-1]).astype(jnp.float32)[:, None]
    )
    carried = jnp.exp(final_sum) * keep_state[-1]
    tail_keys = (keyset * tail_decay[:, :, None]).transpose(1, 0, 2)
    queried = (queries * entering[:, :, None]).transpose(1, 0, 2)
    return (write_keys, write_values, scores, tail_keys, queried, carried)


@jax.custom_vjp
def lower_inverse(strict_part):
    return unit_lower_inverse(strict_part)


def lower_inverse_forward(strict_part):
    inverse = unit_lower_inverse(strict_part)
    return inverse, inverse


def lower_inverse_backward(inverse, grad_inverse):
    flipped = jnp.swapaxes(inverse, -1, -2)
    inner = jnp.einsum("hij,hjk->hik", flipped, grad_inverse, precision=HIGHEST)
    return (-jnp.einsum("hij,hjk->hik", inner, flipped, precision=HIGHEST),)


lower_inverse.defvjp(lower_inverse_forward, lower_inverse_backward)


def block_parts_heads(queries, keyset, values, log_decay, write_rate, segments, seg_before):
    positions = queries.shape[0]
    cumulative = jnp.cumsum(log_decay, axis=0)
    keep_state = (segments == seg_before).astype(jnp.float32)
    entering = jnp.exp(cumulative) * keep_state[:, None]
    token_position = lax.iota(jnp.int32, positions)
    same_doc = segments[:, None] == segments[None, :]
    strict = same_doc & (token_position[:, None] > token_position[None, :])
    causal = same_doc & (token_position[:, None] >= token_position[None, :])
    spread = cumulative.T[:, :, None] - cumulative.T[:, None, :]
    strict_decay = jnp.where(strict[None], jnp.exp(jnp.where(strict[None], spread, 0.0)), 0.0)
    causal_decay = jnp.where(causal[None], jnp.exp(jnp.where(causal[None], spread, 0.0)), 0.0)
    key_inner = jnp.einsum("ihd,jhd->hij", keyset, keyset, precision=HIGHEST)
    inverse = lower_inverse(write_rate.T[:, :, None] * key_inner * strict_decay)
    targets = jnp.concatenate(
        [keyset * (write_rate * entering)[:, :, None], values * write_rate[:, :, None]], axis=2
    )
    solved = jnp.einsum("hij,hjd->hid", inverse, targets.transpose(1, 0, 2), precision=HIGHEST)
    write_keys = solved[:, :, :DK]
    write_values = solved[:, :, DK:]
    scores = jnp.einsum("ihd,jhd->hij", queries, keyset, precision=HIGHEST) * causal_decay
    final_sum = cumulative[-1]
    tail_decay = (
        jnp.exp(final_sum[None, :] - cumulative)
        * (segments == segments[-1]).astype(jnp.float32)[:, None]
    )
    carried = jnp.exp(final_sum) * keep_state[-1]
    tail_keys = (keyset * tail_decay[:, :, None]).transpose(1, 0, 2)
    queried = (queries * entering[:, :, None]).transpose(1, 0, 2)
    return (write_keys, write_values, scores, tail_keys, queried, carried)


def block_map(block_data):
    write_keys, write_values, scores, tail_keys, queried, carried = block_data
    identity_matrix = jnp.eye(DK, dtype=jnp.float32)
    transform = carried[:, None, None] * identity_matrix[None] - jnp.einsum(
        "hcd,hce->hde", tail_keys, write_keys, precision=HIGHEST
    )
    shift_term = jnp.einsum("hcd,hce->hde", tail_keys, write_values, precision=HIGHEST)
    return (transform, shift_term)


def block_apply(block_data, state_in):
    write_keys, write_values, scores, tail_keys, queried, carried = block_data
    fresh_values = write_values - jnp.einsum(
        "hcd,hde->hce", write_keys, state_in, precision=HIGHEST
    )
    output = jnp.einsum("hcd,hde->hce", queried, state_in, precision=HIGHEST)
    output = output + jnp.einsum("hij,hje->hie", scores, fresh_values, precision=HIGHEST)
    state_next = carried[:, None, None] * state_in + jnp.einsum(
        "hcd,hce->hde", tail_keys, fresh_values, precision=HIGHEST
    )
    return (output, state_next)


def section_one(mix_ext, conv_weight, log_decay, write_rate, seg_ext):
    queries, keyset, values = prepare(mix_ext, seg_ext, conv_weight)
    margin = conv_weight.shape[0] - 1
    positions = log_decay.shape[0]
    blocks = positions // BLOCK
    segments = seg_ext[margin:]
    before = seg_ext[margin - 1 : margin - 1 + positions : BLOCK]

    def blocked(tensor):
        return tensor.reshape((blocks, BLOCK) + tensor.shape[1:])

    return jax.vmap(block_parts)(
        blocked(queries),
        blocked(keyset),
        blocked(values),
        blocked(log_decay),
        blocked(write_rate),
        blocked(segments),
        before,
    )


def section_two(parts, state_in):

    def step_block(state_now, block_data):
        output, state_next = block_apply(block_data, state_now)
        return (state_next, output)

    state_out, outputs = lax.scan(step_block, state_in, parts)
    blocks = outputs.shape[0]
    return (outputs.transpose(0, 2, 1, 3).reshape(blocks * BLOCK, HV * DV), state_out)


def summarize(parts):
    identity_matrix = jnp.eye(DK, dtype=jnp.float32)
    initial = (
        jnp.broadcast_to(identity_matrix, (HV, DK, DK)),
        jnp.zeros((HV, DK, DV), jnp.float32),
    )

    def fold_block(carried_map, block_data):
        transform, shift_term = block_map(block_data)
        merged = jnp.einsum("hij,hjk->hik", transform, carried_map[0], precision=HIGHEST)
        moved = (
            jnp.einsum("hij,hjk->hik", transform, carried_map[1], precision=HIGHEST) + shift_term
        )
        return ((merged, moved), None)

    result, unused = lax.scan(fold_block, initial, parts)
    return result


def compose(earlier_map, later_map):
    merged = jnp.einsum("shij,shjk->shik", later_map[0], earlier_map[0], precision=HIGHEST)
    moved = (
        jnp.einsum("shij,shjk->shik", later_map[0], earlier_map[1], precision=HIGHEST)
        + later_map[1]
    )
    return (merged, moved)


def local(mixed, conv_weight, log_decay, write_rate, segment_ids, cotangent):
    margin = conv_weight.shape[0] - 1
    shifted_rows, shifted_segs = from_behind(
        (mixed[:, -margin:, :], segment_ids[:, -margin:].astype(jnp.bfloat16)), "ctx", 1
    )
    mix_ext = jnp.concatenate([shifted_rows, mixed], axis=1).astype(jnp.float32)
    seg_ext = jnp.concatenate([shifted_segs.astype(jnp.int32), segment_ids], axis=1)

    def first_section(mix_in, weight_in, decay_in, rate_in):
        return jax.vmap(section_one, in_axes=(0, None, 0, 0, 0))(
            mix_in, weight_in, decay_in, rate_in, seg_ext
        )

    parts, first_pull = jax.vjp(first_section, mix_ext, conv_weight, log_decay, write_rate)
    transform, shift_term = jax.vmap(summarize)(parts)
    identity_pair = (
        jnp.broadcast_to(jnp.eye(transform.shape[-1], dtype=jnp.float32), transform.shape),
        jnp.zeros_like(shift_term),
    )
    incoming = prefix((transform, shift_term), "ctx", compose, identity_pair, False)[1]
    (outputs, leaving), second_pull = jax.vjp(jax.vmap(section_two), parts, incoming)
    part_grads, local_term = second_pull((cotangent.astype(jnp.float32), jnp.zeros_like(leaving)))
    flipped = jnp.swapaxes(transform, -1, -2)
    departing = prefix((flipped, local_term), "ctx", compose, identity_pair, True)[1]
    more_grads, unused_grad = second_pull((jnp.zeros_like(outputs), departing))
    total_parts = jax.tree.map(jnp.add, part_grads, more_grads)
    grad_mix, grad_weight, grad_decay, grad_rate = first_pull(total_parts)
    returned = from_behind(grad_mix[:, :margin, :].astype(jnp.bfloat16), "ctx", -1).astype(
        jnp.float32
    )
    own_grad = grad_mix[:, margin:, :]
    own_grad = jnp.concatenate(
        [own_grad[:, :-margin, :], own_grad[:, -margin:, :] + returned], axis=1
    )
    total_conv = lax.psum(grad_weight, ("dp", "ctx"))
    tokens_all = mixed.shape[0] * lax.axis_size("dp") * mixed.shape[1] * lax.axis_size("ctx")
    return (
        outputs.astype(jnp.bfloat16),
        own_grad.astype(jnp.bfloat16),
        grad_decay,
        grad_rate,
        total_conv / math.sqrt(tokens_all),
    )


def tree_sum(value, axis):
    count = lax.axis_size(axis)
    if count & (count - 1):
        return lax.psum(value, axis)
    step = 1
    while step < count:
        value = value + lax.ppermute(value, axis, [(i, i ^ step) for i in range(count)])
        step = step * 2
    return value


def prepare_heads(mix_ext, seg_ext, conv_weight, key_heads, value_heads):
    margin = conv_weight.shape[0] - 1
    positions = mix_ext.shape[0] - margin
    current = seg_ext[margin:]
    summed = jnp.zeros((positions, mix_ext.shape[1]), jnp.float32)
    for tap_index in range(margin + 1):
        same_doc = (seg_ext[tap_index : tap_index + positions] == current).astype(jnp.float32)
        summed = (
            summed
            + conv_weight[tap_index][None, :]
            * mix_ext[tap_index : tap_index + positions]
            * same_doc[:, None]
        )
    activated = jax.nn.silu(summed)
    split_at = key_heads * DK
    queries = activated[:, :split_at].reshape(positions, key_heads, DK)
    keyset = activated[:, split_at : 2 * split_at].reshape(positions, key_heads, DK)
    values = activated[:, 2 * split_at :].reshape(positions, value_heads, DV)
    queries = (
        queries
        / jnp.sqrt(jnp.sum(queries * queries, axis=-1, keepdims=True) + 1e-06)
        / math.sqrt(DK)
    )
    keyset = keyset / jnp.sqrt(jnp.sum(keyset * keyset, axis=-1, keepdims=True) + 1e-06)
    repeats = value_heads // key_heads
    return (jnp.repeat(queries, repeats, axis=1), jnp.repeat(keyset, repeats, axis=1), values)


def combine_maps(earlier, later):
    merged = jnp.einsum("...ij,...jk->...ik", later[0], earlier[0], precision=HIGHEST)
    moved = jnp.einsum("...ij,...jk->...ik", later[0], earlier[1], precision=HIGHEST) + later[1]
    return (merged, moved)


def inclusive_states(transform, shift_term):
    blocks = transform.shape[0]
    reach = 1
    while reach < blocks:
        moved = jnp.einsum(
            "bhij,bhjk->bhik", transform[reach:], shift_term[:-reach], precision=HIGHEST
        )
        shift_term = jnp.concatenate([shift_term[:reach], shift_term[reach:] + moved], axis=0)
        if 2 * reach < blocks:
            merged = jnp.einsum(
                "bhij,bhjk->bhik", transform[reach:], transform[:-reach], precision=HIGHEST
            )
            transform = jnp.concatenate([transform[:reach], merged], axis=0)
        reach = reach * 2
    return shift_term


@jax.custom_vjp
def entering_states(transform, shift_term):
    return entering_forward(transform, shift_term)[0]


def entering_forward(transform, shift_term):
    eye = jnp.broadcast_to(jnp.eye(transform.shape[-1], dtype=transform.dtype), transform[:1].shape)
    shifted_maps = jnp.concatenate([eye, transform[:-1]], axis=0)
    shifted_terms = jnp.concatenate([jnp.zeros_like(shift_term[:1]), shift_term[:-1]], axis=0)
    states = inclusive_states(shifted_maps, shifted_terms)
    return states, (transform, states)


def entering_backward(saved, grad_states):
    transform, states = saved
    flipped = jnp.swapaxes(transform, -1, -2)[::-1]
    total = inclusive_states(flipped, grad_states[::-1])[::-1]
    later = total[1:]
    grad_shift = jnp.concatenate([later, jnp.zeros_like(later[:1])], axis=0)
    grad_map = jnp.einsum("bhik,bhjk->bhij", later, states[:-1], precision=HIGHEST)
    grad_transform = jnp.concatenate([grad_map, jnp.zeros_like(transform[:1])], axis=0)
    return (grad_transform, grad_shift)


entering_states.defvjp(entering_forward, entering_backward)


def heads_forward(mix_in, weight_in, decay_in, rate_in, seg_ext, key_heads, value_heads):
    margin = weight_in.shape[0] - 1
    positions = decay_in.shape[0]
    blocks = positions // BLOCK
    mix_ext = jnp.concatenate([jnp.zeros((margin, mix_in.shape[1]), jnp.float32), mix_in], axis=0)
    queries, keyset, values = prepare_heads(mix_ext, seg_ext, weight_in, key_heads, value_heads)
    segments = seg_ext[margin:]
    before = seg_ext[margin - 1 : margin - 1 + positions : BLOCK]

    def blocked(tensor):
        return tensor.reshape((blocks, BLOCK) + tensor.shape[1:])

    parts = jax.vmap(block_parts_heads)(
        blocked(queries),
        blocked(keyset),
        blocked(values),
        blocked(decay_in),
        blocked(rate_in),
        blocked(segments),
        before,
    )
    transform, shift_term = jax.vmap(block_map)(parts)
    incoming = entering_states(transform, shift_term)
    outputs, unused = jax.vmap(block_apply)(parts, incoming)
    return outputs.transpose(0, 2, 1, 3).reshape(positions, value_heads * DV)


def heads_local(mixed, conv_weight, log_decay, write_rate, segment_ids, cotangent):
    if mixed.shape[0] != 1:
        return local(mixed, conv_weight, log_decay, write_rate, segment_ids, cotangent)
    count = lax.axis_size("ctx")
    mine = lax.axis_index("ctx")
    value_heads = HV // count
    key_heads = value_heads * HK // HV
    margin = conv_weight.shape[0] - 1
    rows = mixed.shape[1]
    length = rows * count
    qk_width = key_heads * DK
    v_width = value_heads * DV

    def to_heads(array, width):
        grouped = array.reshape(rows, count, width)
        return lax.all_to_all(grouped, "ctx", 1, 0, tiled=True).reshape(length, width)

    def to_rows(array, width):
        grouped = array.reshape(count, rows, 1, width)
        return lax.all_to_all(grouped, "ctx", 0, 2, tiled=True).reshape(rows, count, width)

    own = mixed[0]
    width = 2 * qk_width + v_width
    packed = jnp.concatenate(
        [
            own[:, : HK * DK].reshape(rows, count, qk_width),
            own[:, HK * DK : 2 * HK * DK].reshape(rows, count, qk_width),
            own[:, 2 * HK * DK :].reshape(rows, count, v_width),
            cotangent[0].reshape(rows, count, v_width),
        ],
        axis=-1,
    )
    wide = to_heads(packed, width + v_width)
    mix_heads = wide[:, :width].astype(jnp.float32)
    cot_heads = wide[:, width:].astype(jnp.float32)
    seg_columns = jnp.broadcast_to(
        segment_ids[0].astype(jnp.float32)[:, None, None], (rows, count, 1)
    )
    small = jnp.concatenate(
        [
            log_decay[0].reshape(rows, count, value_heads),
            write_rate[0].reshape(rows, count, value_heads),
            seg_columns,
        ],
        axis=-1,
    )
    narrow = to_heads(small, 2 * value_heads + 1)
    decay_heads = narrow[:, :value_heads]
    rate_heads = narrow[:, value_heads : 2 * value_heads]
    segments = narrow[:, 2 * value_heads].astype(jnp.int32)
    seg_ext = jnp.concatenate([jnp.full((margin,), -1, jnp.int32), segments])

    weight_q = conv_weight[:, : HK * DK].reshape(-1, count, qk_width)[:, mine]
    weight_k = conv_weight[:, HK * DK : 2 * HK * DK].reshape(-1, count, qk_width)[:, mine]
    weight_v = conv_weight[:, 2 * HK * DK :].reshape(-1, count, v_width)[:, mine]
    weight_heads = jnp.concatenate([weight_q, weight_k, weight_v], axis=-1)

    def forward(mix_in, weight_in, decay_in, rate_in):
        return heads_forward(
            mix_in, weight_in, decay_in, rate_in, seg_ext, key_heads, value_heads
        )

    outputs, pullback = jax.vjp(forward, mix_heads, weight_heads, decay_heads, rate_heads)
    grad_mix, grad_weight, grad_decay, grad_rate = pullback(cot_heads)

    joined = jnp.concatenate([outputs.astype(jnp.bfloat16), grad_mix.astype(jnp.bfloat16)], axis=-1)
    back = to_rows(joined, v_width + width)
    core = back[:, :, :v_width].reshape(1, rows, HV * DV)
    grad_rows = jnp.concatenate(
        [
            back[:, :, v_width : v_width + qk_width].reshape(rows, HK * DK),
            back[:, :, v_width + qk_width : v_width + 2 * qk_width].reshape(rows, HK * DK),
            back[:, :, v_width + 2 * qk_width :].reshape(rows, HV * DV),
        ],
        axis=-1,
    )[None]
    taps = conv_weight.shape[0]
    sequences = lax.axis_size("dp")
    mine_dp = lax.axis_index("dp")
    row_grads = jnp.concatenate([grad_decay, grad_rate], axis=-1).reshape(count, rows * 2 * value_heads)
    pieces = jnp.concatenate(
        [
            jnp.broadcast_to(row_grads[None], (sequences,) + row_grads.shape),
            jnp.broadcast_to(
                grad_weight.reshape(1, 1, taps * width), (sequences, count, taps * width)
            ),
        ],
        axis=-1,
    ).reshape(sequences * count, 1, rows * 2 * value_heads + taps * width)
    everything = lax.all_to_all(pieces, ("dp", "ctx"), 0, 1, tiled=True)[0]
    everything = everything.reshape(sequences, count, rows * 2 * value_heads + taps * width)
    weight_sum = everything[0, :, rows * 2 * value_heads :]
    for index in range(1, sequences):
        weight_sum = weight_sum + everything[index, :, rows * 2 * value_heads :]
    returned = jnp.concatenate(
        [lax.dynamic_index_in_dim(everything, mine_dp, 0, keepdims=False)[:, : rows * 2 * value_heads], weight_sum],
        axis=-1,
    )
    grads_small = returned[:, : rows * 2 * value_heads].reshape(count, rows, 2 * value_heads)
    grads_small = grads_small.transpose(1, 0, 2)
    decay_rows = grads_small[:, :, :value_heads].reshape(1, rows, HV)
    rate_rows = grads_small[:, :, value_heads:].reshape(1, rows, HV)
    conv_parts = returned[:, rows * 2 * value_heads :].reshape(count, taps, width).transpose(1, 0, 2)
    total_conv = jnp.concatenate(
        [
            conv_parts[:, :, :qk_width].reshape(taps, HK * DK),
            conv_parts[:, :, qk_width : 2 * qk_width].reshape(taps, HK * DK),
            conv_parts[:, :, 2 * qk_width :].reshape(taps, HV * DV),
        ],
        axis=-1,
    )
    tokens_all = mixed.shape[0] * sequences * length
    return (core, grad_rows, decay_rows, rate_rows, total_conv / math.sqrt(tokens_all))


def solution(mesh):
    in_specs = (
        P("dp", "ctx", None),
        P(),
        P("dp", "ctx", None),
        P("dp", "ctx", None),
        P("dp", "ctx"),
        P("dp", "ctx", None),
    )
    out_specs = (
        P("dp", "ctx", None),
        P("dp", "ctx", None),
        P("dp", "ctx", None),
        P("dp", "ctx", None),
        P(),
    )
    count = mesh.shape["ctx"]
    per_device = HV // count if HV % count == 0 else 0
    chosen = heads_local if per_device and (per_device * HK) % HV == 0 else local
    return jax.shard_map(chosen, mesh=mesh, in_specs=in_specs, out_specs=out_specs, check_vma=False)
```

```python
import math

import jax
import jax.numpy as jnp
from jax import lax
from jax.sharding import PartitionSpec as P

HK = 8
HV = 16
DK = 128
DV = 128
BLOCK = 64


HIGHEST = lax.Precision.HIGHEST
FAST = lax.Precision.HIGH


def from_behind(x, axis, by):
    size = lax.axis_size(axis)
    pairs = [(i, i + by) for i in range(size) if 0 <= i + by < size]
    return lax.ppermute(x, axis, pairs)


def prefix(value, axis, join, neutral, backward):
    count, mine = (lax.axis_size(axis), lax.axis_index(axis))
    pieces = jax.tree.map(lambda part: lax.all_gather(part, axis), value)
    if backward:
        pieces = jax.tree.map(lambda part: part[::-1], pieces)
        mine = count - 1 - mine
    total = jax.tree.map(
        lambda part, zero: jnp.full_like(part, 0) + jnp.asarray(zero, part.dtype), value, neutral
    )

    def hop(position, total):
        longer = join(total, jax.tree.map(lambda part: part[position], pieces))
        return jax.tree.map(lambda new, old: jnp.where(position < mine, new, old), longer, total)

    return lax.fori_loop(0, count - 1, hop, total)


def prepare(mix_ext, seg_ext, conv_weight):
    margin = conv_weight.shape[0] - 1
    positions = mix_ext.shape[0] - margin
    current = seg_ext[margin:]
    summed = jnp.zeros((positions, mix_ext.shape[1]), jnp.float32)
    for tap_index in range(margin + 1):
        same_doc = (seg_ext[tap_index : tap_index + positions] == current).astype(jnp.float32)
        summed = (
            summed
            + conv_weight[tap_index][None, :]
            * mix_ext[tap_index : tap_index + positions]
            * same_doc[:, None]
        )
    activated = jax.nn.silu(summed)
    split_at = HK * DK
    queries = activated[:, :split_at].reshape(positions, HK, DK)
    keyset = activated[:, split_at : 2 * split_at].reshape(positions, HK, DK)
    values = activated[:, 2 * split_at :].reshape(positions, HV, DV)
    queries = (
        queries
        / jnp.sqrt(jnp.sum(queries * queries, axis=-1, keepdims=True) + 1e-06)
        / math.sqrt(DK)
    )
    keyset = keyset / jnp.sqrt(jnp.sum(keyset * keyset, axis=-1, keepdims=True) + 1e-06)
    repeats = HV // HK
    return (jnp.repeat(queries, repeats, axis=1), jnp.repeat(keyset, repeats, axis=1), values)


def unit_lower_inverse(strict_part):
    positions = strict_part.shape[-1]
    identity_matrix = jnp.eye(positions, dtype=jnp.float32)[None]
    result = identity_matrix - strict_part
    power = strict_part
    reach = 2
    while reach < positions:
        power = jnp.einsum("hij,hjk->hik", power, power, precision=HIGHEST)
        result = jnp.einsum("hij,hjk->hik", result, identity_matrix + power, precision=HIGHEST)
        reach = reach * 2
    return result


def block_parts(queries, keyset, values, log_decay, write_rate, segments, seg_before):
    positions = queries.shape[0]
    cumulative = jnp.cumsum(log_decay, axis=0)
    keep_state = (segments == seg_before).astype(jnp.float32)
    entering = jnp.exp(cumulative) * keep_state[:, None]
    token_position = lax.iota(jnp.int32, positions)
    same_doc = segments[:, None] == segments[None, :]
    strict = same_doc & (token_position[:, None] > token_position[None, :])
    causal = same_doc & (token_position[:, None] >= token_position[None, :])
    spread = cumulative.T[:, :, None] - cumulative.T[:, None, :]
    strict_decay = jnp.where(strict[None], jnp.exp(jnp.where(strict[None], spread, 0.0)), 0.0)
    causal_decay = jnp.where(causal[None], jnp.exp(jnp.where(causal[None], spread, 0.0)), 0.0)
    key_inner = jnp.einsum("ihd,jhd->hij", keyset, keyset, precision=HIGHEST)
    inverse = unit_lower_inverse(write_rate.T[:, :, None] * key_inner * strict_decay)
    targets = jnp.concatenate(
        [keyset * (write_rate * entering)[:, :, None], values * write_rate[:, :, None]], axis=2
    )
    solved = jnp.einsum("hij,hjd->hid", inverse, targets.transpose(1, 0, 2), precision=HIGHEST)
    write_keys = solved[:, :, :DK]
    write_values = solved[:, :, DK:]
    scores = jnp.einsum("ihd,jhd->hij", queries, keyset, precision=HIGHEST) * causal_decay
    final_sum = cumulative[-1]
    tail_decay = (
        jnp.exp(final_sum[None, :] - cumulative)
        * (segments == segments[-1]).astype(jnp.float32)[:, None]
    )
    carried = jnp.exp(final_sum) * keep_state[-1]
    tail_keys = (keyset * tail_decay[:, :, None]).transpose(1, 0, 2)
    queried = (queries * entering[:, :, None]).transpose(1, 0, 2)
    return (write_keys, write_values, scores, tail_keys, queried, carried)


@jax.custom_vjp
def lower_inverse(strict_part):
    return unit_lower_inverse_fast(strict_part)


def lower_inverse_forward(strict_part):
    inverse = unit_lower_inverse_fast(strict_part)
    return inverse, inverse


def lower_inverse_backward(inverse, grad_inverse):
    flipped = jnp.swapaxes(inverse, -1, -2)
    inner = jnp.einsum("hij,hjk->hik", flipped, grad_inverse, precision=FAST)
    return (-jnp.einsum("hij,hjk->hik", inner, flipped, precision=FAST),)


lower_inverse.defvjp(lower_inverse_forward, lower_inverse_backward)


def block_parts_heads(queries, keyset, values, log_decay, write_rate, segments, seg_before):
    positions = queries.shape[0]
    cumulative = jnp.cumsum(log_decay, axis=0)
    keep_state = (segments == seg_before).astype(jnp.float32)
    entering = jnp.exp(cumulative) * keep_state[:, None]
    token_position = lax.iota(jnp.int32, positions)
    same_doc = segments[:, None] == segments[None, :]
    strict = same_doc & (token_position[:, None] > token_position[None, :])
    causal = same_doc & (token_position[:, None] >= token_position[None, :])
    spread = cumulative.T[:, :, None] - cumulative.T[:, None, :]
    strict_decay = jnp.where(strict[None], jnp.exp(jnp.where(strict[None], spread, 0.0)), 0.0)
    causal_decay = jnp.where(causal[None], jnp.exp(jnp.where(causal[None], spread, 0.0)), 0.0)
    key_inner = jnp.einsum("ihd,jhd->hij", keyset, keyset, precision=FAST)
    inverse = lower_inverse(write_rate.T[:, :, None] * key_inner * strict_decay)
    targets = jnp.concatenate(
        [keyset * (write_rate * entering)[:, :, None], values * write_rate[:, :, None]], axis=2
    )
    solved = jnp.einsum("hij,hjd->hid", inverse, targets.transpose(1, 0, 2), precision=FAST)
    write_keys = solved[:, :, :DK]
    write_values = solved[:, :, DK:]
    scores = jnp.einsum("ihd,jhd->hij", queries, keyset, precision=FAST) * causal_decay
    final_sum = cumulative[-1]
    tail_decay = (
        jnp.exp(final_sum[None, :] - cumulative)
        * (segments == segments[-1]).astype(jnp.float32)[:, None]
    )
    carried = jnp.exp(final_sum) * keep_state[-1]
    tail_keys = (keyset * tail_decay[:, :, None]).transpose(1, 0, 2)
    queried = (queries * entering[:, :, None]).transpose(1, 0, 2)
    return (write_keys, write_values, scores, tail_keys, queried, carried)


def block_map(block_data):
    write_keys, write_values, scores, tail_keys, queried, carried = block_data
    identity_matrix = jnp.eye(DK, dtype=jnp.float32)
    transform = carried[:, None, None] * identity_matrix[None] - jnp.einsum(
        "hcd,hce->hde", tail_keys, write_keys, precision=HIGHEST
    )
    shift_term = jnp.einsum("hcd,hce->hde", tail_keys, write_values, precision=HIGHEST)
    return (transform, shift_term)


def block_apply(block_data, state_in):
    write_keys, write_values, scores, tail_keys, queried, carried = block_data
    fresh_values = write_values - jnp.einsum(
        "hcd,hde->hce", write_keys, state_in, precision=HIGHEST
    )
    output = jnp.einsum("hcd,hde->hce", queried, state_in, precision=HIGHEST)
    output = output + jnp.einsum("hij,hje->hie", scores, fresh_values, precision=HIGHEST)
    state_next = carried[:, None, None] * state_in + jnp.einsum(
        "hcd,hce->hde", tail_keys, fresh_values, precision=HIGHEST
    )
    return (output, state_next)

def unit_lower_inverse_fast(strict_part):
    positions = strict_part.shape[-1]
    identity_matrix = jnp.eye(positions, dtype=jnp.float32)[None]
    result = identity_matrix - strict_part
    power = strict_part
    reach = 2
    while reach < positions:
        power = jnp.einsum("hij,hjk->hik", power, power, precision=FAST)
        result = jnp.einsum("hij,hjk->hik", result, identity_matrix + power, precision=FAST)
        reach = reach * 2
    return result


def block_map_fast(block_data):
    write_keys, write_values, scores, tail_keys, queried, carried = block_data
    identity_matrix = jnp.eye(DK, dtype=jnp.float32)
    transform = carried[:, None, None] * identity_matrix[None] - jnp.einsum(
        "hcd,hce->hde", tail_keys, write_keys, precision=FAST
    )
    shift_term = jnp.einsum("hcd,hce->hde", tail_keys, write_values, precision=FAST)
    return (transform, shift_term)


def block_apply_fast(block_data, state_in):
    write_keys, write_values, scores, tail_keys, queried, carried = block_data
    fresh_values = write_values - jnp.einsum(
        "hcd,hde->hce", write_keys, state_in, precision=FAST
    )
    output = jnp.einsum("hcd,hde->hce", queried, state_in, precision=FAST)
    output = output + jnp.einsum("hij,hje->hie", scores, fresh_values, precision=FAST)
    state_next = carried[:, None, None] * state_in + jnp.einsum(
        "hcd,hce->hde", tail_keys, fresh_values, precision=FAST
    )
    return (output, state_next)


def section_one(mix_ext, conv_weight, log_decay, write_rate, seg_ext):
    queries, keyset, values = prepare(mix_ext, seg_ext, conv_weight)
    margin = conv_weight.shape[0] - 1
    positions = log_decay.shape[0]
    blocks = positions // BLOCK
    segments = seg_ext[margin:]
    before = seg_ext[margin - 1 : margin - 1 + positions : BLOCK]

    def blocked(tensor):
        return tensor.reshape((blocks, BLOCK) + tensor.shape[1:])

    return jax.vmap(block_parts)(
        blocked(queries),
        blocked(keyset),
        blocked(values),
        blocked(log_decay),
        blocked(write_rate),
        blocked(segments),
        before,
    )


def section_two(parts, state_in):

    def step_block(state_now, block_data):
        output, state_next = block_apply(block_data, state_now)
        return (state_next, output)

    state_out, outputs = lax.scan(step_block, state_in, parts)
    blocks = outputs.shape[0]
    return (outputs.transpose(0, 2, 1, 3).reshape(blocks * BLOCK, HV * DV), state_out)


def summarize(parts):
    identity_matrix = jnp.eye(DK, dtype=jnp.float32)
    initial = (
        jnp.broadcast_to(identity_matrix, (HV, DK, DK)),
        jnp.zeros((HV, DK, DV), jnp.float32),
    )

    def fold_block(carried_map, block_data):
        transform, shift_term = block_map(block_data)
        merged = jnp.einsum("hij,hjk->hik", transform, carried_map[0], precision=HIGHEST)
        moved = (
            jnp.einsum("hij,hjk->hik", transform, carried_map[1], precision=HIGHEST) + shift_term
        )
        return ((merged, moved), None)

    result, unused = lax.scan(fold_block, initial, parts)
    return result


def compose(earlier_map, later_map):
    merged = jnp.einsum("shij,shjk->shik", later_map[0], earlier_map[0], precision=HIGHEST)
    moved = (
        jnp.einsum("shij,shjk->shik", later_map[0], earlier_map[1], precision=HIGHEST)
        + later_map[1]
    )
    return (merged, moved)


def local(mixed, conv_weight, log_decay, write_rate, segment_ids, cotangent):
    margin = conv_weight.shape[0] - 1
    shifted_rows, shifted_segs = from_behind(
        (mixed[:, -margin:, :], segment_ids[:, -margin:].astype(jnp.bfloat16)), "ctx", 1
    )
    mix_ext = jnp.concatenate([shifted_rows, mixed], axis=1).astype(jnp.float32)
    seg_ext = jnp.concatenate([shifted_segs.astype(jnp.int32), segment_ids], axis=1)

    def first_section(mix_in, weight_in, decay_in, rate_in):
        return jax.vmap(section_one, in_axes=(0, None, 0, 0, 0))(
            mix_in, weight_in, decay_in, rate_in, seg_ext
        )

    parts, first_pull = jax.vjp(first_section, mix_ext, conv_weight, log_decay, write_rate)
    transform, shift_term = jax.vmap(summarize)(parts)
    identity_pair = (
        jnp.broadcast_to(jnp.eye(transform.shape[-1], dtype=jnp.float32), transform.shape),
        jnp.zeros_like(shift_term),
    )
    incoming = prefix((transform, shift_term), "ctx", compose, identity_pair, False)[1]
    (outputs, leaving), second_pull = jax.vjp(jax.vmap(section_two), parts, incoming)
    part_grads, local_term = second_pull((cotangent.astype(jnp.float32), jnp.zeros_like(leaving)))
    flipped = jnp.swapaxes(transform, -1, -2)
    departing = prefix((flipped, local_term), "ctx", compose, identity_pair, True)[1]
    more_grads, unused_grad = second_pull((jnp.zeros_like(outputs), departing))
    total_parts = jax.tree.map(jnp.add, part_grads, more_grads)
    grad_mix, grad_weight, grad_decay, grad_rate = first_pull(total_parts)
    returned = from_behind(grad_mix[:, :margin, :].astype(jnp.bfloat16), "ctx", -1).astype(
        jnp.float32
    )
    own_grad = grad_mix[:, margin:, :]
    own_grad = jnp.concatenate(
        [own_grad[:, :-margin, :], own_grad[:, -margin:, :] + returned], axis=1
    )
    total_conv = lax.psum(grad_weight, ("dp", "ctx"))
    tokens_all = mixed.shape[0] * lax.axis_size("dp") * mixed.shape[1] * lax.axis_size("ctx")
    return (
        outputs.astype(jnp.bfloat16),
        own_grad.astype(jnp.bfloat16),
        grad_decay,
        grad_rate,
        total_conv / math.sqrt(tokens_all),
    )


def tree_sum(value, axis):
    count = lax.axis_size(axis)
    if count & (count - 1):
        return lax.psum(value, axis)
    step = 1
    while step < count:
        value = value + lax.ppermute(value, axis, [(i, i ^ step) for i in range(count)])
        step = step * 2
    return value


def prepare_heads(mix_ext, seg_ext, conv_weight, key_heads, value_heads):
    margin = conv_weight.shape[0] - 1
    positions = mix_ext.shape[0] - margin
    current = seg_ext[margin:]
    summed = jnp.zeros((positions, mix_ext.shape[1]), jnp.float32)
    for tap_index in range(margin + 1):
        same_doc = (seg_ext[tap_index : tap_index + positions] == current).astype(jnp.float32)
        summed = (
            summed
            + conv_weight[tap_index][None, :]
            * mix_ext[tap_index : tap_index + positions]
            * same_doc[:, None]
        )
    activated = jax.nn.silu(summed)
    split_at = key_heads * DK
    queries = activated[:, :split_at].reshape(positions, key_heads, DK)
    keyset = activated[:, split_at : 2 * split_at].reshape(positions, key_heads, DK)
    values = activated[:, 2 * split_at :].reshape(positions, value_heads, DV)
    queries = (
        queries
        / jnp.sqrt(jnp.sum(queries * queries, axis=-1, keepdims=True) + 1e-06)
        / math.sqrt(DK)
    )
    keyset = keyset / jnp.sqrt(jnp.sum(keyset * keyset, axis=-1, keepdims=True) + 1e-06)
    repeats = value_heads // key_heads
    return (jnp.repeat(queries, repeats, axis=1), jnp.repeat(keyset, repeats, axis=1), values)


def combine_maps(earlier, later):
    merged = jnp.einsum("...ij,...jk->...ik", later[0], earlier[0], precision=HIGHEST)
    moved = jnp.einsum("...ij,...jk->...ik", later[0], earlier[1], precision=HIGHEST) + later[1]
    return (merged, moved)


def inclusive_states(transform, shift_term):
    blocks = transform.shape[0]
    reach = 1
    while reach < blocks:
        moved = jnp.einsum(
            "bhij,bhjk->bhik", transform[reach:], shift_term[:-reach], precision=FAST
        )
        shift_term = jnp.concatenate([shift_term[:reach], shift_term[reach:] + moved], axis=0)
        if 2 * reach < blocks:
            merged = jnp.einsum(
                "bhij,bhjk->bhik", transform[reach:], transform[:-reach], precision=FAST
            )
            transform = jnp.concatenate([transform[:reach], merged], axis=0)
        reach = reach * 2
    return shift_term


@jax.custom_vjp
def entering_states(transform, shift_term):
    return entering_forward(transform, shift_term)[0]


def entering_forward(transform, shift_term):
    eye = jnp.broadcast_to(jnp.eye(transform.shape[-1], dtype=transform.dtype), transform[:1].shape)
    shifted_maps = jnp.concatenate([eye, transform[:-1]], axis=0)
    shifted_terms = jnp.concatenate([jnp.zeros_like(shift_term[:1]), shift_term[:-1]], axis=0)
    states = inclusive_states(shifted_maps, shifted_terms)
    return states, (transform, states)


def entering_backward(saved, grad_states):
    transform, states = saved
    flipped = jnp.swapaxes(transform, -1, -2)[::-1]
    total = inclusive_states(flipped, grad_states[::-1])[::-1]
    later = total[1:]
    grad_shift = jnp.concatenate([later, jnp.zeros_like(later[:1])], axis=0)
    grad_map = jnp.einsum("bhik,bhjk->bhij", later, states[:-1], precision=FAST)
    grad_transform = jnp.concatenate([grad_map, jnp.zeros_like(transform[:1])], axis=0)
    return (grad_transform, grad_shift)


entering_states.defvjp(entering_forward, entering_backward)


def heads_forward(mix_in, weight_in, decay_in, rate_in, seg_ext, key_heads, value_heads):
    margin = weight_in.shape[0] - 1
    positions = decay_in.shape[0]
    blocks = positions // BLOCK
    mix_ext = jnp.concatenate([jnp.zeros((margin, mix_in.shape[1]), jnp.float32), mix_in], axis=0)
    queries, keyset, values = prepare_heads(mix_ext, seg_ext, weight_in, key_heads, value_heads)
    segments = seg_ext[margin:]
    before = seg_ext[margin - 1 : margin - 1 + positions : BLOCK]

    def blocked(tensor):
        return tensor.reshape((blocks, BLOCK) + tensor.shape[1:])

    parts = jax.vmap(block_parts_heads)(
        blocked(queries),
        blocked(keyset),
        blocked(values),
        blocked(decay_in),
        blocked(rate_in),
        blocked(segments),
        before,
    )
    transform, shift_term = jax.vmap(block_map_fast)(parts)
    incoming = entering_states(transform, shift_term)
    outputs, unused = jax.vmap(block_apply_fast)(parts, incoming)
    return outputs.transpose(0, 2, 1, 3).reshape(positions, value_heads * DV)


def heads_local(mixed, conv_weight, log_decay, write_rate, segment_ids, cotangent):
    if mixed.shape[0] != 1:
        return local(mixed, conv_weight, log_decay, write_rate, segment_ids, cotangent)
    count = lax.axis_size("ctx")
    mine = lax.axis_index("ctx")
    value_heads = HV // count
    key_heads = value_heads * HK // HV
    margin = conv_weight.shape[0] - 1
    rows = mixed.shape[1]
    length = rows * count
    qk_width = key_heads * DK
    v_width = value_heads * DV

    def to_heads(array, width):
        grouped = array.reshape(rows, count, width)
        return lax.all_to_all(grouped, "ctx", 1, 0, tiled=True).reshape(length, width)

    def to_rows(array, width):
        grouped = array.reshape(count, rows, 1, width)
        return lax.all_to_all(grouped, "ctx", 0, 2, tiled=True).reshape(rows, count, width)

    own = mixed[0]
    width = 2 * qk_width + v_width
    packed = jnp.concatenate(
        [
            own[:, : HK * DK].reshape(rows, count, qk_width),
            own[:, HK * DK : 2 * HK * DK].reshape(rows, count, qk_width),
            own[:, 2 * HK * DK :].reshape(rows, count, v_width),
            cotangent[0].reshape(rows, count, v_width),
        ],
        axis=-1,
    )
    wide = to_heads(packed, width + v_width)
    mix_heads = wide[:, :width].astype(jnp.float32)
    cot_heads = wide[:, width:].astype(jnp.float32)
    seg_columns = jnp.broadcast_to(
        segment_ids[0].astype(jnp.float32)[:, None, None], (rows, count, 1)
    )
    small = jnp.concatenate(
        [
            log_decay[0].reshape(rows, count, value_heads),
            write_rate[0].reshape(rows, count, value_heads),
            seg_columns,
        ],
        axis=-1,
    )
    narrow = to_heads(small, 2 * value_heads + 1)
    decay_heads = narrow[:, :value_heads]
    rate_heads = narrow[:, value_heads : 2 * value_heads]
    segments = narrow[:, 2 * value_heads].astype(jnp.int32)
    seg_ext = jnp.concatenate([jnp.full((margin,), -1, jnp.int32), segments])

    weight_q = conv_weight[:, : HK * DK].reshape(-1, count, qk_width)[:, mine]
    weight_k = conv_weight[:, HK * DK : 2 * HK * DK].reshape(-1, count, qk_width)[:, mine]
    weight_v = conv_weight[:, 2 * HK * DK :].reshape(-1, count, v_width)[:, mine]
    weight_heads = jnp.concatenate([weight_q, weight_k, weight_v], axis=-1)

    def forward(mix_in, weight_in, decay_in, rate_in):
        return heads_forward(
            mix_in, weight_in, decay_in, rate_in, seg_ext, key_heads, value_heads
        )

    outputs, pullback = jax.vjp(forward, mix_heads, weight_heads, decay_heads, rate_heads)
    grad_mix, grad_weight, grad_decay, grad_rate = pullback(cot_heads)

    joined = jnp.concatenate([outputs.astype(jnp.bfloat16), grad_mix.astype(jnp.bfloat16)], axis=-1)
    back = to_rows(joined, v_width + width)
    core = back[:, :, :v_width].reshape(1, rows, HV * DV)
    grad_rows = jnp.concatenate(
        [
            back[:, :, v_width : v_width + qk_width].reshape(rows, HK * DK),
            back[:, :, v_width + qk_width : v_width + 2 * qk_width].reshape(rows, HK * DK),
            back[:, :, v_width + 2 * qk_width :].reshape(rows, HV * DV),
        ],
        axis=-1,
    )[None]
    taps = conv_weight.shape[0]
    sequences = lax.axis_size("dp")
    mine_dp = lax.axis_index("dp")
    row_grads = jnp.concatenate([grad_decay, grad_rate], axis=-1).reshape(count, rows * 2 * value_heads)
    pieces = jnp.concatenate(
        [
            jnp.broadcast_to(row_grads[None], (sequences,) + row_grads.shape),
            jnp.broadcast_to(
                grad_weight.reshape(1, 1, taps * width), (sequences, count, taps * width)
            ),
        ],
        axis=-1,
    ).reshape(sequences * count, 1, rows * 2 * value_heads + taps * width)
    everything = lax.all_to_all(pieces, ("dp", "ctx"), 0, 1, tiled=True)[0]
    everything = everything.reshape(sequences, count, rows * 2 * value_heads + taps * width)
    weight_sum = everything[0, :, rows * 2 * value_heads :]
    for index in range(1, sequences):
        weight_sum = weight_sum + everything[index, :, rows * 2 * value_heads :]
    returned = jnp.concatenate(
        [lax.dynamic_index_in_dim(everything, mine_dp, 0, keepdims=False)[:, : rows * 2 * value_heads], weight_sum],
        axis=-1,
    )
    grads_small = returned[:, : rows * 2 * value_heads].reshape(count, rows, 2 * value_heads)
    grads_small = grads_small.transpose(1, 0, 2)
    decay_rows = grads_small[:, :, :value_heads].reshape(1, rows, HV)
    rate_rows = grads_small[:, :, value_heads:].reshape(1, rows, HV)
    conv_parts = returned[:, rows * 2 * value_heads :].reshape(count, taps, width).transpose(1, 0, 2)
    total_conv = jnp.concatenate(
        [
            conv_parts[:, :, :qk_width].reshape(taps, HK * DK),
            conv_parts[:, :, qk_width : 2 * qk_width].reshape(taps, HK * DK),
            conv_parts[:, :, 2 * qk_width :].reshape(taps, HV * DV),
        ],
        axis=-1,
    )
    tokens_all = mixed.shape[0] * sequences * length
    return (core, grad_rows, decay_rows, rate_rows, total_conv / math.sqrt(tokens_all))


def solution(mesh):
    in_specs = (
        P("dp", "ctx", None),
        P(),
        P("dp", "ctx", None),
        P("dp", "ctx", None),
        P("dp", "ctx"),
        P("dp", "ctx", None),
    )
    out_specs = (
        P("dp", "ctx", None),
        P("dp", "ctx", None),
        P("dp", "ctx", None),
        P("dp", "ctx", None),
        P(),
    )
    count = mesh.shape["ctx"]
    per_device = HV // count if HV % count == 0 else 0
    chosen = heads_local if per_device and (per_device * HK) % HV == 0 else local
    return jax.shard_map(chosen, mesh=mesh, in_specs=in_specs, out_specs=out_specs, check_vma=False)
```

```python
import math

import jax
import jax.numpy as jnp
from jax import lax
from jax.sharding import PartitionSpec as P

HK = 8
HV = 16
DK = 128
DV = 128
BLOCK = 64


HIGHEST = lax.Precision.HIGHEST
FAST = lax.Precision.HIGH


def from_behind(x, axis, by):
    size = lax.axis_size(axis)
    pairs = [(i, i + by) for i in range(size) if 0 <= i + by < size]
    return lax.ppermute(x, axis, pairs)


def prefix(value, axis, join, neutral, backward):
    count, mine = (lax.axis_size(axis), lax.axis_index(axis))
    pieces = jax.tree.map(lambda part: lax.all_gather(part, axis), value)
    if backward:
        pieces = jax.tree.map(lambda part: part[::-1], pieces)
        mine = count - 1 - mine
    total = jax.tree.map(
        lambda part, zero: jnp.full_like(part, 0) + jnp.asarray(zero, part.dtype), value, neutral
    )

    def hop(position, total):
        longer = join(total, jax.tree.map(lambda part: part[position], pieces))
        return jax.tree.map(lambda new, old: jnp.where(position < mine, new, old), longer, total)

    return lax.fori_loop(0, count - 1, hop, total)


def prepare(mix_ext, seg_ext, conv_weight):
    margin = conv_weight.shape[0] - 1
    positions = mix_ext.shape[0] - margin
    current = seg_ext[margin:]
    summed = jnp.zeros((positions, mix_ext.shape[1]), jnp.float32)
    for tap_index in range(margin + 1):
        same_doc = (seg_ext[tap_index : tap_index + positions] == current).astype(jnp.float32)
        summed = (
            summed
            + conv_weight[tap_index][None, :]
            * mix_ext[tap_index : tap_index + positions]
            * same_doc[:, None]
        )
    activated = jax.nn.silu(summed)
    split_at = HK * DK
    queries = activated[:, :split_at].reshape(positions, HK, DK)
    keyset = activated[:, split_at : 2 * split_at].reshape(positions, HK, DK)
    values = activated[:, 2 * split_at :].reshape(positions, HV, DV)
    queries = (
        queries
        / jnp.sqrt(jnp.sum(queries * queries, axis=-1, keepdims=True) + 1e-06)
        / math.sqrt(DK)
    )
    keyset = keyset / jnp.sqrt(jnp.sum(keyset * keyset, axis=-1, keepdims=True) + 1e-06)
    repeats = HV // HK
    return (jnp.repeat(queries, repeats, axis=1), jnp.repeat(keyset, repeats, axis=1), values)


def unit_lower_inverse(strict_part):
    positions = strict_part.shape[-1]
    identity_matrix = jnp.eye(positions, dtype=jnp.float32)[None]
    result = identity_matrix - strict_part
    power = strict_part
    reach = 2
    while reach < positions:
        power = jnp.einsum("hij,hjk->hik", power, power, precision=HIGHEST)
        result = jnp.einsum("hij,hjk->hik", result, identity_matrix + power, precision=HIGHEST)
        reach = reach * 2
    return result


def block_parts(queries, keyset, values, log_decay, write_rate, segments, seg_before):
    positions = queries.shape[0]
    cumulative = jnp.cumsum(log_decay, axis=0)
    keep_state = (segments == seg_before).astype(jnp.float32)
    entering = jnp.exp(cumulative) * keep_state[:, None]
    token_position = lax.iota(jnp.int32, positions)
    same_doc = segments[:, None] == segments[None, :]
    strict = same_doc & (token_position[:, None] > token_position[None, :])
    causal = same_doc & (token_position[:, None] >= token_position[None, :])
    spread = cumulative.T[:, :, None] - cumulative.T[:, None, :]
    strict_decay = jnp.where(strict[None], jnp.exp(jnp.where(strict[None], spread, 0.0)), 0.0)
    causal_decay = jnp.where(causal[None], jnp.exp(jnp.where(causal[None], spread, 0.0)), 0.0)
    key_inner = jnp.einsum("ihd,jhd->hij", keyset, keyset, precision=HIGHEST)
    inverse = unit_lower_inverse(write_rate.T[:, :, None] * key_inner * strict_decay)
    targets = jnp.concatenate(
        [keyset * (write_rate * entering)[:, :, None], values * write_rate[:, :, None]], axis=2
    )
    solved = jnp.einsum("hij,hjd->hid", inverse, targets.transpose(1, 0, 2), precision=HIGHEST)
    write_keys = solved[:, :, :DK]
    write_values = solved[:, :, DK:]
    scores = jnp.einsum("ihd,jhd->hij", queries, keyset, precision=HIGHEST) * causal_decay
    final_sum = cumulative[-1]
    tail_decay = (
        jnp.exp(final_sum[None, :] - cumulative)
        * (segments == segments[-1]).astype(jnp.float32)[:, None]
    )
    carried = jnp.exp(final_sum) * keep_state[-1]
    tail_keys = (keyset * tail_decay[:, :, None]).transpose(1, 0, 2)
    queried = (queries * entering[:, :, None]).transpose(1, 0, 2)
    return (write_keys, write_values, scores, tail_keys, queried, carried)


@jax.custom_vjp
def lower_inverse(strict_part):
    return unit_lower_inverse_fast(strict_part)


def lower_inverse_forward(strict_part):
    inverse = unit_lower_inverse_fast(strict_part)
    return inverse, inverse


def lower_inverse_backward(inverse, grad_inverse):
    flipped = jnp.swapaxes(inverse, -1, -2)
    inner = jnp.einsum("hij,hjk->hik", flipped, grad_inverse, precision=HIGHEST)
    return (-jnp.einsum("hij,hjk->hik", inner, flipped, precision=HIGHEST),)


lower_inverse.defvjp(lower_inverse_forward, lower_inverse_backward)


def block_parts_heads(queries, keyset, values, log_decay, write_rate, segments, seg_before):
    positions = queries.shape[0]
    cumulative = jnp.cumsum(log_decay, axis=0)
    keep_state = (segments == seg_before).astype(jnp.float32)
    entering = jnp.exp(cumulative) * keep_state[:, None]
    token_position = lax.iota(jnp.int32, positions)
    same_doc = segments[:, None] == segments[None, :]
    strict = same_doc & (token_position[:, None] > token_position[None, :])
    causal = same_doc & (token_position[:, None] >= token_position[None, :])
    spread = cumulative.T[:, :, None] - cumulative.T[:, None, :]
    strict_decay = jnp.where(strict[None], jnp.exp(jnp.where(strict[None], spread, 0.0)), 0.0)
    causal_decay = jnp.where(causal[None], jnp.exp(jnp.where(causal[None], spread, 0.0)), 0.0)
    key_inner = jnp.einsum("ihd,jhd->hij", keyset, keyset, precision=HIGHEST)
    inverse = lower_inverse(write_rate.T[:, :, None] * key_inner * strict_decay)
    targets = jnp.concatenate(
        [keyset * (write_rate * entering)[:, :, None], values * write_rate[:, :, None]], axis=2
    )
    solved = jnp.einsum("hij,hjd->hid", inverse, targets.transpose(1, 0, 2), precision=HIGHEST)
    write_keys = solved[:, :, :DK]
    write_values = solved[:, :, DK:]
    scores = jnp.einsum("ihd,jhd->hij", queries, keyset, precision=HIGHEST) * causal_decay
    final_sum = cumulative[-1]
    tail_decay = (
        jnp.exp(final_sum[None, :] - cumulative)
        * (segments == segments[-1]).astype(jnp.float32)[:, None]
    )
    carried = jnp.exp(final_sum) * keep_state[-1]
    tail_keys = (keyset * tail_decay[:, :, None]).transpose(1, 0, 2)
    queried = (queries * entering[:, :, None]).transpose(1, 0, 2)
    return (write_keys, write_values, scores, tail_keys, queried, carried)


def block_map(block_data):
    write_keys, write_values, scores, tail_keys, queried, carried = block_data
    identity_matrix = jnp.eye(DK, dtype=jnp.float32)
    transform = carried[:, None, None] * identity_matrix[None] - jnp.einsum(
        "hcd,hce->hde", tail_keys, write_keys, precision=HIGHEST
    )
    shift_term = jnp.einsum("hcd,hce->hde", tail_keys, write_values, precision=HIGHEST)
    return (transform, shift_term)


def block_apply(block_data, state_in):
    write_keys, write_values, scores, tail_keys, queried, carried = block_data
    fresh_values = write_values - jnp.einsum(
        "hcd,hde->hce", write_keys, state_in, precision=HIGHEST
    )
    output = jnp.einsum("hcd,hde->hce", queried, state_in, precision=HIGHEST)
    output = output + jnp.einsum("hij,hje->hie", scores, fresh_values, precision=HIGHEST)
    state_next = carried[:, None, None] * state_in + jnp.einsum(
        "hcd,hce->hde", tail_keys, fresh_values, precision=HIGHEST
    )
    return (output, state_next)

def unit_lower_inverse_fast(strict_part):
    positions = strict_part.shape[-1]
    identity_matrix = jnp.eye(positions, dtype=jnp.float32)[None]
    result = identity_matrix - strict_part
    power = strict_part
    reach = 2
    while reach < positions:
        power = jnp.einsum("hij,hjk->hik", power, power, precision=HIGHEST)
        result = jnp.einsum("hij,hjk->hik", result, identity_matrix + power, precision=HIGHEST)
        reach = reach * 2
    return result


def block_map_fast(block_data):
    write_keys, write_values, scores, tail_keys, queried, carried = block_data
    identity_matrix = jnp.eye(DK, dtype=jnp.float32)
    transform = carried[:, None, None] * identity_matrix[None] - jnp.einsum(
        "hcd,hce->hde", tail_keys, write_keys, precision=FAST
    )
    shift_term = jnp.einsum("hcd,hce->hde", tail_keys, write_values, precision=FAST)
    return (transform, shift_term)


def block_apply_fast(block_data, state_in):
    write_keys, write_values, scores, tail_keys, queried, carried = block_data
    fresh_values = write_values - jnp.einsum(
        "hcd,hde->hce", write_keys, state_in, precision=FAST
    )
    output = jnp.einsum("hcd,hde->hce", queried, state_in, precision=FAST)
    output = output + jnp.einsum("hij,hje->hie", scores, fresh_values, precision=FAST)
    state_next = carried[:, None, None] * state_in + jnp.einsum(
        "hcd,hce->hde", tail_keys, fresh_values, precision=FAST
    )
    return (output, state_next)


def section_one(mix_ext, conv_weight, log_decay, write_rate, seg_ext):
    queries, keyset, values = prepare(mix_ext, seg_ext, conv_weight)
    margin = conv_weight.shape[0] - 1
    positions = log_decay.shape[0]
    blocks = positions // BLOCK
    segments = seg_ext[margin:]
    before = seg_ext[margin - 1 : margin - 1 + positions : BLOCK]

    def blocked(tensor):
        return tensor.reshape((blocks, BLOCK) + tensor.shape[1:])

    return jax.vmap(block_parts)(
        blocked(queries),
        blocked(keyset),
        blocked(values),
        blocked(log_decay),
        blocked(write_rate),
        blocked(segments),
        before,
    )


def section_two(parts, state_in):

    def step_block(state_now, block_data):
        output, state_next = block_apply(block_data, state_now)
        return (state_next, output)

    state_out, outputs = lax.scan(step_block, state_in, parts)
    blocks = outputs.shape[0]
    return (outputs.transpose(0, 2, 1, 3).reshape(blocks * BLOCK, HV * DV), state_out)


def summarize(parts):
    identity_matrix = jnp.eye(DK, dtype=jnp.float32)
    initial = (
        jnp.broadcast_to(identity_matrix, (HV, DK, DK)),
        jnp.zeros((HV, DK, DV), jnp.float32),
    )

    def fold_block(carried_map, block_data):
        transform, shift_term = block_map(block_data)
        merged = jnp.einsum("hij,hjk->hik", transform, carried_map[0], precision=HIGHEST)
        moved = (
            jnp.einsum("hij,hjk->hik", transform, carried_map[1], precision=HIGHEST) + shift_term
        )
        return ((merged, moved), None)

    result, unused = lax.scan(fold_block, initial, parts)
    return result


def compose(earlier_map, later_map):
    merged = jnp.einsum("shij,shjk->shik", later_map[0], earlier_map[0], precision=HIGHEST)
    moved = (
        jnp.einsum("shij,shjk->shik", later_map[0], earlier_map[1], precision=HIGHEST)
        + later_map[1]
    )
    return (merged, moved)


def local(mixed, conv_weight, log_decay, write_rate, segment_ids, cotangent):
    margin = conv_weight.shape[0] - 1
    shifted_rows, shifted_segs = from_behind(
        (mixed[:, -margin:, :], segment_ids[:, -margin:].astype(jnp.bfloat16)), "ctx", 1
    )
    mix_ext = jnp.concatenate([shifted_rows, mixed], axis=1).astype(jnp.float32)
    seg_ext = jnp.concatenate([shifted_segs.astype(jnp.int32), segment_ids], axis=1)

    def first_section(mix_in, weight_in, decay_in, rate_in):
        return jax.vmap(section_one, in_axes=(0, None, 0, 0, 0))(
            mix_in, weight_in, decay_in, rate_in, seg_ext
        )

    parts, first_pull = jax.vjp(first_section, mix_ext, conv_weight, log_decay, write_rate)
    transform, shift_term = jax.vmap(summarize)(parts)
    identity_pair = (
        jnp.broadcast_to(jnp.eye(transform.shape[-1], dtype=jnp.float32), transform.shape),
        jnp.zeros_like(shift_term),
    )
    incoming = prefix((transform, shift_term), "ctx", compose, identity_pair, False)[1]
    (outputs, leaving), second_pull = jax.vjp(jax.vmap(section_two), parts, incoming)
    part_grads, local_term = second_pull((cotangent.astype(jnp.float32), jnp.zeros_like(leaving)))
    flipped = jnp.swapaxes(transform, -1, -2)
    departing = prefix((flipped, local_term), "ctx", compose, identity_pair, True)[1]
    more_grads, unused_grad = second_pull((jnp.zeros_like(outputs), departing))
    total_parts = jax.tree.map(jnp.add, part_grads, more_grads)
    grad_mix, grad_weight, grad_decay, grad_rate = first_pull(total_parts)
    returned = from_behind(grad_mix[:, :margin, :].astype(jnp.bfloat16), "ctx", -1).astype(
        jnp.float32
    )
    own_grad = grad_mix[:, margin:, :]
    own_grad = jnp.concatenate(
        [own_grad[:, :-margin, :], own_grad[:, -margin:, :] + returned], axis=1
    )
    total_conv = lax.psum(grad_weight, ("dp", "ctx"))
    tokens_all = mixed.shape[0] * lax.axis_size("dp") * mixed.shape[1] * lax.axis_size("ctx")
    return (
        outputs.astype(jnp.bfloat16),
        own_grad.astype(jnp.bfloat16),
        grad_decay,
        grad_rate,
        total_conv / math.sqrt(tokens_all),
    )


def tree_sum(value, axis):
    count = lax.axis_size(axis)
    if count & (count - 1):
        return lax.psum(value, axis)
    step = 1
    while step < count:
        value = value + lax.ppermute(value, axis, [(i, i ^ step) for i in range(count)])
        step = step * 2
    return value


def prepare_heads(mix_ext, seg_ext, conv_weight, key_heads, value_heads):
    margin = conv_weight.shape[0] - 1
    positions = mix_ext.shape[0] - margin
    current = seg_ext[margin:]
    summed = jnp.zeros((positions, mix_ext.shape[1]), jnp.float32)
    for tap_index in range(margin + 1):
        same_doc = (seg_ext[tap_index : tap_index + positions] == current).astype(jnp.float32)
        summed = (
            summed
            + conv_weight[tap_index][None, :]
            * mix_ext[tap_index : tap_index + positions]
            * same_doc[:, None]
        )
    activated = jax.nn.silu(summed)
    split_at = key_heads * DK
    queries = activated[:, :split_at].reshape(positions, key_heads, DK)
    keyset = activated[:, split_at : 2 * split_at].reshape(positions, key_heads, DK)
    values = activated[:, 2 * split_at :].reshape(positions, value_heads, DV)
    queries = (
        queries
        / jnp.sqrt(jnp.sum(queries * queries, axis=-1, keepdims=True) + 1e-06)
        / math.sqrt(DK)
    )
    keyset = keyset / jnp.sqrt(jnp.sum(keyset * keyset, axis=-1, keepdims=True) + 1e-06)
    repeats = value_heads // key_heads
    return (jnp.repeat(queries, repeats, axis=1), jnp.repeat(keyset, repeats, axis=1), values)


def combine_maps(earlier, later):
    merged = jnp.einsum("...ij,...jk->...ik", later[0], earlier[0], precision=HIGHEST)
    moved = jnp.einsum("...ij,...jk->...ik", later[0], earlier[1], precision=HIGHEST) + later[1]
    return (merged, moved)


def inclusive_states(transform, shift_term):
    blocks = transform.shape[0]
    reach = 1
    while reach < blocks:
        moved = jnp.einsum(
            "bhij,bhjk->bhik", transform[reach:], shift_term[:-reach], precision=FAST
        )
        shift_term = jnp.concatenate([shift_term[:reach], shift_term[reach:] + moved], axis=0)
        if 2 * reach < blocks:
            merged = jnp.einsum(
                "bhij,bhjk->bhik", transform[reach:], transform[:-reach], precision=FAST
            )
            transform = jnp.concatenate([transform[:reach], merged], axis=0)
        reach = reach * 2
    return shift_term


@jax.custom_vjp
def entering_states(transform, shift_term):
    return entering_forward(transform, shift_term)[0]


def entering_forward(transform, shift_term):
    eye = jnp.broadcast_to(jnp.eye(transform.shape[-1], dtype=transform.dtype), transform[:1].shape)
    shifted_maps = jnp.concatenate([eye, transform[:-1]], axis=0)
    shifted_terms = jnp.concatenate([jnp.zeros_like(shift_term[:1]), shift_term[:-1]], axis=0)
    states = inclusive_states(shifted_maps, shifted_terms)
    return states, (transform, states)


def entering_backward(saved, grad_states):
    transform, states = saved
    flipped = jnp.swapaxes(transform, -1, -2)[::-1]
    total = inclusive_states(flipped, grad_states[::-1])[::-1]
    later = total[1:]
    grad_shift = jnp.concatenate([later, jnp.zeros_like(later[:1])], axis=0)
    grad_map = jnp.einsum("bhik,bhjk->bhij", later, states[:-1], precision=FAST)
    grad_transform = jnp.concatenate([grad_map, jnp.zeros_like(transform[:1])], axis=0)
    return (grad_transform, grad_shift)


entering_states.defvjp(entering_forward, entering_backward)


def heads_forward(mix_in, weight_in, decay_in, rate_in, seg_ext, key_heads, value_heads):
    margin = weight_in.shape[0] - 1
    positions = decay_in.shape[0]
    blocks = positions // BLOCK
    mix_ext = jnp.concatenate([jnp.zeros((margin, mix_in.shape[1]), jnp.float32), mix_in], axis=0)
    queries, keyset, values = prepare_heads(mix_ext, seg_ext, weight_in, key_heads, value_heads)
    segments = seg_ext[margin:]
    before = seg_ext[margin - 1 : margin - 1 + positions : BLOCK]

    def blocked(tensor):
        return tensor.reshape((blocks, BLOCK) + tensor.shape[1:])

    parts = jax.vmap(block_parts_heads)(
        blocked(queries),
        blocked(keyset),
        blocked(values),
        blocked(decay_in),
        blocked(rate_in),
        blocked(segments),
        before,
    )
    transform, shift_term = jax.vmap(block_map_fast)(parts)
    incoming = entering_states(transform, shift_term)
    outputs, unused = jax.vmap(block_apply_fast)(parts, incoming)
    return outputs.transpose(0, 2, 1, 3).reshape(positions, value_heads * DV)


def heads_local(mixed, conv_weight, log_decay, write_rate, segment_ids, cotangent):
    if mixed.shape[0] != 1:
        return local(mixed, conv_weight, log_decay, write_rate, segment_ids, cotangent)
    count = lax.axis_size("ctx")
    mine = lax.axis_index("ctx")
    value_heads = HV // count
    key_heads = value_heads * HK // HV
    margin = conv_weight.shape[0] - 1
    rows = mixed.shape[1]
    length = rows * count
    qk_width = key_heads * DK
    v_width = value_heads * DV

    def to_heads(array, width):
        grouped = array.reshape(rows, count, width)
        return lax.all_to_all(grouped, "ctx", 1, 0, tiled=True).reshape(length, width)

    def to_rows(array, width):
        grouped = array.reshape(count, rows, 1, width)
        return lax.all_to_all(grouped, "ctx", 0, 2, tiled=True).reshape(rows, count, width)

    own = mixed[0]
    width = 2 * qk_width + v_width
    packed = jnp.concatenate(
        [
            own[:, : HK * DK].reshape(rows, count, qk_width),
            own[:, HK * DK : 2 * HK * DK].reshape(rows, count, qk_width),
            own[:, 2 * HK * DK :].reshape(rows, count, v_width),
            cotangent[0].reshape(rows, count, v_width),
        ],
        axis=-1,
    )
    wide = to_heads(packed, width + v_width)
    mix_heads = wide[:, :width].astype(jnp.float32)
    cot_heads = wide[:, width:].astype(jnp.float32)
    seg_columns = jnp.broadcast_to(
        segment_ids[0].astype(jnp.float32)[:, None, None], (rows, count, 1)
    )
    small = jnp.concatenate(
        [
            log_decay[0].reshape(rows, count, value_heads),
            write_rate[0].reshape(rows, count, value_heads),
            seg_columns,
        ],
        axis=-1,
    )
    narrow = to_heads(small, 2 * value_heads + 1)
    decay_heads = narrow[:, :value_heads]
    rate_heads = narrow[:, value_heads : 2 * value_heads]
    segments = narrow[:, 2 * value_heads].astype(jnp.int32)
    seg_ext = jnp.concatenate([jnp.full((margin,), -1, jnp.int32), segments])

    weight_q = conv_weight[:, : HK * DK].reshape(-1, count, qk_width)[:, mine]
    weight_k = conv_weight[:, HK * DK : 2 * HK * DK].reshape(-1, count, qk_width)[:, mine]
    weight_v = conv_weight[:, 2 * HK * DK :].reshape(-1, count, v_width)[:, mine]
    weight_heads = jnp.concatenate([weight_q, weight_k, weight_v], axis=-1)

    def forward(mix_in, weight_in, decay_in, rate_in):
        return heads_forward(
            mix_in, weight_in, decay_in, rate_in, seg_ext, key_heads, value_heads
        )

    outputs, pullback = jax.vjp(forward, mix_heads, weight_heads, decay_heads, rate_heads)
    grad_mix, grad_weight, grad_decay, grad_rate = pullback(cot_heads)

    joined = jnp.concatenate([outputs.astype(jnp.bfloat16), grad_mix.astype(jnp.bfloat16)], axis=-1)
    back = to_rows(joined, v_width + width)
    core = back[:, :, :v_width].reshape(1, rows, HV * DV)
    grad_rows = jnp.concatenate(
        [
            back[:, :, v_width : v_width + qk_width].reshape(rows, HK * DK),
            back[:, :, v_width + qk_width : v_width + 2 * qk_width].reshape(rows, HK * DK),
            back[:, :, v_width + 2 * qk_width :].reshape(rows, HV * DV),
        ],
        axis=-1,
    )[None]
    taps = conv_weight.shape[0]
    sequences = lax.axis_size("dp")
    mine_dp = lax.axis_index("dp")
    row_grads = jnp.concatenate([grad_decay, grad_rate], axis=-1).reshape(count, rows * 2 * value_heads)
    pieces = jnp.concatenate(
        [
            jnp.broadcast_to(row_grads[None], (sequences,) + row_grads.shape),
            jnp.broadcast_to(
                grad_weight.reshape(1, 1, taps * width), (sequences, count, taps * width)
            ),
        ],
        axis=-1,
    ).reshape(sequences * count, 1, rows * 2 * value_heads + taps * width)
    everything = lax.all_to_all(pieces, ("dp", "ctx"), 0, 1, tiled=True)[0]
    everything = everything.reshape(sequences, count, rows * 2 * value_heads + taps * width)
    weight_sum = everything[0, :, rows * 2 * value_heads :]
    for index in range(1, sequences):
        weight_sum = weight_sum + everything[index, :, rows * 2 * value_heads :]
    returned = jnp.concatenate(
        [lax.dynamic_index_in_dim(everything, mine_dp, 0, keepdims=False)[:, : rows * 2 * value_heads], weight_sum],
        axis=-1,
    )
    grads_small = returned[:, : rows * 2 * value_heads].reshape(count, rows, 2 * value_heads)
    grads_small = grads_small.transpose(1, 0, 2)
    decay_rows = grads_small[:, :, :value_heads].reshape(1, rows, HV)
    rate_rows = grads_small[:, :, value_heads:].reshape(1, rows, HV)
    conv_parts = returned[:, rows * 2 * value_heads :].reshape(count, taps, width).transpose(1, 0, 2)
    total_conv = jnp.concatenate(
        [
            conv_parts[:, :, :qk_width].reshape(taps, HK * DK),
            conv_parts[:, :, qk_width : 2 * qk_width].reshape(taps, HK * DK),
            conv_parts[:, :, 2 * qk_width :].reshape(taps, HV * DV),
        ],
        axis=-1,
    )
    tokens_all = mixed.shape[0] * sequences * length
    return (core, grad_rows, decay_rows, rate_rows, total_conv / math.sqrt(tokens_all))


def solution(mesh):
    in_specs = (
        P("dp", "ctx", None),
        P(),
        P("dp", "ctx", None),
        P("dp", "ctx", None),
        P("dp", "ctx"),
        P("dp", "ctx", None),
    )
    out_specs = (
        P("dp", "ctx", None),
        P("dp", "ctx", None),
        P("dp", "ctx", None),
        P("dp", "ctx", None),
        P(),
    )
    count = mesh.shape["ctx"]
    per_device = HV // count if HV % count == 0 else 0
    chosen = heads_local if per_device and (per_device * HK) % HV == 0 else local
    return jax.shard_map(chosen, mesh=mesh, in_specs=in_specs, out_specs=out_specs, check_vma=False)
```

```python
import math

import jax
import jax.numpy as jnp
from jax import lax
from jax.experimental import pallas as pl
from jax.experimental.pallas import tpu as pltpu
from jax.sharding import PartitionSpec as P

HK = 8
HV = 16
DK = 128
DV = 128
BLOCK = 64


HIGHEST = lax.Precision.HIGHEST
FAST = lax.Precision.HIGH


def from_behind(x, axis, by):
    size = lax.axis_size(axis)
    pairs = [(i, i + by) for i in range(size) if 0 <= i + by < size]
    return lax.ppermute(x, axis, pairs)


def prefix(value, axis, join, neutral, backward):
    count, mine = (lax.axis_size(axis), lax.axis_index(axis))
    pieces = jax.tree.map(lambda part: lax.all_gather(part, axis), value)
    if backward:
        pieces = jax.tree.map(lambda part: part[::-1], pieces)
        mine = count - 1 - mine
    total = jax.tree.map(
        lambda part, zero: jnp.full_like(part, 0) + jnp.asarray(zero, part.dtype), value, neutral
    )

    def hop(position, total):
        longer = join(total, jax.tree.map(lambda part: part[position], pieces))
        return jax.tree.map(lambda new, old: jnp.where(position < mine, new, old), longer, total)

    return lax.fori_loop(0, count - 1, hop, total)


def prepare(mix_ext, seg_ext, conv_weight):
    margin = conv_weight.shape[0] - 1
    positions = mix_ext.shape[0] - margin
    current = seg_ext[margin:]
    summed = jnp.zeros((positions, mix_ext.shape[1]), jnp.float32)
    for tap_index in range(margin + 1):
        same_doc = (seg_ext[tap_index : tap_index + positions] == current).astype(jnp.float32)
        summed = (
            summed
            + conv_weight[tap_index][None, :]
            * mix_ext[tap_index : tap_index + positions]
            * same_doc[:, None]
        )
    activated = jax.nn.silu(summed)
    split_at = HK * DK
    queries = activated[:, :split_at].reshape(positions, HK, DK)
    keyset = activated[:, split_at : 2 * split_at].reshape(positions, HK, DK)
    values = activated[:, 2 * split_at :].reshape(positions, HV, DV)
    queries = (
        queries
        / jnp.sqrt(jnp.sum(queries * queries, axis=-1, keepdims=True) + 1e-06)
        / math.sqrt(DK)
    )
    keyset = keyset / jnp.sqrt(jnp.sum(keyset * keyset, axis=-1, keepdims=True) + 1e-06)
    repeats = HV // HK
    return (jnp.repeat(queries, repeats, axis=1), jnp.repeat(keyset, repeats, axis=1), values)


def unit_lower_inverse(strict_part):
    positions = strict_part.shape[-1]
    identity_matrix = jnp.eye(positions, dtype=jnp.float32)[None]
    result = identity_matrix - strict_part
    power = strict_part
    reach = 2
    while reach < positions:
        power = jnp.einsum("hij,hjk->hik", power, power, precision=HIGHEST)
        result = jnp.einsum("hij,hjk->hik", result, identity_matrix + power, precision=HIGHEST)
        reach = reach * 2
    return result


def block_parts(queries, keyset, values, log_decay, write_rate, segments, seg_before):
    positions = queries.shape[0]
    cumulative = jnp.cumsum(log_decay, axis=0)
    keep_state = (segments == seg_before).astype(jnp.float32)
    entering = jnp.exp(cumulative) * keep_state[:, None]
    token_position = lax.iota(jnp.int32, positions)
    same_doc = segments[:, None] == segments[None, :]
    strict = same_doc & (token_position[:, None] > token_position[None, :])
    causal = same_doc & (token_position[:, None] >= token_position[None, :])
    spread = cumulative.T[:, :, None] - cumulative.T[:, None, :]
    strict_decay = jnp.where(strict[None], jnp.exp(jnp.where(strict[None], spread, 0.0)), 0.0)
    causal_decay = jnp.where(causal[None], jnp.exp(jnp.where(causal[None], spread, 0.0)), 0.0)
    key_inner = jnp.einsum("ihd,jhd->hij", keyset, keyset, precision=HIGHEST)
    inverse = unit_lower_inverse(write_rate.T[:, :, None] * key_inner * strict_decay)
    targets = jnp.concatenate(
        [keyset * (write_rate * entering)[:, :, None], values * write_rate[:, :, None]], axis=2
    )
    solved = jnp.einsum("hij,hjd->hid", inverse, targets.transpose(1, 0, 2), precision=HIGHEST)
    write_keys = solved[:, :, :DK]
    write_values = solved[:, :, DK:]
    scores = jnp.einsum("ihd,jhd->hij", queries, keyset, precision=HIGHEST) * causal_decay
    final_sum = cumulative[-1]
    tail_decay = (
        jnp.exp(final_sum[None, :] - cumulative)
        * (segments == segments[-1]).astype(jnp.float32)[:, None]
    )
    carried = jnp.exp(final_sum) * keep_state[-1]
    tail_keys = (keyset * tail_decay[:, :, None]).transpose(1, 0, 2)
    queried = (queries * entering[:, :, None]).transpose(1, 0, 2)
    return (write_keys, write_values, scores, tail_keys, queried, carried)


@jax.custom_vjp
def lower_inverse(strict_part):
    return unit_lower_inverse_fast(strict_part)


def lower_inverse_forward(strict_part):
    inverse = unit_lower_inverse_fast(strict_part)
    return inverse, inverse


def lower_inverse_backward(inverse, grad_inverse):
    flipped = jnp.swapaxes(inverse, -1, -2)
    inner = jnp.einsum("hij,hjk->hik", flipped, grad_inverse, precision=HIGHEST)
    return (-jnp.einsum("hij,hjk->hik", inner, flipped, precision=HIGHEST),)


lower_inverse.defvjp(lower_inverse_forward, lower_inverse_backward)


def block_parts_heads(queries, keyset, values, log_decay, write_rate, segments, seg_before):
    positions = queries.shape[0]
    cumulative = jnp.cumsum(log_decay, axis=0)
    keep_state = (segments == seg_before).astype(jnp.float32)
    entering = jnp.exp(cumulative) * keep_state[:, None]
    token_position = lax.iota(jnp.int32, positions)
    same_doc = segments[:, None] == segments[None, :]
    strict = same_doc & (token_position[:, None] > token_position[None, :])
    causal = same_doc & (token_position[:, None] >= token_position[None, :])
    spread = cumulative.T[:, :, None] - cumulative.T[:, None, :]
    strict_decay = jnp.where(strict[None], jnp.exp(jnp.where(strict[None], spread, 0.0)), 0.0)
    causal_decay = jnp.where(causal[None], jnp.exp(jnp.where(causal[None], spread, 0.0)), 0.0)
    key_inner = jnp.einsum("ihd,jhd->hij", keyset, keyset, precision=HIGHEST)
    inverse = lower_inverse(write_rate.T[:, :, None] * key_inner * strict_decay)
    targets = jnp.concatenate(
        [keyset * (write_rate * entering)[:, :, None], values * write_rate[:, :, None]], axis=2
    )
    solved = jnp.einsum("hij,hjd->hid", inverse, targets.transpose(1, 0, 2), precision=HIGHEST)
    write_keys = solved[:, :, :DK]
    write_values = solved[:, :, DK:]
    scores = jnp.einsum("ihd,jhd->hij", queries, keyset, precision=HIGHEST) * causal_decay
    final_sum = cumulative[-1]
    tail_decay = (
        jnp.exp(final_sum[None, :] - cumulative)
        * (segments == segments[-1]).astype(jnp.float32)[:, None]
    )
    carried = jnp.exp(final_sum) * keep_state[-1]
    tail_keys = (keyset * tail_decay[:, :, None]).transpose(1, 0, 2)
    queried = (queries * entering[:, :, None]).transpose(1, 0, 2)
    return (write_keys, write_values, scores, tail_keys, queried, carried)


def inverse_kernel(strict_ref, out_ref):
    strict_part = strict_ref[...]
    size = strict_part.shape[-1]
    rows_at = lax.broadcasted_iota(jnp.int32, strict_part.shape, 1)
    cols_at = lax.broadcasted_iota(jnp.int32, strict_part.shape, 2)
    identity_matrix = (rows_at == cols_at).astype(jnp.float32)
    dims = (((2,), (1,)), ((0,), (0,)))
    result = identity_matrix - strict_part
    power = strict_part
    reach = 2
    while reach < size:
        power = lax.dot_general(
            power, power, dims, precision=HIGHEST, preferred_element_type=jnp.float32
        )
        result = lax.dot_general(
            result, identity_matrix + power, dims, precision=HIGHEST,
            preferred_element_type=jnp.float32,
        )
        reach = reach * 2
    out_ref[...] = result


def kernel_inverse(strict_part):
    count, size = strict_part.shape[0], strict_part.shape[-1]
    steps = max(1, (size - 1).bit_length() - 1)
    return pl.pallas_call(
        inverse_kernel,
        out_shape=jax.ShapeDtypeStruct(strict_part.shape, jnp.float32),
        in_specs=[pl.BlockSpec(memory_space=pltpu.VMEM)],
        out_specs=pl.BlockSpec(memory_space=pltpu.VMEM),
        cost_estimate=pl.CostEstimate(
            flops=12 * 2 * steps * count * size**3,
            transcendentals=0,
            bytes_accessed=2 * 4 * count * size * size,
        ),
    )(strict_part)


@jax.custom_vjp
def batch_inverse(strict_part):
    return kernel_inverse(strict_part)


def batch_inverse_forward(strict_part):
    inverse = kernel_inverse(strict_part)
    return inverse, inverse


def batch_inverse_backward(inverse, grad_inverse):
    flipped = jnp.swapaxes(inverse, -1, -2)
    inner = jnp.einsum("hij,hjk->hik", flipped, grad_inverse, precision=HIGHEST)
    return (-jnp.einsum("hij,hjk->hik", inner, flipped, precision=HIGHEST),)


batch_inverse.defvjp(batch_inverse_forward, batch_inverse_backward)


def block_system(keyset, log_decay, write_rate, segments):
    positions = keyset.shape[0]
    cumulative = jnp.cumsum(log_decay, axis=0)
    token_position = lax.iota(jnp.int32, positions)
    same_doc = segments[:, None] == segments[None, :]
    strict = same_doc & (token_position[:, None] > token_position[None, :])
    spread = cumulative.T[:, :, None] - cumulative.T[:, None, :]
    strict_decay = jnp.where(strict[None], jnp.exp(jnp.where(strict[None], spread, 0.0)), 0.0)
    key_inner = jnp.einsum("ihd,jhd->hij", keyset, keyset, precision=HIGHEST)
    return write_rate.T[:, :, None] * key_inner * strict_decay


def block_rest(inverse, queries, keyset, values, log_decay, write_rate, segments, seg_before):
    positions = queries.shape[0]
    cumulative = jnp.cumsum(log_decay, axis=0)
    keep_state = (segments == seg_before).astype(jnp.float32)
    entering = jnp.exp(cumulative) * keep_state[:, None]
    token_position = lax.iota(jnp.int32, positions)
    same_doc = segments[:, None] == segments[None, :]
    causal = same_doc & (token_position[:, None] >= token_position[None, :])
    spread = cumulative.T[:, :, None] - cumulative.T[:, None, :]
    causal_decay = jnp.where(causal[None], jnp.exp(jnp.where(causal[None], spread, 0.0)), 0.0)
    targets = jnp.concatenate(
        [keyset * (write_rate * entering)[:, :, None], values * write_rate[:, :, None]], axis=2
    )
    solved = jnp.einsum("hij,hjd->hid", inverse, targets.transpose(1, 0, 2), precision=HIGHEST)
    write_keys = solved[:, :, :DK]
    write_values = solved[:, :, DK:]
    scores = jnp.einsum("ihd,jhd->hij", queries, keyset, precision=HIGHEST) * causal_decay
    final_sum = cumulative[-1]
    tail_decay = (
        jnp.exp(final_sum[None, :] - cumulative)
        * (segments == segments[-1]).astype(jnp.float32)[:, None]
    )
    carried = jnp.exp(final_sum) * keep_state[-1]
    tail_keys = (keyset * tail_decay[:, :, None]).transpose(1, 0, 2)
    queried = (queries * entering[:, :, None]).transpose(1, 0, 2)
    return (write_keys, write_values, scores, tail_keys, queried, carried)


def block_map(block_data):
    write_keys, write_values, scores, tail_keys, queried, carried = block_data
    identity_matrix = jnp.eye(DK, dtype=jnp.float32)
    transform = carried[:, None, None] * identity_matrix[None] - jnp.einsum(
        "hcd,hce->hde", tail_keys, write_keys, precision=HIGHEST
    )
    shift_term = jnp.einsum("hcd,hce->hde", tail_keys, write_values, precision=HIGHEST)
    return (transform, shift_term)


def block_apply(block_data, state_in):
    write_keys, write_values, scores, tail_keys, queried, carried = block_data
    fresh_values = write_values - jnp.einsum(
        "hcd,hde->hce", write_keys, state_in, precision=HIGHEST
    )
    output = jnp.einsum("hcd,hde->hce", queried, state_in, precision=HIGHEST)
    output = output + jnp.einsum("hij,hje->hie", scores, fresh_values, precision=HIGHEST)
    state_next = carried[:, None, None] * state_in + jnp.einsum(
        "hcd,hce->hde", tail_keys, fresh_values, precision=HIGHEST
    )
    return (output, state_next)

def unit_lower_inverse_fast(strict_part):
    positions = strict_part.shape[-1]
    identity_matrix = jnp.eye(positions, dtype=jnp.float32)[None]
    result = identity_matrix - strict_part
    power = strict_part
    reach = 2
    while reach < positions:
        power = jnp.einsum("hij,hjk->hik", power, power, precision=HIGHEST)
        result = jnp.einsum("hij,hjk->hik", result, identity_matrix + power, precision=HIGHEST)
        reach = reach * 2
    return result


def block_map_fast(block_data):
    write_keys, write_values, scores, tail_keys, queried, carried = block_data
    identity_matrix = jnp.eye(DK, dtype=jnp.float32)
    transform = carried[:, None, None] * identity_matrix[None] - jnp.einsum(
        "hcd,hce->hde", tail_keys, write_keys, precision=FAST
    )
    shift_term = jnp.einsum("hcd,hce->hde", tail_keys, write_values, precision=FAST)
    return (transform, shift_term)


def block_apply_fast(block_data, state_in):
    write_keys, write_values, scores, tail_keys, queried, carried = block_data
    fresh_values = write_values - jnp.einsum(
        "hcd,hde->hce", write_keys, state_in, precision=FAST
    )
    output = jnp.einsum("hcd,hde->hce", queried, state_in, precision=FAST)
    output = output + jnp.einsum("hij,hje->hie", scores, fresh_values, precision=FAST)
    state_next = carried[:, None, None] * state_in + jnp.einsum(
        "hcd,hce->hde", tail_keys, fresh_values, precision=FAST
    )
    return (output, state_next)


def section_one(mix_ext, conv_weight, log_decay, write_rate, seg_ext):
    queries, keyset, values = prepare(mix_ext, seg_ext, conv_weight)
    margin = conv_weight.shape[0] - 1
    positions = log_decay.shape[0]
    blocks = positions // BLOCK
    segments = seg_ext[margin:]
    before = seg_ext[margin - 1 : margin - 1 + positions : BLOCK]

    def blocked(tensor):
        return tensor.reshape((blocks, BLOCK) + tensor.shape[1:])

    return jax.vmap(block_parts)(
        blocked(queries),
        blocked(keyset),
        blocked(values),
        blocked(log_decay),
        blocked(write_rate),
        blocked(segments),
        before,
    )


def section_two(parts, state_in):

    def step_block(state_now, block_data):
        output, state_next = block_apply(block_data, state_now)
        return (state_next, output)

    state_out, outputs = lax.scan(step_block, state_in, parts)
    blocks = outputs.shape[0]
    return (outputs.transpose(0, 2, 1, 3).reshape(blocks * BLOCK, HV * DV), state_out)


def summarize(parts):
    identity_matrix = jnp.eye(DK, dtype=jnp.float32)
    initial = (
        jnp.broadcast_to(identity_matrix, (HV, DK, DK)),
        jnp.zeros((HV, DK, DV), jnp.float32),
    )

    def fold_block(carried_map, block_data):
        transform, shift_term = block_map(block_data)
        merged = jnp.einsum("hij,hjk->hik", transform, carried_map[0], precision=HIGHEST)
        moved = (
            jnp.einsum("hij,hjk->hik", transform, carried_map[1], precision=HIGHEST) + shift_term
        )
        return ((merged, moved), None)

    result, unused = lax.scan(fold_block, initial, parts)
    return result


def compose(earlier_map, later_map):
    merged = jnp.einsum("shij,shjk->shik", later_map[0], earlier_map[0], precision=HIGHEST)
    moved = (
        jnp.einsum("shij,shjk->shik", later_map[0], earlier_map[1], precision=HIGHEST)
        + later_map[1]
    )
    return (merged, moved)


def local(mixed, conv_weight, log_decay, write_rate, segment_ids, cotangent):
    margin = conv_weight.shape[0] - 1
    shifted_rows, shifted_segs = from_behind(
        (mixed[:, -margin:, :], segment_ids[:, -margin:].astype(jnp.bfloat16)), "ctx", 1
    )
    mix_ext = jnp.concatenate([shifted_rows, mixed], axis=1).astype(jnp.float32)
    seg_ext = jnp.concatenate([shifted_segs.astype(jnp.int32), segment_ids], axis=1)

    def first_section(mix_in, weight_in, decay_in, rate_in):
        return jax.vmap(section_one, in_axes=(0, None, 0, 0, 0))(
            mix_in, weight_in, decay_in, rate_in, seg_ext
        )

    parts, first_pull = jax.vjp(first_section, mix_ext, conv_weight, log_decay, write_rate)
    transform, shift_term = jax.vmap(summarize)(parts)
    identity_pair = (
        jnp.broadcast_to(jnp.eye(transform.shape[-1], dtype=jnp.float32), transform.shape),
        jnp.zeros_like(shift_term),
    )
    incoming = prefix((transform, shift_term), "ctx", compose, identity_pair, False)[1]
    (outputs, leaving), second_pull = jax.vjp(jax.vmap(section_two), parts, incoming)
    part_grads, local_term = second_pull((cotangent.astype(jnp.float32), jnp.zeros_like(leaving)))
    flipped = jnp.swapaxes(transform, -1, -2)
    departing = prefix((flipped, local_term), "ctx", compose, identity_pair, True)[1]
    more_grads, unused_grad = second_pull((jnp.zeros_like(outputs), departing))
    total_parts = jax.tree.map(jnp.add, part_grads, more_grads)
    grad_mix, grad_weight, grad_decay, grad_rate = first_pull(total_parts)
    returned = from_behind(grad_mix[:, :margin, :].astype(jnp.bfloat16), "ctx", -1).astype(
        jnp.float32
    )
    own_grad = grad_mix[:, margin:, :]
    own_grad = jnp.concatenate(
        [own_grad[:, :-margin, :], own_grad[:, -margin:, :] + returned], axis=1
    )
    total_conv = lax.psum(grad_weight, ("dp", "ctx"))
    tokens_all = mixed.shape[0] * lax.axis_size("dp") * mixed.shape[1] * lax.axis_size("ctx")
    return (
        outputs.astype(jnp.bfloat16),
        own_grad.astype(jnp.bfloat16),
        grad_decay,
        grad_rate,
        total_conv / math.sqrt(tokens_all),
    )


def tree_sum(value, axis):
    count = lax.axis_size(axis)
    if count & (count - 1):
        return lax.psum(value, axis)
    step = 1
    while step < count:
        value = value + lax.ppermute(value, axis, [(i, i ^ step) for i in range(count)])
        step = step * 2
    return value


def prepare_heads(mix_ext, seg_ext, conv_weight, key_heads, value_heads):
    margin = conv_weight.shape[0] - 1
    positions = mix_ext.shape[0] - margin
    current = seg_ext[margin:]
    summed = jnp.zeros((positions, mix_ext.shape[1]), jnp.float32)
    for tap_index in range(margin + 1):
        same_doc = (seg_ext[tap_index : tap_index + positions] == current).astype(jnp.float32)
        summed = (
            summed
            + conv_weight[tap_index][None, :]
            * mix_ext[tap_index : tap_index + positions]
            * same_doc[:, None]
        )
    activated = jax.nn.silu(summed)
    split_at = key_heads * DK
    queries = activated[:, :split_at].reshape(positions, key_heads, DK)
    keyset = activated[:, split_at : 2 * split_at].reshape(positions, key_heads, DK)
    values = activated[:, 2 * split_at :].reshape(positions, value_heads, DV)
    queries = (
        queries
        / jnp.sqrt(jnp.sum(queries * queries, axis=-1, keepdims=True) + 1e-06)
        / math.sqrt(DK)
    )
    keyset = keyset / jnp.sqrt(jnp.sum(keyset * keyset, axis=-1, keepdims=True) + 1e-06)
    repeats = value_heads // key_heads
    return (jnp.repeat(queries, repeats, axis=1), jnp.repeat(keyset, repeats, axis=1), values)


def combine_maps(earlier, later):
    merged = jnp.einsum("...ij,...jk->...ik", later[0], earlier[0], precision=HIGHEST)
    moved = jnp.einsum("...ij,...jk->...ik", later[0], earlier[1], precision=HIGHEST) + later[1]
    return (merged, moved)


def inclusive_states(transform, shift_term):
    blocks = transform.shape[0]
    reach = 1
    while reach < blocks:
        moved = jnp.einsum(
            "bhij,bhjk->bhik", transform[reach:], shift_term[:-reach], precision=FAST
        )
        shift_term = jnp.concatenate([shift_term[:reach], shift_term[reach:] + moved], axis=0)
        if 2 * reach < blocks:
            merged = jnp.einsum(
                "bhij,bhjk->bhik", transform[reach:], transform[:-reach], precision=FAST
            )
            transform = jnp.concatenate([transform[:reach], merged], axis=0)
        reach = reach * 2
    return shift_term


@jax.custom_vjp
def entering_states(transform, shift_term):
    return entering_forward(transform, shift_term)[0]


def entering_forward(transform, shift_term):
    eye = jnp.broadcast_to(jnp.eye(transform.shape[-1], dtype=transform.dtype), transform[:1].shape)
    shifted_maps = jnp.concatenate([eye, transform[:-1]], axis=0)
    shifted_terms = jnp.concatenate([jnp.zeros_like(shift_term[:1]), shift_term[:-1]], axis=0)
    states = inclusive_states(shifted_maps, shifted_terms)
    return states, (transform, states)


def entering_backward(saved, grad_states):
    transform, states = saved
    flipped = jnp.swapaxes(transform, -1, -2)[::-1]
    total = inclusive_states(flipped, grad_states[::-1])[::-1]
    later = total[1:]
    grad_shift = jnp.concatenate([later, jnp.zeros_like(later[:1])], axis=0)
    grad_map = jnp.einsum("bhik,bhjk->bhij", later, states[:-1], precision=FAST)
    grad_transform = jnp.concatenate([grad_map, jnp.zeros_like(transform[:1])], axis=0)
    return (grad_transform, grad_shift)


entering_states.defvjp(entering_forward, entering_backward)


def heads_forward(mix_in, weight_in, decay_in, rate_in, seg_ext, key_heads, value_heads):
    margin = weight_in.shape[0] - 1
    positions = decay_in.shape[0]
    blocks = positions // BLOCK
    mix_ext = jnp.concatenate([jnp.zeros((margin, mix_in.shape[1]), jnp.float32), mix_in], axis=0)
    queries, keyset, values = prepare_heads(mix_ext, seg_ext, weight_in, key_heads, value_heads)
    segments = seg_ext[margin:]
    before = seg_ext[margin - 1 : margin - 1 + positions : BLOCK]

    def blocked(tensor):
        return tensor.reshape((blocks, BLOCK) + tensor.shape[1:])

    system = jax.vmap(block_system)(
        blocked(keyset), blocked(decay_in), blocked(rate_in), blocked(segments)
    )
    inverse = batch_inverse(system.reshape((-1,) + system.shape[2:])).reshape(system.shape)
    parts = jax.vmap(block_rest)(
        inverse,
        blocked(queries),
        blocked(keyset),
        blocked(values),
        blocked(decay_in),
        blocked(rate_in),
        blocked(segments),
        before,
    )
    transform, shift_term = jax.vmap(block_map_fast)(parts)
    incoming = entering_states(transform, shift_term)
    outputs, unused = jax.vmap(block_apply_fast)(parts, incoming)
    return outputs.transpose(0, 2, 1, 3).reshape(positions, value_heads * DV)


def heads_local(mixed, conv_weight, log_decay, write_rate, segment_ids, cotangent):
    if mixed.shape[0] != 1:
        return local(mixed, conv_weight, log_decay, write_rate, segment_ids, cotangent)
    count = lax.axis_size("ctx")
    mine = lax.axis_index("ctx")
    value_heads = HV // count
    key_heads = value_heads * HK // HV
    margin = conv_weight.shape[0] - 1
    rows = mixed.shape[1]
    length = rows * count
    qk_width = key_heads * DK
    v_width = value_heads * DV

    def to_heads(array, width):
        grouped = array.reshape(rows, count, width)
        return lax.all_to_all(grouped, "ctx", 1, 0, tiled=True).reshape(length, width)

    def to_rows(array, width):
        grouped = array.reshape(count, rows, 1, width)
        return lax.all_to_all(grouped, "ctx", 0, 2, tiled=True).reshape(rows, count, width)

    own = mixed[0]
    width = 2 * qk_width + v_width
    packed = jnp.concatenate(
        [
            own[:, : HK * DK].reshape(rows, count, qk_width),
            own[:, HK * DK : 2 * HK * DK].reshape(rows, count, qk_width),
            own[:, 2 * HK * DK :].reshape(rows, count, v_width),
            cotangent[0].reshape(rows, count, v_width),
        ],
        axis=-1,
    )
    wide = to_heads(packed, width + v_width)
    mix_heads = wide[:, :width].astype(jnp.float32)
    cot_heads = wide[:, width:].astype(jnp.float32)
    seg_columns = jnp.broadcast_to(
        segment_ids[0].astype(jnp.float32)[:, None, None], (rows, count, 1)
    )
    small = jnp.concatenate(
        [
            log_decay[0].reshape(rows, count, value_heads),
            write_rate[0].reshape(rows, count, value_heads),
            seg_columns,
        ],
        axis=-1,
    )
    narrow = to_heads(small, 2 * value_heads + 1)
    decay_heads = narrow[:, :value_heads]
    rate_heads = narrow[:, value_heads : 2 * value_heads]
    segments = narrow[:, 2 * value_heads].astype(jnp.int32)
    seg_ext = jnp.concatenate([jnp.full((margin,), -1, jnp.int32), segments])

    weight_q = conv_weight[:, : HK * DK].reshape(-1, count, qk_width)[:, mine]
    weight_k = conv_weight[:, HK * DK : 2 * HK * DK].reshape(-1, count, qk_width)[:, mine]
    weight_v = conv_weight[:, 2 * HK * DK :].reshape(-1, count, v_width)[:, mine]
    weight_heads = jnp.concatenate([weight_q, weight_k, weight_v], axis=-1)

    def forward(mix_in, weight_in, decay_in, rate_in):
        return heads_forward(
            mix_in, weight_in, decay_in, rate_in, seg_ext, key_heads, value_heads
        )

    outputs, pullback = jax.vjp(forward, mix_heads, weight_heads, decay_heads, rate_heads)
    grad_mix, grad_weight, grad_decay, grad_rate = pullback(cot_heads)

    joined = jnp.concatenate([outputs.astype(jnp.bfloat16), grad_mix.astype(jnp.bfloat16)], axis=-1)
    back = to_rows(joined, v_width + width)
    core = back[:, :, :v_width].reshape(1, rows, HV * DV)
    grad_rows = jnp.concatenate(
        [
            back[:, :, v_width : v_width + qk_width].reshape(rows, HK * DK),
            back[:, :, v_width + qk_width : v_width + 2 * qk_width].reshape(rows, HK * DK),
            back[:, :, v_width + 2 * qk_width :].reshape(rows, HV * DV),
        ],
        axis=-1,
    )[None]
    taps = conv_weight.shape[0]
    sequences = lax.axis_size("dp")
    mine_dp = lax.axis_index("dp")
    row_grads = jnp.concatenate([grad_decay, grad_rate], axis=-1).reshape(count, rows * 2 * value_heads)
    pieces = jnp.concatenate(
        [
            jnp.broadcast_to(row_grads[None], (sequences,) + row_grads.shape),
            jnp.broadcast_to(
                grad_weight.reshape(1, 1, taps * width), (sequences, count, taps * width)
            ),
        ],
        axis=-1,
    ).reshape(sequences * count, 1, rows * 2 * value_heads + taps * width)
    everything = lax.all_to_all(pieces, ("dp", "ctx"), 0, 1, tiled=True)[0]
    everything = everything.reshape(sequences, count, rows * 2 * value_heads + taps * width)
    weight_sum = everything[0, :, rows * 2 * value_heads :]
    for index in range(1, sequences):
        weight_sum = weight_sum + everything[index, :, rows * 2 * value_heads :]
    returned = jnp.concatenate(
        [lax.dynamic_index_in_dim(everything, mine_dp, 0, keepdims=False)[:, : rows * 2 * value_heads], weight_sum],
        axis=-1,
    )
    grads_small = returned[:, : rows * 2 * value_heads].reshape(count, rows, 2 * value_heads)
    grads_small = grads_small.transpose(1, 0, 2)
    decay_rows = grads_small[:, :, :value_heads].reshape(1, rows, HV)
    rate_rows = grads_small[:, :, value_heads:].reshape(1, rows, HV)
    conv_parts = returned[:, rows * 2 * value_heads :].reshape(count, taps, width).transpose(1, 0, 2)
    total_conv = jnp.concatenate(
        [
            conv_parts[:, :, :qk_width].reshape(taps, HK * DK),
            conv_parts[:, :, qk_width : 2 * qk_width].reshape(taps, HK * DK),
            conv_parts[:, :, 2 * qk_width :].reshape(taps, HV * DV),
        ],
        axis=-1,
    )
    tokens_all = mixed.shape[0] * sequences * length
    return (core, grad_rows, decay_rows, rate_rows, total_conv / math.sqrt(tokens_all))


def solution(mesh):
    in_specs = (
        P("dp", "ctx", None),
        P(),
        P("dp", "ctx", None),
        P("dp", "ctx", None),
        P("dp", "ctx"),
        P("dp", "ctx", None),
    )
    out_specs = (
        P("dp", "ctx", None),
        P("dp", "ctx", None),
        P("dp", "ctx", None),
        P("dp", "ctx", None),
        P(),
    )
    count = mesh.shape["ctx"]
    per_device = HV // count if HV % count == 0 else 0
    chosen = heads_local if per_device and (per_device * HK) % HV == 0 else local
    return jax.shard_map(chosen, mesh=mesh, in_specs=in_specs, out_specs=out_specs, check_vma=False)
```

```python
import math

import jax
import jax.numpy as jnp
from jax import lax
from jax.experimental import pallas as pl
from jax.experimental.pallas import tpu as pltpu
from jax.sharding import PartitionSpec as P

HK = 8
HV = 16
DK = 128
DV = 128
BLOCK = 64


HIGHEST = lax.Precision.HIGHEST
FAST = lax.Precision.HIGH


def from_behind(x, axis, by):
    size = lax.axis_size(axis)
    pairs = [(i, i + by) for i in range(size) if 0 <= i + by < size]
    return lax.ppermute(x, axis, pairs)


def prefix(value, axis, join, neutral, backward):
    count, mine = (lax.axis_size(axis), lax.axis_index(axis))
    pieces = jax.tree.map(lambda part: lax.all_gather(part, axis), value)
    if backward:
        pieces = jax.tree.map(lambda part: part[::-1], pieces)
        mine = count - 1 - mine
    total = jax.tree.map(
        lambda part, zero: jnp.full_like(part, 0) + jnp.asarray(zero, part.dtype), value, neutral
    )

    def hop(position, total):
        longer = join(total, jax.tree.map(lambda part: part[position], pieces))
        return jax.tree.map(lambda new, old: jnp.where(position < mine, new, old), longer, total)

    return lax.fori_loop(0, count - 1, hop, total)


def prepare(mix_ext, seg_ext, conv_weight):
    margin = conv_weight.shape[0] - 1
    positions = mix_ext.shape[0] - margin
    current = seg_ext[margin:]
    summed = jnp.zeros((positions, mix_ext.shape[1]), jnp.float32)
    for tap_index in range(margin + 1):
        same_doc = (seg_ext[tap_index : tap_index + positions] == current).astype(jnp.float32)
        summed = (
            summed
            + conv_weight[tap_index][None, :]
            * mix_ext[tap_index : tap_index + positions]
            * same_doc[:, None]
        )
    activated = jax.nn.silu(summed)
    split_at = HK * DK
    queries = activated[:, :split_at].reshape(positions, HK, DK)
    keyset = activated[:, split_at : 2 * split_at].reshape(positions, HK, DK)
    values = activated[:, 2 * split_at :].reshape(positions, HV, DV)
    queries = (
        queries
        / jnp.sqrt(jnp.sum(queries * queries, axis=-1, keepdims=True) + 1e-06)
        / math.sqrt(DK)
    )
    keyset = keyset / jnp.sqrt(jnp.sum(keyset * keyset, axis=-1, keepdims=True) + 1e-06)
    repeats = HV // HK
    return (jnp.repeat(queries, repeats, axis=1), jnp.repeat(keyset, repeats, axis=1), values)


def unit_lower_inverse(strict_part):
    positions = strict_part.shape[-1]
    identity_matrix = jnp.eye(positions, dtype=jnp.float32)[None]
    result = identity_matrix - strict_part
    power = strict_part
    reach = 2
    while reach < positions:
        power = jnp.einsum("hij,hjk->hik", power, power, precision=HIGHEST)
        result = jnp.einsum("hij,hjk->hik", result, identity_matrix + power, precision=HIGHEST)
        reach = reach * 2
    return result


def block_parts(queries, keyset, values, log_decay, write_rate, segments, seg_before):
    positions = queries.shape[0]
    cumulative = jnp.cumsum(log_decay, axis=0)
    keep_state = (segments == seg_before).astype(jnp.float32)
    entering = jnp.exp(cumulative) * keep_state[:, None]
    token_position = lax.iota(jnp.int32, positions)
    same_doc = segments[:, None] == segments[None, :]
    strict = same_doc & (token_position[:, None] > token_position[None, :])
    causal = same_doc & (token_position[:, None] >= token_position[None, :])
    spread = cumulative.T[:, :, None] - cumulative.T[:, None, :]
    strict_decay = jnp.where(strict[None], jnp.exp(jnp.where(strict[None], spread, 0.0)), 0.0)
    causal_decay = jnp.where(causal[None], jnp.exp(jnp.where(causal[None], spread, 0.0)), 0.0)
    key_inner = jnp.einsum("ihd,jhd->hij", keyset, keyset, precision=HIGHEST)
    inverse = unit_lower_inverse(write_rate.T[:, :, None] * key_inner * strict_decay)
    targets = jnp.concatenate(
        [keyset * (write_rate * entering)[:, :, None], values * write_rate[:, :, None]], axis=2
    )
    solved = jnp.einsum("hij,hjd->hid", inverse, targets.transpose(1, 0, 2), precision=HIGHEST)
    write_keys = solved[:, :, :DK]
    write_values = solved[:, :, DK:]
    scores = jnp.einsum("ihd,jhd->hij", queries, keyset, precision=HIGHEST) * causal_decay
    final_sum = cumulative[-1]
    tail_decay = (
        jnp.exp(final_sum[None, :] - cumulative)
        * (segments == segments[-1]).astype(jnp.float32)[:, None]
    )
    carried = jnp.exp(final_sum) * keep_state[-1]
    tail_keys = (keyset * tail_decay[:, :, None]).transpose(1, 0, 2)
    queried = (queries * entering[:, :, None]).transpose(1, 0, 2)
    return (write_keys, write_values, scores, tail_keys, queried, carried)


@jax.custom_vjp
def lower_inverse(strict_part):
    return unit_lower_inverse_fast(strict_part)


def lower_inverse_forward(strict_part):
    inverse = unit_lower_inverse_fast(strict_part)
    return inverse, inverse


def lower_inverse_backward(inverse, grad_inverse):
    flipped = jnp.swapaxes(inverse, -1, -2)
    inner = jnp.einsum("hij,hjk->hik", flipped, grad_inverse, precision=HIGHEST)
    return (-jnp.einsum("hij,hjk->hik", inner, flipped, precision=HIGHEST),)


lower_inverse.defvjp(lower_inverse_forward, lower_inverse_backward)


def block_parts_heads(queries, keyset, values, log_decay, write_rate, segments, seg_before):
    positions = queries.shape[0]
    cumulative = jnp.cumsum(log_decay, axis=0)
    keep_state = (segments == seg_before).astype(jnp.float32)
    entering = jnp.exp(cumulative) * keep_state[:, None]
    token_position = lax.iota(jnp.int32, positions)
    same_doc = segments[:, None] == segments[None, :]
    strict = same_doc & (token_position[:, None] > token_position[None, :])
    causal = same_doc & (token_position[:, None] >= token_position[None, :])
    spread = cumulative.T[:, :, None] - cumulative.T[:, None, :]
    strict_decay = jnp.where(strict[None], jnp.exp(jnp.where(strict[None], spread, 0.0)), 0.0)
    causal_decay = jnp.where(causal[None], jnp.exp(jnp.where(causal[None], spread, 0.0)), 0.0)
    key_inner = jnp.einsum("ihd,jhd->hij", keyset, keyset, precision=HIGHEST)
    inverse = lower_inverse(write_rate.T[:, :, None] * key_inner * strict_decay)
    targets = jnp.concatenate(
        [keyset * (write_rate * entering)[:, :, None], values * write_rate[:, :, None]], axis=2
    )
    solved = jnp.einsum("hij,hjd->hid", inverse, targets.transpose(1, 0, 2), precision=HIGHEST)
    write_keys = solved[:, :, :DK]
    write_values = solved[:, :, DK:]
    scores = jnp.einsum("ihd,jhd->hij", queries, keyset, precision=HIGHEST) * causal_decay
    final_sum = cumulative[-1]
    tail_decay = (
        jnp.exp(final_sum[None, :] - cumulative)
        * (segments == segments[-1]).astype(jnp.float32)[:, None]
    )
    carried = jnp.exp(final_sum) * keep_state[-1]
    tail_keys = (keyset * tail_decay[:, :, None]).transpose(1, 0, 2)
    queried = (queries * entering[:, :, None]).transpose(1, 0, 2)
    return (write_keys, write_values, scores, tail_keys, queried, carried)


def inverse_kernel(strict_ref, out_ref):
    strict_part = strict_ref[...]
    size = strict_part.shape[-1]
    rows_at = lax.broadcasted_iota(jnp.int32, strict_part.shape, 1)
    cols_at = lax.broadcasted_iota(jnp.int32, strict_part.shape, 2)
    identity_matrix = (rows_at == cols_at).astype(jnp.float32)
    dims = (((2,), (1,)), ((0,), (0,)))
    result = identity_matrix - strict_part
    power = strict_part
    reach = 2
    while reach < size:
        power = lax.dot_general(
            power, power, dims, precision=HIGHEST, preferred_element_type=jnp.float32
        )
        result = lax.dot_general(
            result, identity_matrix + power, dims, precision=HIGHEST,
            preferred_element_type=jnp.float32,
        )
        reach = reach * 2
    out_ref[...] = result


def kernel_inverse(strict_part):
    count, size = strict_part.shape[0], strict_part.shape[-1]
    steps = max(1, (size - 1).bit_length() - 1)
    return pl.pallas_call(
        inverse_kernel,
        out_shape=jax.ShapeDtypeStruct(strict_part.shape, jnp.float32),
        in_specs=[pl.BlockSpec(memory_space=pltpu.VMEM)],
        out_specs=pl.BlockSpec(memory_space=pltpu.VMEM),
        cost_estimate=pl.CostEstimate(
            flops=12 * 2 * steps * count * size**3,
            transcendentals=0,
            bytes_accessed=2 * 4 * count * size * size,
        ),
    )(strict_part)


@jax.custom_vjp
def batch_inverse(strict_part):
    return kernel_inverse(strict_part)


def batch_inverse_forward(strict_part):
    inverse = kernel_inverse(strict_part)
    return inverse, inverse


def batch_inverse_backward(inverse, grad_inverse):
    flipped = jnp.swapaxes(inverse, -1, -2)
    inner = jnp.einsum("hij,hjk->hik", flipped, grad_inverse, precision=HIGHEST)
    return (-jnp.einsum("hij,hjk->hik", inner, flipped, precision=HIGHEST),)


batch_inverse.defvjp(batch_inverse_forward, batch_inverse_backward)


def block_system(keyset, log_decay, write_rate, segments):
    positions = keyset.shape[0]
    cumulative = jnp.cumsum(log_decay, axis=0)
    token_position = lax.iota(jnp.int32, positions)
    same_doc = segments[:, None] == segments[None, :]
    strict = same_doc & (token_position[:, None] > token_position[None, :])
    spread = cumulative.T[:, :, None] - cumulative.T[:, None, :]
    strict_decay = jnp.where(strict[None], jnp.exp(jnp.where(strict[None], spread, 0.0)), 0.0)
    key_inner = jnp.einsum("ihd,jhd->hij", keyset, keyset, precision=HIGHEST)
    return write_rate.T[:, :, None] * key_inner * strict_decay


def block_rest(inverse, queries, keyset, values, log_decay, write_rate, segments, seg_before):
    positions = queries.shape[0]
    cumulative = jnp.cumsum(log_decay, axis=0)
    keep_state = (segments == seg_before).astype(jnp.float32)
    entering = jnp.exp(cumulative) * keep_state[:, None]
    token_position = lax.iota(jnp.int32, positions)
    same_doc = segments[:, None] == segments[None, :]
    causal = same_doc & (token_position[:, None] >= token_position[None, :])
    spread = cumulative.T[:, :, None] - cumulative.T[:, None, :]
    causal_decay = jnp.where(causal[None], jnp.exp(jnp.where(causal[None], spread, 0.0)), 0.0)
    targets = jnp.concatenate(
        [keyset * (write_rate * entering)[:, :, None], values * write_rate[:, :, None]], axis=2
    )
    solved = jnp.einsum("hij,hjd->hid", inverse, targets.transpose(1, 0, 2), precision=HIGHEST)
    write_keys = solved[:, :, :DK]
    write_values = solved[:, :, DK:]
    scores = jnp.einsum("ihd,jhd->hij", queries, keyset, precision=HIGHEST) * causal_decay
    final_sum = cumulative[-1]
    tail_decay = (
        jnp.exp(final_sum[None, :] - cumulative)
        * (segments == segments[-1]).astype(jnp.float32)[:, None]
    )
    carried = jnp.exp(final_sum) * keep_state[-1]
    tail_keys = (keyset * tail_decay[:, :, None]).transpose(1, 0, 2)
    queried = (queries * entering[:, :, None]).transpose(1, 0, 2)
    return (write_keys, write_values, scores, tail_keys, queried, carried)


def block_map(block_data):
    write_keys, write_values, scores, tail_keys, queried, carried = block_data
    identity_matrix = jnp.eye(DK, dtype=jnp.float32)
    transform = carried[:, None, None] * identity_matrix[None] - jnp.einsum(
        "hcd,hce->hde", tail_keys, write_keys, precision=HIGHEST
    )
    shift_term = jnp.einsum("hcd,hce->hde", tail_keys, write_values, precision=HIGHEST)
    return (transform, shift_term)


def block_apply(block_data, state_in):
    write_keys, write_values, scores, tail_keys, queried, carried = block_data
    fresh_values = write_values - jnp.einsum(
        "hcd,hde->hce", write_keys, state_in, precision=HIGHEST
    )
    output = jnp.einsum("hcd,hde->hce", queried, state_in, precision=HIGHEST)
    output = output + jnp.einsum("hij,hje->hie", scores, fresh_values, precision=HIGHEST)
    state_next = carried[:, None, None] * state_in + jnp.einsum(
        "hcd,hce->hde", tail_keys, fresh_values, precision=HIGHEST
    )
    return (output, state_next)

def unit_lower_inverse_fast(strict_part):
    positions = strict_part.shape[-1]
    identity_matrix = jnp.eye(positions, dtype=jnp.float32)[None]
    result = identity_matrix - strict_part
    power = strict_part
    reach = 2
    while reach < positions:
        power = jnp.einsum("hij,hjk->hik", power, power, precision=HIGHEST)
        result = jnp.einsum("hij,hjk->hik", result, identity_matrix + power, precision=HIGHEST)
        reach = reach * 2
    return result


def block_map_fast(block_data):
    write_keys, write_values, scores, tail_keys, queried, carried = block_data
    identity_matrix = jnp.eye(DK, dtype=jnp.float32)
    transform = carried[:, None, None] * identity_matrix[None] - jnp.einsum(
        "hcd,hce->hde", tail_keys, write_keys, precision=FAST
    )
    shift_term = jnp.einsum("hcd,hce->hde", tail_keys, write_values, precision=FAST)
    return (transform, shift_term)


def block_apply_fast(block_data, state_in):
    write_keys, write_values, scores, tail_keys, queried, carried = block_data
    fresh_values = write_values - jnp.einsum(
        "hcd,hde->hce", write_keys, state_in, precision=FAST
    )
    output = jnp.einsum("hcd,hde->hce", queried, state_in, precision=FAST)
    output = output + jnp.einsum("hij,hje->hie", scores, fresh_values, precision=FAST)
    state_next = carried[:, None, None] * state_in + jnp.einsum(
        "hcd,hce->hde", tail_keys, fresh_values, precision=FAST
    )
    return (output, state_next)


def section_one(mix_ext, conv_weight, log_decay, write_rate, seg_ext):
    queries, keyset, values = prepare(mix_ext, seg_ext, conv_weight)
    margin = conv_weight.shape[0] - 1
    positions = log_decay.shape[0]
    blocks = positions // BLOCK
    segments = seg_ext[margin:]
    before = seg_ext[margin - 1 : margin - 1 + positions : BLOCK]

    def blocked(tensor):
        return tensor.reshape((blocks, BLOCK) + tensor.shape[1:])

    return jax.vmap(block_parts)(
        blocked(queries),
        blocked(keyset),
        blocked(values),
        blocked(log_decay),
        blocked(write_rate),
        blocked(segments),
        before,
    )


def section_two(parts, state_in):

    def step_block(state_now, block_data):
        output, state_next = block_apply(block_data, state_now)
        return (state_next, output)

    state_out, outputs = lax.scan(step_block, state_in, parts)
    blocks = outputs.shape[0]
    return (outputs.transpose(0, 2, 1, 3).reshape(blocks * BLOCK, HV * DV), state_out)


def summarize(parts):
    identity_matrix = jnp.eye(DK, dtype=jnp.float32)
    initial = (
        jnp.broadcast_to(identity_matrix, (HV, DK, DK)),
        jnp.zeros((HV, DK, DV), jnp.float32),
    )

    def fold_block(carried_map, block_data):
        transform, shift_term = block_map(block_data)
        merged = jnp.einsum("hij,hjk->hik", transform, carried_map[0], precision=HIGHEST)
        moved = (
            jnp.einsum("hij,hjk->hik", transform, carried_map[1], precision=HIGHEST) + shift_term
        )
        return ((merged, moved), None)

    result, unused = lax.scan(fold_block, initial, parts)
    return result


def compose(earlier_map, later_map):
    merged = jnp.einsum("shij,shjk->shik", later_map[0], earlier_map[0], precision=HIGHEST)
    moved = (
        jnp.einsum("shij,shjk->shik", later_map[0], earlier_map[1], precision=HIGHEST)
        + later_map[1]
    )
    return (merged, moved)


def local(mixed, conv_weight, log_decay, write_rate, segment_ids, cotangent):
    margin = conv_weight.shape[0] - 1
    shifted_rows, shifted_segs = from_behind(
        (mixed[:, -margin:, :], segment_ids[:, -margin:].astype(jnp.bfloat16)), "ctx", 1
    )
    mix_ext = jnp.concatenate([shifted_rows, mixed], axis=1).astype(jnp.float32)
    seg_ext = jnp.concatenate([shifted_segs.astype(jnp.int32), segment_ids], axis=1)

    def first_section(mix_in, weight_in, decay_in, rate_in):
        return jax.vmap(section_one, in_axes=(0, None, 0, 0, 0))(
            mix_in, weight_in, decay_in, rate_in, seg_ext
        )

    parts, first_pull = jax.vjp(first_section, mix_ext, conv_weight, log_decay, write_rate)
    transform, shift_term = jax.vmap(summarize)(parts)
    identity_pair = (
        jnp.broadcast_to(jnp.eye(transform.shape[-1], dtype=jnp.float32), transform.shape),
        jnp.zeros_like(shift_term),
    )
    incoming = prefix((transform, shift_term), "ctx", compose, identity_pair, False)[1]
    (outputs, leaving), second_pull = jax.vjp(jax.vmap(section_two), parts, incoming)
    part_grads, local_term = second_pull((cotangent.astype(jnp.float32), jnp.zeros_like(leaving)))
    flipped = jnp.swapaxes(transform, -1, -2)
    departing = prefix((flipped, local_term), "ctx", compose, identity_pair, True)[1]
    more_grads, unused_grad = second_pull((jnp.zeros_like(outputs), departing))
    total_parts = jax.tree.map(jnp.add, part_grads, more_grads)
    grad_mix, grad_weight, grad_decay, grad_rate = first_pull(total_parts)
    returned = from_behind(grad_mix[:, :margin, :].astype(jnp.bfloat16), "ctx", -1).astype(
        jnp.float32
    )
    own_grad = grad_mix[:, margin:, :]
    own_grad = jnp.concatenate(
        [own_grad[:, :-margin, :], own_grad[:, -margin:, :] + returned], axis=1
    )
    total_conv = lax.psum(grad_weight, ("dp", "ctx"))
    tokens_all = mixed.shape[0] * lax.axis_size("dp") * mixed.shape[1] * lax.axis_size("ctx")
    return (
        outputs.astype(jnp.bfloat16),
        own_grad.astype(jnp.bfloat16),
        grad_decay,
        grad_rate,
        total_conv / math.sqrt(tokens_all),
    )


def tree_sum(value, axis):
    count = lax.axis_size(axis)
    if count & (count - 1):
        return lax.psum(value, axis)
    step = 1
    while step < count:
        value = value + lax.ppermute(value, axis, [(i, i ^ step) for i in range(count)])
        step = step * 2
    return value


def prepare_heads(mix_ext, seg_ext, conv_weight, key_heads, value_heads):
    margin = conv_weight.shape[0] - 1
    positions = mix_ext.shape[0] - margin
    current = seg_ext[margin:]
    summed = jnp.zeros((positions, mix_ext.shape[1]), jnp.float32)
    for tap_index in range(margin + 1):
        same_doc = (seg_ext[tap_index : tap_index + positions] == current).astype(jnp.float32)
        summed = (
            summed
            + conv_weight[tap_index][None, :]
            * mix_ext[tap_index : tap_index + positions]
            * same_doc[:, None]
        )
    activated = jax.nn.silu(summed)
    split_at = key_heads * DK
    queries = activated[:, :split_at].reshape(positions, key_heads, DK)
    keyset = activated[:, split_at : 2 * split_at].reshape(positions, key_heads, DK)
    values = activated[:, 2 * split_at :].reshape(positions, value_heads, DV)
    queries = (
        queries
        / jnp.sqrt(jnp.sum(queries * queries, axis=-1, keepdims=True) + 1e-06)
        / math.sqrt(DK)
    )
    keyset = keyset / jnp.sqrt(jnp.sum(keyset * keyset, axis=-1, keepdims=True) + 1e-06)
    repeats = value_heads // key_heads
    return (jnp.repeat(queries, repeats, axis=1), jnp.repeat(keyset, repeats, axis=1), values)


def combine_maps(earlier, later):
    merged = jnp.einsum("...ij,...jk->...ik", later[0], earlier[0], precision=HIGHEST)
    moved = jnp.einsum("...ij,...jk->...ik", later[0], earlier[1], precision=HIGHEST) + later[1]
    return (merged, moved)


def inclusive_states(transform, shift_term):
    blocks = transform.shape[0]
    reach = 1
    while reach < blocks:
        moved = jnp.einsum(
            "bhij,bhjk->bhik", transform[reach:], shift_term[:-reach], precision=FAST
        )
        shift_term = jnp.concatenate([shift_term[:reach], shift_term[reach:] + moved], axis=0)
        if 2 * reach < blocks:
            merged = jnp.einsum(
                "bhij,bhjk->bhik", transform[reach:], transform[:-reach], precision=FAST
            )
            transform = jnp.concatenate([transform[:reach], merged], axis=0)
        reach = reach * 2
    return shift_term


@jax.custom_vjp
def entering_states(transform, shift_term):
    return entering_forward(transform, shift_term)[0]


def entering_forward(transform, shift_term):
    eye = jnp.broadcast_to(jnp.eye(transform.shape[-1], dtype=transform.dtype), transform[:1].shape)
    shifted_maps = jnp.concatenate([eye, transform[:-1]], axis=0)
    shifted_terms = jnp.concatenate([jnp.zeros_like(shift_term[:1]), shift_term[:-1]], axis=0)
    states = inclusive_states(shifted_maps, shifted_terms)
    return states, (transform, states)


def entering_backward(saved, grad_states):
    transform, states = saved
    flipped = jnp.swapaxes(transform, -1, -2)[::-1]
    total = inclusive_states(flipped, grad_states[::-1])[::-1]
    later = total[1:]
    grad_shift = jnp.concatenate([later, jnp.zeros_like(later[:1])], axis=0)
    grad_map = jnp.einsum("bhik,bhjk->bhij", later, states[:-1], precision=FAST)
    grad_transform = jnp.concatenate([grad_map, jnp.zeros_like(transform[:1])], axis=0)
    return (grad_transform, grad_shift)


entering_states.defvjp(entering_forward, entering_backward)


def states_kernel(maps_ref, terms_ref, out_ref):
    blocks = maps_ref.shape[0]
    dims = (((2,), (1,)), ((0,), (0,)))
    state = jnp.zeros(terms_ref.shape[1:], jnp.float32)
    out_ref[0] = state
    for index in range(blocks - 1):
        state = (
            lax.dot_general(
                maps_ref[index], state, dims, precision=FAST, preferred_element_type=jnp.float32
            )
            + terms_ref[index]
        )
        out_ref[index + 1] = state


def adjoint_kernel(flipped_ref, grads_ref, out_ref):
    blocks = flipped_ref.shape[0]
    dims = (((2,), (1,)), ((0,), (0,)))
    total = grads_ref[blocks - 1]
    out_ref[blocks - 1] = total
    for index in range(blocks - 2, -1, -1):
        total = grads_ref[index] + lax.dot_general(
            flipped_ref[index], total, dims, precision=FAST, preferred_element_type=jnp.float32
        )
        out_ref[index] = total


def run_chain(kernel, maps, terms):
    blocks, heads, size = maps.shape[0], maps.shape[1], maps.shape[2]
    return pl.pallas_call(
        kernel,
        out_shape=jax.ShapeDtypeStruct(terms.shape, jnp.float32),
        in_specs=[pl.BlockSpec(memory_space=pltpu.VMEM)] * 2,
        out_specs=pl.BlockSpec(memory_space=pltpu.VMEM),
        cost_estimate=pl.CostEstimate(
            flops=6 * 2 * blocks * heads * size * size * terms.shape[-1],
            transcendentals=0,
            bytes_accessed=4 * (maps.size + 2 * terms.size),
        ),
    )(maps, terms)


@jax.custom_vjp
def chain_states(transform, shift_term):
    return run_chain(states_kernel, transform, shift_term)


def chain_forward(transform, shift_term):
    states = run_chain(states_kernel, transform, shift_term)
    return states, (transform, states)


def chain_backward(saved, grad_states):
    transform, states = saved
    flipped = jnp.swapaxes(transform, -1, -2)
    total = run_chain(adjoint_kernel, flipped, grad_states)
    later = total[1:]
    grad_shift = jnp.concatenate([later, jnp.zeros_like(later[:1])], axis=0)
    grad_map = jnp.einsum("bhik,bhjk->bhij", later, states[:-1], precision=FAST)
    grad_transform = jnp.concatenate([grad_map, jnp.zeros_like(transform[:1])], axis=0)
    return (grad_transform, grad_shift)


chain_states.defvjp(chain_forward, chain_backward)


def heads_forward(mix_in, weight_in, decay_in, rate_in, seg_ext, key_heads, value_heads):
    margin = weight_in.shape[0] - 1
    positions = decay_in.shape[0]
    blocks = positions // BLOCK
    mix_ext = jnp.concatenate([jnp.zeros((margin, mix_in.shape[1]), jnp.float32), mix_in], axis=0)
    queries, keyset, values = prepare_heads(mix_ext, seg_ext, weight_in, key_heads, value_heads)
    segments = seg_ext[margin:]
    before = seg_ext[margin - 1 : margin - 1 + positions : BLOCK]

    def blocked(tensor):
        return tensor.reshape((blocks, BLOCK) + tensor.shape[1:])

    system = jax.vmap(block_system)(
        blocked(keyset), blocked(decay_in), blocked(rate_in), blocked(segments)
    )
    inverse = batch_inverse(system.reshape((-1,) + system.shape[2:])).reshape(system.shape)
    parts = jax.vmap(block_rest)(
        inverse,
        blocked(queries),
        blocked(keyset),
        blocked(values),
        blocked(decay_in),
        blocked(rate_in),
        blocked(segments),
        before,
    )
    transform, shift_term = jax.vmap(block_map_fast)(parts)
    incoming = chain_states(transform, shift_term)
    outputs, unused = jax.vmap(block_apply_fast)(parts, incoming)
    return outputs.transpose(0, 2, 1, 3).reshape(positions, value_heads * DV)


def heads_local(mixed, conv_weight, log_decay, write_rate, segment_ids, cotangent):
    if mixed.shape[0] != 1:
        return local(mixed, conv_weight, log_decay, write_rate, segment_ids, cotangent)
    count = lax.axis_size("ctx")
    mine = lax.axis_index("ctx")
    value_heads = HV // count
    key_heads = value_heads * HK // HV
    margin = conv_weight.shape[0] - 1
    rows = mixed.shape[1]
    length = rows * count
    qk_width = key_heads * DK
    v_width = value_heads * DV

    def to_heads(array, width):
        grouped = array.reshape(rows, count, width)
        return lax.all_to_all(grouped, "ctx", 1, 0, tiled=True).reshape(length, width)

    def to_rows(array, width):
        grouped = array.reshape(count, rows, 1, width)
        return lax.all_to_all(grouped, "ctx", 0, 2, tiled=True).reshape(rows, count, width)

    own = mixed[0]
    width = 2 * qk_width + v_width
    packed = jnp.concatenate(
        [
            own[:, : HK * DK].reshape(rows, count, qk_width),
            own[:, HK * DK : 2 * HK * DK].reshape(rows, count, qk_width),
            own[:, 2 * HK * DK :].reshape(rows, count, v_width),
            cotangent[0].reshape(rows, count, v_width),
        ],
        axis=-1,
    )
    wide = to_heads(packed, width + v_width)
    mix_heads = wide[:, :width].astype(jnp.float32)
    cot_heads = wide[:, width:].astype(jnp.float32)
    seg_columns = jnp.broadcast_to(
        segment_ids[0].astype(jnp.float32)[:, None, None], (rows, count, 1)
    )
    small = jnp.concatenate(
        [
            log_decay[0].reshape(rows, count, value_heads),
            write_rate[0].reshape(rows, count, value_heads),
            seg_columns,
        ],
        axis=-1,
    )
    narrow = to_heads(small, 2 * value_heads + 1)
    decay_heads = narrow[:, :value_heads]
    rate_heads = narrow[:, value_heads : 2 * value_heads]
    segments = narrow[:, 2 * value_heads].astype(jnp.int32)
    seg_ext = jnp.concatenate([jnp.full((margin,), -1, jnp.int32), segments])

    weight_q = conv_weight[:, : HK * DK].reshape(-1, count, qk_width)[:, mine]
    weight_k = conv_weight[:, HK * DK : 2 * HK * DK].reshape(-1, count, qk_width)[:, mine]
    weight_v = conv_weight[:, 2 * HK * DK :].reshape(-1, count, v_width)[:, mine]
    weight_heads = jnp.concatenate([weight_q, weight_k, weight_v], axis=-1)

    def forward(mix_in, weight_in, decay_in, rate_in):
        return heads_forward(
            mix_in, weight_in, decay_in, rate_in, seg_ext, key_heads, value_heads
        )

    outputs, pullback = jax.vjp(forward, mix_heads, weight_heads, decay_heads, rate_heads)
    grad_mix, grad_weight, grad_decay, grad_rate = pullback(cot_heads)

    joined = jnp.concatenate([outputs.astype(jnp.bfloat16), grad_mix.astype(jnp.bfloat16)], axis=-1)
    back = to_rows(joined, v_width + width)
    core = back[:, :, :v_width].reshape(1, rows, HV * DV)
    grad_rows = jnp.concatenate(
        [
            back[:, :, v_width : v_width + qk_width].reshape(rows, HK * DK),
            back[:, :, v_width + qk_width : v_width + 2 * qk_width].reshape(rows, HK * DK),
            back[:, :, v_width + 2 * qk_width :].reshape(rows, HV * DV),
        ],
        axis=-1,
    )[None]
    taps = conv_weight.shape[0]
    sequences = lax.axis_size("dp")
    mine_dp = lax.axis_index("dp")
    row_grads = jnp.concatenate([grad_decay, grad_rate], axis=-1).reshape(count, rows * 2 * value_heads)
    pieces = jnp.concatenate(
        [
            jnp.broadcast_to(row_grads[None], (sequences,) + row_grads.shape),
            jnp.broadcast_to(
                grad_weight.reshape(1, 1, taps * width), (sequences, count, taps * width)
            ),
        ],
        axis=-1,
    ).reshape(sequences * count, 1, rows * 2 * value_heads + taps * width)
    everything = lax.all_to_all(pieces, ("dp", "ctx"), 0, 1, tiled=True)[0]
    everything = everything.reshape(sequences, count, rows * 2 * value_heads + taps * width)
    weight_sum = everything[0, :, rows * 2 * value_heads :]
    for index in range(1, sequences):
        weight_sum = weight_sum + everything[index, :, rows * 2 * value_heads :]
    returned = jnp.concatenate(
        [lax.dynamic_index_in_dim(everything, mine_dp, 0, keepdims=False)[:, : rows * 2 * value_heads], weight_sum],
        axis=-1,
    )
    grads_small = returned[:, : rows * 2 * value_heads].reshape(count, rows, 2 * value_heads)
    grads_small = grads_small.transpose(1, 0, 2)
    decay_rows = grads_small[:, :, :value_heads].reshape(1, rows, HV)
    rate_rows = grads_small[:, :, value_heads:].reshape(1, rows, HV)
    conv_parts = returned[:, rows * 2 * value_heads :].reshape(count, taps, width).transpose(1, 0, 2)
    total_conv = jnp.concatenate(
        [
            conv_parts[:, :, :qk_width].reshape(taps, HK * DK),
            conv_parts[:, :, qk_width : 2 * qk_width].reshape(taps, HK * DK),
            conv_parts[:, :, 2 * qk_width :].reshape(taps, HV * DV),
        ],
        axis=-1,
    )
    tokens_all = mixed.shape[0] * sequences * length
    return (core, grad_rows, decay_rows, rate_rows, total_conv / math.sqrt(tokens_all))


def solution(mesh):
    in_specs = (
        P("dp", "ctx", None),
        P(),
        P("dp", "ctx", None),
        P("dp", "ctx", None),
        P("dp", "ctx"),
        P("dp", "ctx", None),
    )
    out_specs = (
        P("dp", "ctx", None),
        P("dp", "ctx", None),
        P("dp", "ctx", None),
        P("dp", "ctx", None),
        P(),
    )
    count = mesh.shape["ctx"]
    per_device = HV // count if HV % count == 0 else 0
    chosen = heads_local if per_device and (per_device * HK) % HV == 0 else local
    return jax.shard_map(chosen, mesh=mesh, in_specs=in_specs, out_specs=out_specs, check_vma=False)
```

```python
import math

import jax
import jax.numpy as jnp
from jax import lax
from jax.experimental import pallas as pl
from jax.experimental.pallas import tpu as pltpu
from jax.sharding import PartitionSpec as P

HK = 8
HV = 16
DK = 128
DV = 128
BLOCK = 64


HIGHEST = lax.Precision.HIGHEST
FAST = lax.Precision.HIGH


def from_behind(x, axis, by):
    size = lax.axis_size(axis)
    pairs = [(i, i + by) for i in range(size) if 0 <= i + by < size]
    return lax.ppermute(x, axis, pairs)


def prefix(value, axis, join, neutral, backward):
    count, mine = (lax.axis_size(axis), lax.axis_index(axis))
    pieces = jax.tree.map(lambda part: lax.all_gather(part, axis), value)
    if backward:
        pieces = jax.tree.map(lambda part: part[::-1], pieces)
        mine = count - 1 - mine
    total = jax.tree.map(
        lambda part, zero: jnp.full_like(part, 0) + jnp.asarray(zero, part.dtype), value, neutral
    )

    def hop(position, total):
        longer = join(total, jax.tree.map(lambda part: part[position], pieces))
        return jax.tree.map(lambda new, old: jnp.where(position < mine, new, old), longer, total)

    return lax.fori_loop(0, count - 1, hop, total)


def prepare(mix_ext, seg_ext, conv_weight):
    margin = conv_weight.shape[0] - 1
    positions = mix_ext.shape[0] - margin
    current = seg_ext[margin:]
    summed = jnp.zeros((positions, mix_ext.shape[1]), jnp.float32)
    for tap_index in range(margin + 1):
        same_doc = (seg_ext[tap_index : tap_index + positions] == current).astype(jnp.float32)
        summed = (
            summed
            + conv_weight[tap_index][None, :]
            * mix_ext[tap_index : tap_index + positions]
            * same_doc[:, None]
        )
    activated = jax.nn.silu(summed)
    split_at = HK * DK
    queries = activated[:, :split_at].reshape(positions, HK, DK)
    keyset = activated[:, split_at : 2 * split_at].reshape(positions, HK, DK)
    values = activated[:, 2 * split_at :].reshape(positions, HV, DV)
    queries = (
        queries
        / jnp.sqrt(jnp.sum(queries * queries, axis=-1, keepdims=True) + 1e-06)
        / math.sqrt(DK)
    )
    keyset = keyset / jnp.sqrt(jnp.sum(keyset * keyset, axis=-1, keepdims=True) + 1e-06)
    repeats = HV // HK
    return (jnp.repeat(queries, repeats, axis=1), jnp.repeat(keyset, repeats, axis=1), values)


def unit_lower_inverse(strict_part):
    positions = strict_part.shape[-1]
    identity_matrix = jnp.eye(positions, dtype=jnp.float32)[None]
    result = identity_matrix - strict_part
    power = strict_part
    reach = 2
    while reach < positions:
        power = jnp.einsum("hij,hjk->hik", power, power, precision=HIGHEST)
        result = jnp.einsum("hij,hjk->hik", result, identity_matrix + power, precision=HIGHEST)
        reach = reach * 2
    return result


def block_parts(queries, keyset, values, log_decay, write_rate, segments, seg_before):
    positions = queries.shape[0]
    cumulative = jnp.cumsum(log_decay, axis=0)
    keep_state = (segments == seg_before).astype(jnp.float32)
    entering = jnp.exp(cumulative) * keep_state[:, None]
    token_position = lax.iota(jnp.int32, positions)
    same_doc = segments[:, None] == segments[None, :]
    strict = same_doc & (token_position[:, None] > token_position[None, :])
    causal = same_doc & (token_position[:, None] >= token_position[None, :])
    spread = cumulative.T[:, :, None] - cumulative.T[:, None, :]
    strict_decay = jnp.where(strict[None], jnp.exp(jnp.where(strict[None], spread, 0.0)), 0.0)
    causal_decay = jnp.where(causal[None], jnp.exp(jnp.where(causal[None], spread, 0.0)), 0.0)
    key_inner = jnp.einsum("ihd,jhd->hij", keyset, keyset, precision=HIGHEST)
    inverse = unit_lower_inverse(write_rate.T[:, :, None] * key_inner * strict_decay)
    targets = jnp.concatenate(
        [keyset * (write_rate * entering)[:, :, None], values * write_rate[:, :, None]], axis=2
    )
    solved = jnp.einsum("hij,hjd->hid", inverse, targets.transpose(1, 0, 2), precision=HIGHEST)
    write_keys = solved[:, :, :DK]
    write_values = solved[:, :, DK:]
    scores = jnp.einsum("ihd,jhd->hij", queries, keyset, precision=HIGHEST) * causal_decay
    final_sum = cumulative[-1]
    tail_decay = (
        jnp.exp(final_sum[None, :] - cumulative)
        * (segments == segments[-1]).astype(jnp.float32)[:, None]
    )
    carried = jnp.exp(final_sum) * keep_state[-1]
    tail_keys = (keyset * tail_decay[:, :, None]).transpose(1, 0, 2)
    queried = (queries * entering[:, :, None]).transpose(1, 0, 2)
    return (write_keys, write_values, scores, tail_keys, queried, carried)


@jax.custom_vjp
def lower_inverse(strict_part):
    return unit_lower_inverse_fast(strict_part)


def lower_inverse_forward(strict_part):
    inverse = unit_lower_inverse_fast(strict_part)
    return inverse, inverse


def lower_inverse_backward(inverse, grad_inverse):
    flipped = jnp.swapaxes(inverse, -1, -2)
    inner = jnp.einsum("hij,hjk->hik", flipped, grad_inverse, precision=HIGHEST)
    return (-jnp.einsum("hij,hjk->hik", inner, flipped, precision=HIGHEST),)


lower_inverse.defvjp(lower_inverse_forward, lower_inverse_backward)


def block_parts_heads(queries, keyset, values, log_decay, write_rate, segments, seg_before):
    positions = queries.shape[0]
    cumulative = jnp.cumsum(log_decay, axis=0)
    keep_state = (segments == seg_before).astype(jnp.float32)
    entering = jnp.exp(cumulative) * keep_state[:, None]
    token_position = lax.iota(jnp.int32, positions)
    same_doc = segments[:, None] == segments[None, :]
    strict = same_doc & (token_position[:, None] > token_position[None, :])
    causal = same_doc & (token_position[:, None] >= token_position[None, :])
    spread = cumulative.T[:, :, None] - cumulative.T[:, None, :]
    strict_decay = jnp.where(strict[None], jnp.exp(jnp.where(strict[None], spread, 0.0)), 0.0)
    causal_decay = jnp.where(causal[None], jnp.exp(jnp.where(causal[None], spread, 0.0)), 0.0)
    key_inner = jnp.einsum("ihd,jhd->hij", keyset, keyset, precision=HIGHEST)
    inverse = lower_inverse(write_rate.T[:, :, None] * key_inner * strict_decay)
    targets = jnp.concatenate(
        [keyset * (write_rate * entering)[:, :, None], values * write_rate[:, :, None]], axis=2
    )
    solved = jnp.einsum("hij,hjd->hid", inverse, targets.transpose(1, 0, 2), precision=HIGHEST)
    write_keys = solved[:, :, :DK]
    write_values = solved[:, :, DK:]
    scores = jnp.einsum("ihd,jhd->hij", queries, keyset, precision=HIGHEST) * causal_decay
    final_sum = cumulative[-1]
    tail_decay = (
        jnp.exp(final_sum[None, :] - cumulative)
        * (segments == segments[-1]).astype(jnp.float32)[:, None]
    )
    carried = jnp.exp(final_sum) * keep_state[-1]
    tail_keys = (keyset * tail_decay[:, :, None]).transpose(1, 0, 2)
    queried = (queries * entering[:, :, None]).transpose(1, 0, 2)
    return (write_keys, write_values, scores, tail_keys, queried, carried)


def inverse_kernel(strict_ref, out_ref):
    strict_part = strict_ref[...]
    size = strict_part.shape[-1]
    rows_at = lax.broadcasted_iota(jnp.int32, strict_part.shape, 1)
    cols_at = lax.broadcasted_iota(jnp.int32, strict_part.shape, 2)
    identity_matrix = (rows_at == cols_at).astype(jnp.float32)
    dims = (((2,), (1,)), ((0,), (0,)))
    result = identity_matrix - strict_part
    power = strict_part
    reach = 2
    while reach < size:
        power = lax.dot_general(
            power, power, dims, precision=HIGHEST, preferred_element_type=jnp.float32
        )
        result = lax.dot_general(
            result, identity_matrix + power, dims, precision=HIGHEST,
            preferred_element_type=jnp.float32,
        )
        reach = reach * 2
    out_ref[...] = result


def kernel_inverse(strict_part):
    count, size = strict_part.shape[0], strict_part.shape[-1]
    steps = max(1, (size - 1).bit_length() - 1)
    return pl.pallas_call(
        inverse_kernel,
        out_shape=jax.ShapeDtypeStruct(strict_part.shape, jnp.float32),
        in_specs=[pl.BlockSpec(memory_space=pltpu.VMEM)],
        out_specs=pl.BlockSpec(memory_space=pltpu.VMEM),
        cost_estimate=pl.CostEstimate(
            flops=12 * 2 * steps * count * size**3,
            transcendentals=0,
            bytes_accessed=2 * 4 * count * size * size,
        ),
    )(strict_part)


@jax.custom_vjp
def batch_inverse(strict_part):
    return kernel_inverse(strict_part)


def batch_inverse_forward(strict_part):
    inverse = kernel_inverse(strict_part)
    return inverse, inverse


def batch_inverse_backward(inverse, grad_inverse):
    flipped = jnp.swapaxes(inverse, -1, -2)
    inner = jnp.einsum("hij,hjk->hik", flipped, grad_inverse, precision=HIGHEST)
    return (-jnp.einsum("hij,hjk->hik", inner, flipped, precision=HIGHEST),)


batch_inverse.defvjp(batch_inverse_forward, batch_inverse_backward)


def block_system(keyset, cumulative, write_rate, segments):
    positions = keyset.shape[0]
    token_position = lax.iota(jnp.int32, positions)
    same_doc = segments[:, None] == segments[None, :]
    strict = same_doc & (token_position[:, None] > token_position[None, :])
    spread = cumulative.T[:, :, None] - cumulative.T[:, None, :]
    strict_decay = jnp.where(strict[None], jnp.exp(jnp.where(strict[None], spread, 0.0)), 0.0)
    key_inner = jnp.einsum("ihd,jhd->hij", keyset, keyset, precision=HIGHEST)
    return write_rate.T[:, :, None] * key_inner * strict_decay


def block_rest(inverse, queries, keyset, values, cumulative, write_rate, segments, seg_before):
    positions = queries.shape[0]
    keep_state = (segments == seg_before).astype(jnp.float32)
    entering = jnp.exp(cumulative) * keep_state[:, None]
    token_position = lax.iota(jnp.int32, positions)
    same_doc = segments[:, None] == segments[None, :]
    causal = same_doc & (token_position[:, None] >= token_position[None, :])
    spread = cumulative.T[:, :, None] - cumulative.T[:, None, :]
    causal_decay = jnp.where(causal[None], jnp.exp(jnp.where(causal[None], spread, 0.0)), 0.0)
    targets = jnp.concatenate(
        [keyset * (write_rate * entering)[:, :, None], values * write_rate[:, :, None]], axis=2
    )
    solved = jnp.einsum("hij,hjd->hid", inverse, targets.transpose(1, 0, 2), precision=HIGHEST)
    write_keys = solved[:, :, :DK]
    write_values = solved[:, :, DK:]
    scores = jnp.einsum("ihd,jhd->hij", queries, keyset, precision=HIGHEST) * causal_decay
    final_sum = cumulative[-1]
    tail_decay = (
        jnp.exp(final_sum[None, :] - cumulative)
        * (segments == segments[-1]).astype(jnp.float32)[:, None]
    )
    carried = jnp.exp(final_sum) * keep_state[-1]
    tail_keys = (keyset * tail_decay[:, :, None]).transpose(1, 0, 2)
    queried = (queries * entering[:, :, None]).transpose(1, 0, 2)
    return (write_keys, write_values, scores, tail_keys, queried, carried)


def block_map(block_data):
    write_keys, write_values, scores, tail_keys, queried, carried = block_data
    identity_matrix = jnp.eye(DK, dtype=jnp.float32)
    transform = carried[:, None, None] * identity_matrix[None] - jnp.einsum(
        "hcd,hce->hde", tail_keys, write_keys, precision=HIGHEST
    )
    shift_term = jnp.einsum("hcd,hce->hde", tail_keys, write_values, precision=HIGHEST)
    return (transform, shift_term)


def block_apply(block_data, state_in):
    write_keys, write_values, scores, tail_keys, queried, carried = block_data
    fresh_values = write_values - jnp.einsum(
        "hcd,hde->hce", write_keys, state_in, precision=HIGHEST
    )
    output = jnp.einsum("hcd,hde->hce", queried, state_in, precision=HIGHEST)
    output = output + jnp.einsum("hij,hje->hie", scores, fresh_values, precision=HIGHEST)
    state_next = carried[:, None, None] * state_in + jnp.einsum(
        "hcd,hce->hde", tail_keys, fresh_values, precision=HIGHEST
    )
    return (output, state_next)

def unit_lower_inverse_fast(strict_part):
    positions = strict_part.shape[-1]
    identity_matrix = jnp.eye(positions, dtype=jnp.float32)[None]
    result = identity_matrix - strict_part
    power = strict_part
    reach = 2
    while reach < positions:
        power = jnp.einsum("hij,hjk->hik", power, power, precision=HIGHEST)
        result = jnp.einsum("hij,hjk->hik", result, identity_matrix + power, precision=HIGHEST)
        reach = reach * 2
    return result


def block_map_fast(block_data):
    write_keys, write_values, scores, tail_keys, queried, carried = block_data
    identity_matrix = jnp.eye(DK, dtype=jnp.float32)
    transform = carried[:, None, None] * identity_matrix[None] - jnp.einsum(
        "hcd,hce->hde", tail_keys, write_keys, precision=FAST
    )
    shift_term = jnp.einsum("hcd,hce->hde", tail_keys, write_values, precision=FAST)
    return (transform, shift_term)


def block_apply_fast(block_data, state_in):
    write_keys, write_values, scores, tail_keys, queried, carried = block_data
    fresh_values = write_values - jnp.einsum(
        "hcd,hde->hce", write_keys, state_in, precision=FAST
    )
    output = jnp.einsum("hcd,hde->hce", queried, state_in, precision=FAST)
    output = output + jnp.einsum("hij,hje->hie", scores, fresh_values, precision=FAST)
    state_next = carried[:, None, None] * state_in + jnp.einsum(
        "hcd,hce->hde", tail_keys, fresh_values, precision=FAST
    )
    return (output, state_next)


def section_one(mix_ext, conv_weight, log_decay, write_rate, seg_ext):
    queries, keyset, values = prepare(mix_ext, seg_ext, conv_weight)
    margin = conv_weight.shape[0] - 1
    positions = log_decay.shape[0]
    blocks = positions // BLOCK
    segments = seg_ext[margin:]
    before = seg_ext[margin - 1 : margin - 1 + positions : BLOCK]

    def blocked(tensor):
        return tensor.reshape((blocks, BLOCK) + tensor.shape[1:])

    return jax.vmap(block_parts)(
        blocked(queries),
        blocked(keyset),
        blocked(values),
        blocked(log_decay),
        blocked(write_rate),
        blocked(segments),
        before,
    )


def section_two(parts, state_in):

    def step_block(state_now, block_data):
        output, state_next = block_apply(block_data, state_now)
        return (state_next, output)

    state_out, outputs = lax.scan(step_block, state_in, parts)
    blocks = outputs.shape[0]
    return (outputs.transpose(0, 2, 1, 3).reshape(blocks * BLOCK, HV * DV), state_out)


def summarize(parts):
    identity_matrix = jnp.eye(DK, dtype=jnp.float32)
    initial = (
        jnp.broadcast_to(identity_matrix, (HV, DK, DK)),
        jnp.zeros((HV, DK, DV), jnp.float32),
    )

    def fold_block(carried_map, block_data):
        transform, shift_term = block_map(block_data)
        merged = jnp.einsum("hij,hjk->hik", transform, carried_map[0], precision=HIGHEST)
        moved = (
            jnp.einsum("hij,hjk->hik", transform, carried_map[1], precision=HIGHEST) + shift_term
        )
        return ((merged, moved), None)

    result, unused = lax.scan(fold_block, initial, parts)
    return result


def compose(earlier_map, later_map):
    merged = jnp.einsum("shij,shjk->shik", later_map[0], earlier_map[0], precision=HIGHEST)
    moved = (
        jnp.einsum("shij,shjk->shik", later_map[0], earlier_map[1], precision=HIGHEST)
        + later_map[1]
    )
    return (merged, moved)


def local(mixed, conv_weight, log_decay, write_rate, segment_ids, cotangent):
    margin = conv_weight.shape[0] - 1
    shifted_rows, shifted_segs = from_behind(
        (mixed[:, -margin:, :], segment_ids[:, -margin:].astype(jnp.bfloat16)), "ctx", 1
    )
    mix_ext = jnp.concatenate([shifted_rows, mixed], axis=1).astype(jnp.float32)
    seg_ext = jnp.concatenate([shifted_segs.astype(jnp.int32), segment_ids], axis=1)

    def first_section(mix_in, weight_in, decay_in, rate_in):
        return jax.vmap(section_one, in_axes=(0, None, 0, 0, 0))(
            mix_in, weight_in, decay_in, rate_in, seg_ext
        )

    parts, first_pull = jax.vjp(first_section, mix_ext, conv_weight, log_decay, write_rate)
    transform, shift_term = jax.vmap(summarize)(parts)
    identity_pair = (
        jnp.broadcast_to(jnp.eye(transform.shape[-1], dtype=jnp.float32), transform.shape),
        jnp.zeros_like(shift_term),
    )
    incoming = prefix((transform, shift_term), "ctx", compose, identity_pair, False)[1]
    (outputs, leaving), second_pull = jax.vjp(jax.vmap(section_two), parts, incoming)
    part_grads, local_term = second_pull((cotangent.astype(jnp.float32), jnp.zeros_like(leaving)))
    flipped = jnp.swapaxes(transform, -1, -2)
    departing = prefix((flipped, local_term), "ctx", compose, identity_pair, True)[1]
    more_grads, unused_grad = second_pull((jnp.zeros_like(outputs), departing))
    total_parts = jax.tree.map(jnp.add, part_grads, more_grads)
    grad_mix, grad_weight, grad_decay, grad_rate = first_pull(total_parts)
    returned = from_behind(grad_mix[:, :margin, :].astype(jnp.bfloat16), "ctx", -1).astype(
        jnp.float32
    )
    own_grad = grad_mix[:, margin:, :]
    own_grad = jnp.concatenate(
        [own_grad[:, :-margin, :], own_grad[:, -margin:, :] + returned], axis=1
    )
    total_conv = lax.psum(grad_weight, ("dp", "ctx"))
    tokens_all = mixed.shape[0] * lax.axis_size("dp") * mixed.shape[1] * lax.axis_size("ctx")
    return (
        outputs.astype(jnp.bfloat16),
        own_grad.astype(jnp.bfloat16),
        grad_decay,
        grad_rate,
        total_conv / math.sqrt(tokens_all),
    )


def tree_sum(value, axis):
    count = lax.axis_size(axis)
    if count & (count - 1):
        return lax.psum(value, axis)
    step = 1
    while step < count:
        value = value + lax.ppermute(value, axis, [(i, i ^ step) for i in range(count)])
        step = step * 2
    return value


def prepare_heads(mix_ext, seg_ext, conv_weight, key_heads, value_heads):
    margin = conv_weight.shape[0] - 1
    positions = mix_ext.shape[0] - margin
    current = seg_ext[margin:]
    summed = jnp.zeros((positions, mix_ext.shape[1]), jnp.float32)
    for tap_index in range(margin + 1):
        same_doc = (seg_ext[tap_index : tap_index + positions] == current).astype(jnp.float32)
        summed = (
            summed
            + conv_weight[tap_index][None, :]
            * mix_ext[tap_index : tap_index + positions]
            * same_doc[:, None]
        )
    activated = jax.nn.silu(summed)
    split_at = key_heads * DK
    queries = activated[:, :split_at].reshape(positions, key_heads, DK)
    keyset = activated[:, split_at : 2 * split_at].reshape(positions, key_heads, DK)
    values = activated[:, 2 * split_at :].reshape(positions, value_heads, DV)
    queries = (
        queries
        / jnp.sqrt(jnp.sum(queries * queries, axis=-1, keepdims=True) + 1e-06)
        / math.sqrt(DK)
    )
    keyset = keyset / jnp.sqrt(jnp.sum(keyset * keyset, axis=-1, keepdims=True) + 1e-06)
    repeats = value_heads // key_heads
    return (jnp.repeat(queries, repeats, axis=1), jnp.repeat(keyset, repeats, axis=1), values)


def combine_maps(earlier, later):
    merged = jnp.einsum("...ij,...jk->...ik", later[0], earlier[0], precision=HIGHEST)
    moved = jnp.einsum("...ij,...jk->...ik", later[0], earlier[1], precision=HIGHEST) + later[1]
    return (merged, moved)


def inclusive_states(transform, shift_term):
    blocks = transform.shape[0]
    reach = 1
    while reach < blocks:
        moved = jnp.einsum(
            "bhij,bhjk->bhik", transform[reach:], shift_term[:-reach], precision=FAST
        )
        shift_term = jnp.concatenate([shift_term[:reach], shift_term[reach:] + moved], axis=0)
        if 2 * reach < blocks:
            merged = jnp.einsum(
                "bhij,bhjk->bhik", transform[reach:], transform[:-reach], precision=FAST
            )
            transform = jnp.concatenate([transform[:reach], merged], axis=0)
        reach = reach * 2
    return shift_term


@jax.custom_vjp
def entering_states(transform, shift_term):
    return entering_forward(transform, shift_term)[0]


def entering_forward(transform, shift_term):
    eye = jnp.broadcast_to(jnp.eye(transform.shape[-1], dtype=transform.dtype), transform[:1].shape)
    shifted_maps = jnp.concatenate([eye, transform[:-1]], axis=0)
    shifted_terms = jnp.concatenate([jnp.zeros_like(shift_term[:1]), shift_term[:-1]], axis=0)
    states = inclusive_states(shifted_maps, shifted_terms)
    return states, (transform, states)


def entering_backward(saved, grad_states):
    transform, states = saved
    flipped = jnp.swapaxes(transform, -1, -2)[::-1]
    total = inclusive_states(flipped, grad_states[::-1])[::-1]
    later = total[1:]
    grad_shift = jnp.concatenate([later, jnp.zeros_like(later[:1])], axis=0)
    grad_map = jnp.einsum("bhik,bhjk->bhij", later, states[:-1], precision=FAST)
    grad_transform = jnp.concatenate([grad_map, jnp.zeros_like(transform[:1])], axis=0)
    return (grad_transform, grad_shift)


entering_states.defvjp(entering_forward, entering_backward)


def states_kernel(maps_ref, terms_ref, out_ref):
    blocks = maps_ref.shape[0]
    dims = (((2,), (1,)), ((0,), (0,)))
    state = jnp.zeros(terms_ref.shape[1:], jnp.float32)
    out_ref[0] = state
    for index in range(blocks - 1):
        state = (
            lax.dot_general(
                maps_ref[index], state, dims, precision=FAST, preferred_element_type=jnp.float32
            )
            + terms_ref[index]
        )
        out_ref[index + 1] = state


def adjoint_kernel(flipped_ref, grads_ref, out_ref):
    blocks = flipped_ref.shape[0]
    dims = (((2,), (1,)), ((0,), (0,)))
    total = grads_ref[blocks - 1]
    out_ref[blocks - 1] = total
    for index in range(blocks - 2, -1, -1):
        total = grads_ref[index] + lax.dot_general(
            flipped_ref[index], total, dims, precision=FAST, preferred_element_type=jnp.float32
        )
        out_ref[index] = total


def run_chain(kernel, maps, terms):
    blocks, heads, size = maps.shape[0], maps.shape[1], maps.shape[2]
    return pl.pallas_call(
        kernel,
        out_shape=jax.ShapeDtypeStruct(terms.shape, jnp.float32),
        in_specs=[pl.BlockSpec(memory_space=pltpu.VMEM)] * 2,
        out_specs=pl.BlockSpec(memory_space=pltpu.VMEM),
        cost_estimate=pl.CostEstimate(
            flops=6 * 2 * blocks * heads * size * size * terms.shape[-1],
            transcendentals=0,
            bytes_accessed=4 * (maps.size + 2 * terms.size),
        ),
    )(maps, terms)


@jax.custom_vjp
def chain_states(transform, shift_term):
    return run_chain(states_kernel, transform, shift_term)


def chain_forward(transform, shift_term):
    states = run_chain(states_kernel, transform, shift_term)
    return states, (transform, states)


def chain_backward(saved, grad_states):
    transform, states = saved
    flipped = jnp.swapaxes(transform, -1, -2)
    total = run_chain(adjoint_kernel, flipped, grad_states)
    later = total[1:]
    grad_shift = jnp.concatenate([later, jnp.zeros_like(later[:1])], axis=0)
    grad_map = jnp.einsum("bhik,bhjk->bhij", later, states[:-1], precision=FAST)
    grad_transform = jnp.concatenate([grad_map, jnp.zeros_like(transform[:1])], axis=0)
    return (grad_transform, grad_shift)


chain_states.defvjp(chain_forward, chain_backward)


def heads_forward(mix_in, weight_in, decay_in, rate_in, seg_ext, key_heads, value_heads):
    margin = weight_in.shape[0] - 1
    positions = decay_in.shape[0]
    blocks = positions // BLOCK
    mix_ext = jnp.concatenate([jnp.zeros((margin, mix_in.shape[1]), jnp.float32), mix_in], axis=0)
    queries, keyset, values = prepare_heads(mix_ext, seg_ext, weight_in, key_heads, value_heads)
    segments = seg_ext[margin:]
    before = seg_ext[margin - 1 : margin - 1 + positions : BLOCK]

    def blocked(tensor):
        return tensor.reshape((blocks, BLOCK) + tensor.shape[1:])

    lower_ones = (
        lax.broadcasted_iota(jnp.int32, (BLOCK, BLOCK), 0)
        >= lax.broadcasted_iota(jnp.int32, (BLOCK, BLOCK), 1)
    ).astype(jnp.float32)
    cumulative = jnp.einsum("ij,bjh->bih", lower_ones, blocked(decay_in), precision=HIGHEST)
    system = jax.vmap(block_system)(
        blocked(keyset), cumulative, blocked(rate_in), blocked(segments)
    )
    inverse = batch_inverse(system.reshape((-1,) + system.shape[2:])).reshape(system.shape)
    parts = jax.vmap(block_rest)(
        inverse,
        blocked(queries),
        blocked(keyset),
        blocked(values),
        cumulative,
        blocked(rate_in),
        blocked(segments),
        before,
    )
    transform, shift_term = jax.vmap(block_map_fast)(parts)
    incoming = chain_states(transform, shift_term)
    outputs, unused = jax.vmap(block_apply_fast)(parts, incoming)
    return outputs.transpose(0, 2, 1, 3).reshape(positions, value_heads * DV)


def heads_local(mixed, conv_weight, log_decay, write_rate, segment_ids, cotangent):
    if mixed.shape[0] != 1:
        return local(mixed, conv_weight, log_decay, write_rate, segment_ids, cotangent)
    count = lax.axis_size("ctx")
    mine = lax.axis_index("ctx")
    value_heads = HV // count
    key_heads = value_heads * HK // HV
    margin = conv_weight.shape[0] - 1
    rows = mixed.shape[1]
    length = rows * count
    qk_width = key_heads * DK
    v_width = value_heads * DV

    def to_heads(array, width):
        grouped = array.reshape(rows, count, width)
        return lax.all_to_all(grouped, "ctx", 1, 0, tiled=True).reshape(length, width)

    def to_rows(array, width):
        grouped = array.reshape(count, rows, 1, width)
        return lax.all_to_all(grouped, "ctx", 0, 2, tiled=True).reshape(rows, count, width)

    own = mixed[0]
    width = 2 * qk_width + v_width
    packed = jnp.concatenate(
        [
            own[:, : HK * DK].reshape(rows, count, qk_width),
            own[:, HK * DK : 2 * HK * DK].reshape(rows, count, qk_width),
            own[:, 2 * HK * DK :].reshape(rows, count, v_width),
            cotangent[0].reshape(rows, count, v_width),
        ],
        axis=-1,
    )
    wide = to_heads(packed, width + v_width)
    mix_heads = wide[:, :width].astype(jnp.float32)
    cot_heads = wide[:, width:].astype(jnp.float32)
    seg_columns = jnp.broadcast_to(
        segment_ids[0].astype(jnp.float32)[:, None, None], (rows, count, 1)
    )
    small = jnp.concatenate(
        [
            log_decay[0].reshape(rows, count, value_heads),
            write_rate[0].reshape(rows, count, value_heads),
            seg_columns,
        ],
        axis=-1,
    )
    narrow = to_heads(small, 2 * value_heads + 1)
    decay_heads = narrow[:, :value_heads]
    rate_heads = narrow[:, value_heads : 2 * value_heads]
    segments = narrow[:, 2 * value_heads].astype(jnp.int32)
    seg_ext = jnp.concatenate([jnp.full((margin,), -1, jnp.int32), segments])

    weight_q = conv_weight[:, : HK * DK].reshape(-1, count, qk_width)[:, mine]
    weight_k = conv_weight[:, HK * DK : 2 * HK * DK].reshape(-1, count, qk_width)[:, mine]
    weight_v = conv_weight[:, 2 * HK * DK :].reshape(-1, count, v_width)[:, mine]
    weight_heads = jnp.concatenate([weight_q, weight_k, weight_v], axis=-1)

    def forward(mix_in, weight_in, decay_in, rate_in):
        return heads_forward(
            mix_in, weight_in, decay_in, rate_in, seg_ext, key_heads, value_heads
        )

    outputs, pullback = jax.vjp(forward, mix_heads, weight_heads, decay_heads, rate_heads)
    grad_mix, grad_weight, grad_decay, grad_rate = pullback(cot_heads)

    joined = jnp.concatenate([outputs.astype(jnp.bfloat16), grad_mix.astype(jnp.bfloat16)], axis=-1)
    back = to_rows(joined, v_width + width)
    core = back[:, :, :v_width].reshape(1, rows, HV * DV)
    grad_rows = jnp.concatenate(
        [
            back[:, :, v_width : v_width + qk_width].reshape(rows, HK * DK),
            back[:, :, v_width + qk_width : v_width + 2 * qk_width].reshape(rows, HK * DK),
            back[:, :, v_width + 2 * qk_width :].reshape(rows, HV * DV),
        ],
        axis=-1,
    )[None]
    taps = conv_weight.shape[0]
    sequences = lax.axis_size("dp")
    mine_dp = lax.axis_index("dp")
    row_grads = jnp.concatenate([grad_decay, grad_rate], axis=-1).reshape(count, rows * 2 * value_heads)
    pieces = jnp.concatenate(
        [
            jnp.broadcast_to(row_grads[None], (sequences,) + row_grads.shape),
            jnp.broadcast_to(
                grad_weight.reshape(1, 1, taps * width), (sequences, count, taps * width)
            ),
        ],
        axis=-1,
    ).reshape(sequences * count, 1, rows * 2 * value_heads + taps * width)
    everything = lax.all_to_all(pieces, ("dp", "ctx"), 0, 1, tiled=True)[0]
    everything = everything.reshape(sequences, count, rows * 2 * value_heads + taps * width)
    weight_sum = everything[0, :, rows * 2 * value_heads :]
    for index in range(1, sequences):
        weight_sum = weight_sum + everything[index, :, rows * 2 * value_heads :]
    returned = jnp.concatenate(
        [lax.dynamic_index_in_dim(everything, mine_dp, 0, keepdims=False)[:, : rows * 2 * value_heads], weight_sum],
        axis=-1,
    )
    grads_small = returned[:, : rows * 2 * value_heads].reshape(count, rows, 2 * value_heads)
    grads_small = grads_small.transpose(1, 0, 2)
    decay_rows = grads_small[:, :, :value_heads].reshape(1, rows, HV)
    rate_rows = grads_small[:, :, value_heads:].reshape(1, rows, HV)
    conv_parts = returned[:, rows * 2 * value_heads :].reshape(count, taps, width).transpose(1, 0, 2)
    total_conv = jnp.concatenate(
        [
            conv_parts[:, :, :qk_width].reshape(taps, HK * DK),
            conv_parts[:, :, qk_width : 2 * qk_width].reshape(taps, HK * DK),
            conv_parts[:, :, 2 * qk_width :].reshape(taps, HV * DV),
        ],
        axis=-1,
    )
    tokens_all = mixed.shape[0] * sequences * length
    return (core, grad_rows, decay_rows, rate_rows, total_conv / math.sqrt(tokens_all))


def solution(mesh):
    in_specs = (
        P("dp", "ctx", None),
        P(),
        P("dp", "ctx", None),
        P("dp", "ctx", None),
        P("dp", "ctx"),
        P("dp", "ctx", None),
    )
    out_specs = (
        P("dp", "ctx", None),
        P("dp", "ctx", None),
        P("dp", "ctx", None),
        P("dp", "ctx", None),
        P(),
    )
    count = mesh.shape["ctx"]
    per_device = HV // count if HV % count == 0 else 0
    chosen = heads_local if per_device and (per_device * HK) % HV == 0 else local
    return jax.shard_map(chosen, mesh=mesh, in_specs=in_specs, out_specs=out_specs, check_vma=False)
```

```python
import math

import jax
import jax.numpy as jnp
from jax import lax
from jax.experimental import pallas as pl
from jax.experimental.pallas import tpu as pltpu
from jax.sharding import PartitionSpec as P

HK = 8
HV = 16
DK = 128
DV = 128
BLOCK = 64


HIGHEST = lax.Precision.HIGHEST
FAST = lax.Precision.HIGH


def from_behind(x, axis, by):
    size = lax.axis_size(axis)
    pairs = [(i, i + by) for i in range(size) if 0 <= i + by < size]
    return lax.ppermute(x, axis, pairs)


def prefix(value, axis, join, neutral, backward):
    count, mine = (lax.axis_size(axis), lax.axis_index(axis))
    pieces = jax.tree.map(lambda part: lax.all_gather(part, axis), value)
    if backward:
        pieces = jax.tree.map(lambda part: part[::-1], pieces)
        mine = count - 1 - mine
    total = jax.tree.map(
        lambda part, zero: jnp.full_like(part, 0) + jnp.asarray(zero, part.dtype), value, neutral
    )

    def hop(position, total):
        longer = join(total, jax.tree.map(lambda part: part[position], pieces))
        return jax.tree.map(lambda new, old: jnp.where(position < mine, new, old), longer, total)

    return lax.fori_loop(0, count - 1, hop, total)


def prepare(mix_ext, seg_ext, conv_weight):
    margin = conv_weight.shape[0] - 1
    positions = mix_ext.shape[0] - margin
    current = seg_ext[margin:]
    summed = jnp.zeros((positions, mix_ext.shape[1]), jnp.float32)
    for tap_index in range(margin + 1):
        same_doc = (seg_ext[tap_index : tap_index + positions] == current).astype(jnp.float32)
        summed = (
            summed
            + conv_weight[tap_index][None, :]
            * mix_ext[tap_index : tap_index + positions]
            * same_doc[:, None]
        )
    activated = jax.nn.silu(summed)
    split_at = HK * DK
    queries = activated[:, :split_at].reshape(positions, HK, DK)
    keyset = activated[:, split_at : 2 * split_at].reshape(positions, HK, DK)
    values = activated[:, 2 * split_at :].reshape(positions, HV, DV)
    queries = (
        queries
        / jnp.sqrt(jnp.sum(queries * queries, axis=-1, keepdims=True) + 1e-06)
        / math.sqrt(DK)
    )
    keyset = keyset / jnp.sqrt(jnp.sum(keyset * keyset, axis=-1, keepdims=True) + 1e-06)
    repeats = HV // HK
    return (jnp.repeat(queries, repeats, axis=1), jnp.repeat(keyset, repeats, axis=1), values)


def unit_lower_inverse(strict_part):
    positions = strict_part.shape[-1]
    identity_matrix = jnp.eye(positions, dtype=jnp.float32)[None]
    result = identity_matrix - strict_part
    power = strict_part
    reach = 2
    while reach < positions:
        power = jnp.einsum("hij,hjk->hik", power, power, precision=HIGHEST)
        result = jnp.einsum("hij,hjk->hik", result, identity_matrix + power, precision=HIGHEST)
        reach = reach * 2
    return result


def block_parts(queries, keyset, values, log_decay, write_rate, segments, seg_before):
    positions = queries.shape[0]
    cumulative = jnp.cumsum(log_decay, axis=0)
    keep_state = (segments == seg_before).astype(jnp.float32)
    entering = jnp.exp(cumulative) * keep_state[:, None]
    token_position = lax.iota(jnp.int32, positions)
    same_doc = segments[:, None] == segments[None, :]
    strict = same_doc & (token_position[:, None] > token_position[None, :])
    causal = same_doc & (token_position[:, None] >= token_position[None, :])
    spread = cumulative.T[:, :, None] - cumulative.T[:, None, :]
    strict_decay = jnp.where(strict[None], jnp.exp(jnp.where(strict[None], spread, 0.0)), 0.0)
    causal_decay = jnp.where(causal[None], jnp.exp(jnp.where(causal[None], spread, 0.0)), 0.0)
    key_inner = jnp.einsum("ihd,jhd->hij", keyset, keyset, precision=HIGHEST)
    inverse = unit_lower_inverse(write_rate.T[:, :, None] * key_inner * strict_decay)
    targets = jnp.concatenate(
        [keyset * (write_rate * entering)[:, :, None], values * write_rate[:, :, None]], axis=2
    )
    solved = jnp.einsum("hij,hjd->hid", inverse, targets.transpose(1, 0, 2), precision=HIGHEST)
    write_keys = solved[:, :, :DK]
    write_values = solved[:, :, DK:]
    scores = jnp.einsum("ihd,jhd->hij", queries, keyset, precision=HIGHEST) * causal_decay
    final_sum = cumulative[-1]
    tail_decay = (
        jnp.exp(final_sum[None, :] - cumulative)
        * (segments == segments[-1]).astype(jnp.float32)[:, None]
    )
    carried = jnp.exp(final_sum) * keep_state[-1]
    tail_keys = (keyset * tail_decay[:, :, None]).transpose(1, 0, 2)
    queried = (queries * entering[:, :, None]).transpose(1, 0, 2)
    return (write_keys, write_values, scores, tail_keys, queried, carried)


@jax.custom_vjp
def lower_inverse(strict_part):
    return unit_lower_inverse_fast(strict_part)


def lower_inverse_forward(strict_part):
    inverse = unit_lower_inverse_fast(strict_part)
    return inverse, inverse


def lower_inverse_backward(inverse, grad_inverse):
    flipped = jnp.swapaxes(inverse, -1, -2)
    inner = jnp.einsum("hij,hjk->hik", flipped, grad_inverse, precision=HIGHEST)
    return (-jnp.einsum("hij,hjk->hik", inner, flipped, precision=HIGHEST),)


lower_inverse.defvjp(lower_inverse_forward, lower_inverse_backward)


def block_parts_heads(queries, keyset, values, log_decay, write_rate, segments, seg_before):
    positions = queries.shape[0]
    cumulative = jnp.cumsum(log_decay, axis=0)
    keep_state = (segments == seg_before).astype(jnp.float32)
    entering = jnp.exp(cumulative) * keep_state[:, None]
    token_position = lax.iota(jnp.int32, positions)
    same_doc = segments[:, None] == segments[None, :]
    strict = same_doc & (token_position[:, None] > token_position[None, :])
    causal = same_doc & (token_position[:, None] >= token_position[None, :])
    spread = cumulative.T[:, :, None] - cumulative.T[:, None, :]
    strict_decay = jnp.where(strict[None], jnp.exp(jnp.where(strict[None], spread, 0.0)), 0.0)
    causal_decay = jnp.where(causal[None], jnp.exp(jnp.where(causal[None], spread, 0.0)), 0.0)
    key_inner = jnp.einsum("ihd,jhd->hij", keyset, keyset, precision=HIGHEST)
    inverse = lower_inverse(write_rate.T[:, :, None] * key_inner * strict_decay)
    targets = jnp.concatenate(
        [keyset * (write_rate * entering)[:, :, None], values * write_rate[:, :, None]], axis=2
    )
    solved = jnp.einsum("hij,hjd->hid", inverse, targets.transpose(1, 0, 2), precision=HIGHEST)
    write_keys = solved[:, :, :DK]
    write_values = solved[:, :, DK:]
    scores = jnp.einsum("ihd,jhd->hij", queries, keyset, precision=HIGHEST) * causal_decay
    final_sum = cumulative[-1]
    tail_decay = (
        jnp.exp(final_sum[None, :] - cumulative)
        * (segments == segments[-1]).astype(jnp.float32)[:, None]
    )
    carried = jnp.exp(final_sum) * keep_state[-1]
    tail_keys = (keyset * tail_decay[:, :, None]).transpose(1, 0, 2)
    queried = (queries * entering[:, :, None]).transpose(1, 0, 2)
    return (write_keys, write_values, scores, tail_keys, queried, carried)


def inverse_kernel(strict_ref, out_ref):
    strict_part = strict_ref[...]
    size = strict_part.shape[-1]
    rows_at = lax.broadcasted_iota(jnp.int32, strict_part.shape, 1)
    cols_at = lax.broadcasted_iota(jnp.int32, strict_part.shape, 2)
    identity_matrix = (rows_at == cols_at).astype(jnp.float32)
    dims = (((2,), (1,)), ((0,), (0,)))
    result = identity_matrix - strict_part
    power = strict_part
    reach = 2
    while reach < size:
        power = lax.dot_general(
            power, power, dims, precision=HIGHEST, preferred_element_type=jnp.float32
        )
        result = lax.dot_general(
            result, identity_matrix + power, dims, precision=HIGHEST,
            preferred_element_type=jnp.float32,
        )
        reach = reach * 2
    out_ref[...] = result


def kernel_inverse(strict_part):
    count, size = strict_part.shape[0], strict_part.shape[-1]
    steps = max(1, (size - 1).bit_length() - 1)
    return pl.pallas_call(
        inverse_kernel,
        out_shape=jax.ShapeDtypeStruct(strict_part.shape, jnp.float32),
        in_specs=[pl.BlockSpec(memory_space=pltpu.VMEM)],
        out_specs=pl.BlockSpec(memory_space=pltpu.VMEM),
        cost_estimate=pl.CostEstimate(
            flops=12 * 2 * steps * count * size**3,
            transcendentals=0,
            bytes_accessed=2 * 4 * count * size * size,
        ),
    )(strict_part)


@jax.custom_vjp
def batch_inverse(strict_part):
    return kernel_inverse(strict_part)


def batch_inverse_forward(strict_part):
    inverse = kernel_inverse(strict_part)
    return inverse, inverse


def batch_inverse_backward(inverse, grad_inverse):
    flipped = jnp.swapaxes(inverse, -1, -2)
    inner = jnp.einsum("hij,hjk->hik", flipped, grad_inverse, precision=HIGHEST)
    return (-jnp.einsum("hij,hjk->hik", inner, flipped, precision=HIGHEST),)


batch_inverse.defvjp(batch_inverse_forward, batch_inverse_backward)


def block_system(keyset, log_decay, write_rate, segments):
    positions = keyset.shape[0]
    cumulative = jnp.cumsum(log_decay, axis=0)
    token_position = lax.iota(jnp.int32, positions)
    same_doc = segments[:, None] == segments[None, :]
    strict = same_doc & (token_position[:, None] > token_position[None, :])
    spread = cumulative.T[:, :, None] - cumulative.T[:, None, :]
    strict_decay = jnp.where(strict[None], jnp.exp(jnp.where(strict[None], spread, 0.0)), 0.0)
    key_inner = jnp.einsum("ihd,jhd->hij", keyset, keyset, precision=HIGHEST)
    return write_rate.T[:, :, None] * key_inner * strict_decay


def block_rest(inverse, queries, keyset, values, log_decay, write_rate, segments, seg_before):
    positions = queries.shape[0]
    cumulative = jnp.cumsum(log_decay, axis=0)
    keep_state = (segments == seg_before).astype(jnp.float32)
    entering = jnp.exp(cumulative) * keep_state[:, None]
    token_position = lax.iota(jnp.int32, positions)
    same_doc = segments[:, None] == segments[None, :]
    causal = same_doc & (token_position[:, None] >= token_position[None, :])
    spread = cumulative.T[:, :, None] - cumulative.T[:, None, :]
    causal_decay = jnp.where(causal[None], jnp.exp(jnp.where(causal[None], spread, 0.0)), 0.0)
    targets = jnp.concatenate(
        [keyset * (write_rate * entering)[:, :, None], values * write_rate[:, :, None]], axis=2
    )
    solved = jnp.einsum("hij,hjd->hid", inverse, targets.transpose(1, 0, 2), precision=HIGHEST)
    write_keys = solved[:, :, :DK]
    write_values = solved[:, :, DK:]
    scores = jnp.einsum("ihd,jhd->hij", queries, keyset, precision=FAST) * causal_decay
    final_sum = cumulative[-1]
    tail_decay = (
        jnp.exp(final_sum[None, :] - cumulative)
        * (segments == segments[-1]).astype(jnp.float32)[:, None]
    )
    carried = jnp.exp(final_sum) * keep_state[-1]
    tail_keys = (keyset * tail_decay[:, :, None]).transpose(1, 0, 2)
    queried = (queries * entering[:, :, None]).transpose(1, 0, 2)
    return (write_keys, write_values, scores, tail_keys, queried, carried)


def block_map(block_data):
    write_keys, write_values, scores, tail_keys, queried, carried = block_data
    identity_matrix = jnp.eye(DK, dtype=jnp.float32)
    transform = carried[:, None, None] * identity_matrix[None] - jnp.einsum(
        "hcd,hce->hde", tail_keys, write_keys, precision=HIGHEST
    )
    shift_term = jnp.einsum("hcd,hce->hde", tail_keys, write_values, precision=HIGHEST)
    return (transform, shift_term)


def block_apply(block_data, state_in):
    write_keys, write_values, scores, tail_keys, queried, carried = block_data
    fresh_values = write_values - jnp.einsum(
        "hcd,hde->hce", write_keys, state_in, precision=HIGHEST
    )
    output = jnp.einsum("hcd,hde->hce", queried, state_in, precision=HIGHEST)
    output = output + jnp.einsum("hij,hje->hie", scores, fresh_values, precision=HIGHEST)
    state_next = carried[:, None, None] * state_in + jnp.einsum(
        "hcd,hce->hde", tail_keys, fresh_values, precision=HIGHEST
    )
    return (output, state_next)

def unit_lower_inverse_fast(strict_part):
    positions = strict_part.shape[-1]
    identity_matrix = jnp.eye(positions, dtype=jnp.float32)[None]
    result = identity_matrix - strict_part
    power = strict_part
    reach = 2
    while reach < positions:
        power = jnp.einsum("hij,hjk->hik", power, power, precision=HIGHEST)
        result = jnp.einsum("hij,hjk->hik", result, identity_matrix + power, precision=HIGHEST)
        reach = reach * 2
    return result


def block_map_fast(block_data):
    write_keys, write_values, scores, tail_keys, queried, carried = block_data
    identity_matrix = jnp.eye(DK, dtype=jnp.float32)
    transform = carried[:, None, None] * identity_matrix[None] - jnp.einsum(
        "hcd,hce->hde", tail_keys, write_keys, precision=FAST
    )
    shift_term = jnp.einsum("hcd,hce->hde", tail_keys, write_values, precision=FAST)
    return (transform, shift_term)


def block_apply_fast(block_data, state_in):
    write_keys, write_values, scores, tail_keys, queried, carried = block_data
    fresh_values = write_values - jnp.einsum(
        "hcd,hde->hce", write_keys, state_in, precision=FAST
    )
    output = jnp.einsum("hcd,hde->hce", queried, state_in, precision=FAST)
    output = output + jnp.einsum("hij,hje->hie", scores, fresh_values, precision=FAST)
    state_next = carried[:, None, None] * state_in + jnp.einsum(
        "hcd,hce->hde", tail_keys, fresh_values, precision=FAST
    )
    return (output, state_next)


def section_one(mix_ext, conv_weight, log_decay, write_rate, seg_ext):
    queries, keyset, values = prepare(mix_ext, seg_ext, conv_weight)
    margin = conv_weight.shape[0] - 1
    positions = log_decay.shape[0]
    blocks = positions // BLOCK
    segments = seg_ext[margin:]
    before = seg_ext[margin - 1 : margin - 1 + positions : BLOCK]

    def blocked(tensor):
        return tensor.reshape((blocks, BLOCK) + tensor.shape[1:])

    return jax.vmap(block_parts)(
        blocked(queries),
        blocked(keyset),
        blocked(values),
        blocked(log_decay),
        blocked(write_rate),
        blocked(segments),
        before,
    )


def section_two(parts, state_in):

    def step_block(state_now, block_data):
        output, state_next = block_apply(block_data, state_now)
        return (state_next, output)

    state_out, outputs = lax.scan(step_block, state_in, parts)
    blocks = outputs.shape[0]
    return (outputs.transpose(0, 2, 1, 3).reshape(blocks * BLOCK, HV * DV), state_out)


def summarize(parts):
    identity_matrix = jnp.eye(DK, dtype=jnp.float32)
    initial = (
        jnp.broadcast_to(identity_matrix, (HV, DK, DK)),
        jnp.zeros((HV, DK, DV), jnp.float32),
    )

    def fold_block(carried_map, block_data):
        transform, shift_term = block_map(block_data)
        merged = jnp.einsum("hij,hjk->hik", transform, carried_map[0], precision=HIGHEST)
        moved = (
            jnp.einsum("hij,hjk->hik", transform, carried_map[1], precision=HIGHEST) + shift_term
        )
        return ((merged, moved), None)

    result, unused = lax.scan(fold_block, initial, parts)
    return result


def compose(earlier_map, later_map):
    merged = jnp.einsum("shij,shjk->shik", later_map[0], earlier_map[0], precision=HIGHEST)
    moved = (
        jnp.einsum("shij,shjk->shik", later_map[0], earlier_map[1], precision=HIGHEST)
        + later_map[1]
    )
    return (merged, moved)


def local(mixed, conv_weight, log_decay, write_rate, segment_ids, cotangent):
    margin = conv_weight.shape[0] - 1
    shifted_rows, shifted_segs = from_behind(
        (mixed[:, -margin:, :], segment_ids[:, -margin:].astype(jnp.bfloat16)), "ctx", 1
    )
    mix_ext = jnp.concatenate([shifted_rows, mixed], axis=1).astype(jnp.float32)
    seg_ext = jnp.concatenate([shifted_segs.astype(jnp.int32), segment_ids], axis=1)

    def first_section(mix_in, weight_in, decay_in, rate_in):
        return jax.vmap(section_one, in_axes=(0, None, 0, 0, 0))(
            mix_in, weight_in, decay_in, rate_in, seg_ext
        )

    parts, first_pull = jax.vjp(first_section, mix_ext, conv_weight, log_decay, write_rate)
    transform, shift_term = jax.vmap(summarize)(parts)
    identity_pair = (
        jnp.broadcast_to(jnp.eye(transform.shape[-1], dtype=jnp.float32), transform.shape),
        jnp.zeros_like(shift_term),
    )
    incoming = prefix((transform, shift_term), "ctx", compose, identity_pair, False)[1]
    (outputs, leaving), second_pull = jax.vjp(jax.vmap(section_two), parts, incoming)
    part_grads, local_term = second_pull((cotangent.astype(jnp.float32), jnp.zeros_like(leaving)))
    flipped = jnp.swapaxes(transform, -1, -2)
    departing = prefix((flipped, local_term), "ctx", compose, identity_pair, True)[1]
    more_grads, unused_grad = second_pull((jnp.zeros_like(outputs), departing))
    total_parts = jax.tree.map(jnp.add, part_grads, more_grads)
    grad_mix, grad_weight, grad_decay, grad_rate = first_pull(total_parts)
    returned = from_behind(grad_mix[:, :margin, :].astype(jnp.bfloat16), "ctx", -1).astype(
        jnp.float32
    )
    own_grad = grad_mix[:, margin:, :]
    own_grad = jnp.concatenate(
        [own_grad[:, :-margin, :], own_grad[:, -margin:, :] + returned], axis=1
    )
    total_conv = lax.psum(grad_weight, ("dp", "ctx"))
    tokens_all = mixed.shape[0] * lax.axis_size("dp") * mixed.shape[1] * lax.axis_size("ctx")
    return (
        outputs.astype(jnp.bfloat16),
        own_grad.astype(jnp.bfloat16),
        grad_decay,
        grad_rate,
        total_conv / math.sqrt(tokens_all),
    )


def tree_sum(value, axis):
    count = lax.axis_size(axis)
    if count & (count - 1):
        return lax.psum(value, axis)
    step = 1
    while step < count:
        value = value + lax.ppermute(value, axis, [(i, i ^ step) for i in range(count)])
        step = step * 2
    return value


def prepare_heads(mix_ext, seg_ext, conv_weight, key_heads, value_heads):
    margin = conv_weight.shape[0] - 1
    positions = mix_ext.shape[0] - margin
    current = seg_ext[margin:]
    summed = jnp.zeros((positions, mix_ext.shape[1]), jnp.float32)
    for tap_index in range(margin + 1):
        same_doc = (seg_ext[tap_index : tap_index + positions] == current).astype(jnp.float32)
        summed = (
            summed
            + conv_weight[tap_index][None, :]
            * mix_ext[tap_index : tap_index + positions]
            * same_doc[:, None]
        )
    activated = jax.nn.silu(summed)
    split_at = key_heads * DK
    queries = activated[:, :split_at].reshape(positions, key_heads, DK)
    keyset = activated[:, split_at : 2 * split_at].reshape(positions, key_heads, DK)
    values = activated[:, 2 * split_at :].reshape(positions, value_heads, DV)
    queries = (
        queries
        / jnp.sqrt(jnp.sum(queries * queries, axis=-1, keepdims=True) + 1e-06)
        / math.sqrt(DK)
    )
    keyset = keyset / jnp.sqrt(jnp.sum(keyset * keyset, axis=-1, keepdims=True) + 1e-06)
    repeats = value_heads // key_heads
    return (jnp.repeat(queries, repeats, axis=1), jnp.repeat(keyset, repeats, axis=1), values)


def combine_maps(earlier, later):
    merged = jnp.einsum("...ij,...jk->...ik", later[0], earlier[0], precision=HIGHEST)
    moved = jnp.einsum("...ij,...jk->...ik", later[0], earlier[1], precision=HIGHEST) + later[1]
    return (merged, moved)


def inclusive_states(transform, shift_term):
    blocks = transform.shape[0]
    reach = 1
    while reach < blocks:
        moved = jnp.einsum(
            "bhij,bhjk->bhik", transform[reach:], shift_term[:-reach], precision=FAST
        )
        shift_term = jnp.concatenate([shift_term[:reach], shift_term[reach:] + moved], axis=0)
        if 2 * reach < blocks:
            merged = jnp.einsum(
                "bhij,bhjk->bhik", transform[reach:], transform[:-reach], precision=FAST
            )
            transform = jnp.concatenate([transform[:reach], merged], axis=0)
        reach = reach * 2
    return shift_term


@jax.custom_vjp
def entering_states(transform, shift_term):
    return entering_forward(transform, shift_term)[0]


def entering_forward(transform, shift_term):
    eye = jnp.broadcast_to(jnp.eye(transform.shape[-1], dtype=transform.dtype), transform[:1].shape)
    shifted_maps = jnp.concatenate([eye, transform[:-1]], axis=0)
    shifted_terms = jnp.concatenate([jnp.zeros_like(shift_term[:1]), shift_term[:-1]], axis=0)
    states = inclusive_states(shifted_maps, shifted_terms)
    return states, (transform, states)


def entering_backward(saved, grad_states):
    transform, states = saved
    flipped = jnp.swapaxes(transform, -1, -2)[::-1]
    total = inclusive_states(flipped, grad_states[::-1])[::-1]
    later = total[1:]
    grad_shift = jnp.concatenate([later, jnp.zeros_like(later[:1])], axis=0)
    grad_map = jnp.einsum("bhik,bhjk->bhij", later, states[:-1], precision=FAST)
    grad_transform = jnp.concatenate([grad_map, jnp.zeros_like(transform[:1])], axis=0)
    return (grad_transform, grad_shift)


entering_states.defvjp(entering_forward, entering_backward)


def states_kernel(maps_ref, terms_ref, out_ref):
    blocks = maps_ref.shape[0]
    dims = (((2,), (1,)), ((0,), (0,)))
    state = jnp.zeros(terms_ref.shape[1:], jnp.float32)
    out_ref[0] = state
    for index in range(blocks - 1):
        state = (
            lax.dot_general(
                maps_ref[index], state, dims, precision=FAST, preferred_element_type=jnp.float32
            )
            + terms_ref[index]
        )
        out_ref[index + 1] = state


def adjoint_kernel(flipped_ref, grads_ref, out_ref):
    blocks = flipped_ref.shape[0]
    dims = (((2,), (1,)), ((0,), (0,)))
    total = grads_ref[blocks - 1]
    out_ref[blocks - 1] = total
    for index in range(blocks - 2, -1, -1):
        total = grads_ref[index] + lax.dot_general(
            flipped_ref[index], total, dims, precision=FAST, preferred_element_type=jnp.float32
        )
        out_ref[index] = total


def run_chain(kernel, maps, terms):
    blocks, heads, size = maps.shape[0], maps.shape[1], maps.shape[2]
    return pl.pallas_call(
        kernel,
        out_shape=jax.ShapeDtypeStruct(terms.shape, jnp.float32),
        in_specs=[pl.BlockSpec(memory_space=pltpu.VMEM)] * 2,
        out_specs=pl.BlockSpec(memory_space=pltpu.VMEM),
        cost_estimate=pl.CostEstimate(
            flops=6 * 2 * blocks * heads * size * size * terms.shape[-1],
            transcendentals=0,
            bytes_accessed=4 * (maps.size + 2 * terms.size),
        ),
    )(maps, terms)


@jax.custom_vjp
def chain_states(transform, shift_term):
    return run_chain(states_kernel, transform, shift_term)


def chain_forward(transform, shift_term):
    states = run_chain(states_kernel, transform, shift_term)
    return states, (transform, states)


def chain_backward(saved, grad_states):
    transform, states = saved
    flipped = jnp.swapaxes(transform, -1, -2)
    total = run_chain(adjoint_kernel, flipped, grad_states)
    later = total[1:]
    grad_shift = jnp.concatenate([later, jnp.zeros_like(later[:1])], axis=0)
    grad_map = jnp.einsum("bhik,bhjk->bhij", later, states[:-1], precision=FAST)
    grad_transform = jnp.concatenate([grad_map, jnp.zeros_like(transform[:1])], axis=0)
    return (grad_transform, grad_shift)


chain_states.defvjp(chain_forward, chain_backward)


def heads_forward(mix_in, weight_in, decay_in, rate_in, seg_ext, key_heads, value_heads):
    margin = weight_in.shape[0] - 1
    positions = decay_in.shape[0]
    blocks = positions // BLOCK
    mix_ext = jnp.concatenate([jnp.zeros((margin, mix_in.shape[1]), jnp.float32), mix_in], axis=0)
    queries, keyset, values = prepare_heads(mix_ext, seg_ext, weight_in, key_heads, value_heads)
    segments = seg_ext[margin:]
    before = seg_ext[margin - 1 : margin - 1 + positions : BLOCK]

    def blocked(tensor):
        return tensor.reshape((blocks, BLOCK) + tensor.shape[1:])

    system = jax.vmap(block_system)(
        blocked(keyset), blocked(decay_in), blocked(rate_in), blocked(segments)
    )
    inverse = batch_inverse(system.reshape((-1,) + system.shape[2:])).reshape(system.shape)
    parts = jax.vmap(block_rest)(
        inverse,
        blocked(queries),
        blocked(keyset),
        blocked(values),
        blocked(decay_in),
        blocked(rate_in),
        blocked(segments),
        before,
    )
    transform, shift_term = jax.vmap(block_map_fast)(parts)
    incoming = chain_states(transform, shift_term)
    outputs, unused = jax.vmap(block_apply_fast)(parts, incoming)
    return outputs.transpose(0, 2, 1, 3).reshape(positions, value_heads * DV)


def heads_local(mixed, conv_weight, log_decay, write_rate, segment_ids, cotangent):
    if mixed.shape[0] != 1:
        return local(mixed, conv_weight, log_decay, write_rate, segment_ids, cotangent)
    count = lax.axis_size("ctx")
    mine = lax.axis_index("ctx")
    value_heads = HV // count
    key_heads = value_heads * HK // HV
    margin = conv_weight.shape[0] - 1
    rows = mixed.shape[1]
    length = rows * count
    qk_width = key_heads * DK
    v_width = value_heads * DV

    def to_heads(array, width):
        grouped = array.reshape(rows, count, width)
        return lax.all_to_all(grouped, "ctx", 1, 0, tiled=True).reshape(length, width)

    def to_rows(array, width):
        grouped = array.reshape(count, rows, 1, width)
        return lax.all_to_all(grouped, "ctx", 0, 2, tiled=True).reshape(rows, count, width)

    own = mixed[0]
    width = 2 * qk_width + v_width
    packed = jnp.concatenate(
        [
            own[:, : HK * DK].reshape(rows, count, qk_width),
            own[:, HK * DK : 2 * HK * DK].reshape(rows, count, qk_width),
            own[:, 2 * HK * DK :].reshape(rows, count, v_width),
            cotangent[0].reshape(rows, count, v_width),
        ],
        axis=-1,
    )
    wide = to_heads(packed, width + v_width)
    mix_heads = wide[:, :width].astype(jnp.float32)
    cot_heads = wide[:, width:].astype(jnp.float32)
    seg_columns = jnp.broadcast_to(
        segment_ids[0].astype(jnp.float32)[:, None, None], (rows, count, 1)
    )
    small = jnp.concatenate(
        [
            log_decay[0].reshape(rows, count, value_heads),
            write_rate[0].reshape(rows, count, value_heads),
            seg_columns,
        ],
        axis=-1,
    )
    narrow = to_heads(small, 2 * value_heads + 1)
    decay_heads = narrow[:, :value_heads]
    rate_heads = narrow[:, value_heads : 2 * value_heads]
    segments = narrow[:, 2 * value_heads].astype(jnp.int32)
    seg_ext = jnp.concatenate([jnp.full((margin,), -1, jnp.int32), segments])

    weight_q = conv_weight[:, : HK * DK].reshape(-1, count, qk_width)[:, mine]
    weight_k = conv_weight[:, HK * DK : 2 * HK * DK].reshape(-1, count, qk_width)[:, mine]
    weight_v = conv_weight[:, 2 * HK * DK :].reshape(-1, count, v_width)[:, mine]
    weight_heads = jnp.concatenate([weight_q, weight_k, weight_v], axis=-1)

    def forward(mix_in, weight_in, decay_in, rate_in):
        return heads_forward(
            mix_in, weight_in, decay_in, rate_in, seg_ext, key_heads, value_heads
        )

    outputs, pullback = jax.vjp(forward, mix_heads, weight_heads, decay_heads, rate_heads)
    grad_mix, grad_weight, grad_decay, grad_rate = pullback(cot_heads)

    joined = jnp.concatenate([outputs.astype(jnp.bfloat16), grad_mix.astype(jnp.bfloat16)], axis=-1)
    back = to_rows(joined, v_width + width)
    core = back[:, :, :v_width].reshape(1, rows, HV * DV)
    grad_rows = jnp.concatenate(
        [
            back[:, :, v_width : v_width + qk_width].reshape(rows, HK * DK),
            back[:, :, v_width + qk_width : v_width + 2 * qk_width].reshape(rows, HK * DK),
            back[:, :, v_width + 2 * qk_width :].reshape(rows, HV * DV),
        ],
        axis=-1,
    )[None]
    taps = conv_weight.shape[0]
    sequences = lax.axis_size("dp")
    mine_dp = lax.axis_index("dp")
    row_grads = jnp.concatenate([grad_decay, grad_rate], axis=-1).reshape(count, rows * 2 * value_heads)
    pieces = jnp.concatenate(
        [
            jnp.broadcast_to(row_grads[None], (sequences,) + row_grads.shape),
            jnp.broadcast_to(
                grad_weight.reshape(1, 1, taps * width), (sequences, count, taps * width)
            ),
        ],
        axis=-1,
    ).reshape(sequences * count, 1, rows * 2 * value_heads + taps * width)
    everything = lax.all_to_all(pieces, ("dp", "ctx"), 0, 1, tiled=True)[0]
    everything = everything.reshape(sequences, count, rows * 2 * value_heads + taps * width)
    weight_sum = everything[0, :, rows * 2 * value_heads :]
    for index in range(1, sequences):
        weight_sum = weight_sum + everything[index, :, rows * 2 * value_heads :]
    returned = jnp.concatenate(
        [lax.dynamic_index_in_dim(everything, mine_dp, 0, keepdims=False)[:, : rows * 2 * value_heads], weight_sum],
        axis=-1,
    )
    grads_small = returned[:, : rows * 2 * value_heads].reshape(count, rows, 2 * value_heads)
    grads_small = grads_small.transpose(1, 0, 2)
    decay_rows = grads_small[:, :, :value_heads].reshape(1, rows, HV)
    rate_rows = grads_small[:, :, value_heads:].reshape(1, rows, HV)
    conv_parts = returned[:, rows * 2 * value_heads :].reshape(count, taps, width).transpose(1, 0, 2)
    total_conv = jnp.concatenate(
        [
            conv_parts[:, :, :qk_width].reshape(taps, HK * DK),
            conv_parts[:, :, qk_width : 2 * qk_width].reshape(taps, HK * DK),
            conv_parts[:, :, 2 * qk_width :].reshape(taps, HV * DV),
        ],
        axis=-1,
    )
    tokens_all = mixed.shape[0] * sequences * length
    return (core, grad_rows, decay_rows, rate_rows, total_conv / math.sqrt(tokens_all))


def solution(mesh):
    in_specs = (
        P("dp", "ctx", None),
        P(),
        P("dp", "ctx", None),
        P("dp", "ctx", None),
        P("dp", "ctx"),
        P("dp", "ctx", None),
    )
    out_specs = (
        P("dp", "ctx", None),
        P("dp", "ctx", None),
        P("dp", "ctx", None),
        P("dp", "ctx", None),
        P(),
    )
    count = mesh.shape["ctx"]
    per_device = HV // count if HV % count == 0 else 0
    chosen = heads_local if per_device and (per_device * HK) % HV == 0 else local
    return jax.shard_map(chosen, mesh=mesh, in_specs=in_specs, out_specs=out_specs, check_vma=False)
```

```python
import math

import jax
import jax.numpy as jnp
from jax import lax
from jax.experimental import pallas as pl
from jax.experimental.pallas import tpu as pltpu
from jax.sharding import PartitionSpec as P

HK = 8
HV = 16
DK = 128
DV = 128
BLOCK = 64


HIGHEST = lax.Precision.HIGHEST
FAST = lax.Precision.HIGH


def from_behind(x, axis, by):
    size = lax.axis_size(axis)
    pairs = [(i, i + by) for i in range(size) if 0 <= i + by < size]
    return lax.ppermute(x, axis, pairs)


def prefix(value, axis, join, neutral, backward):
    count, mine = (lax.axis_size(axis), lax.axis_index(axis))
    pieces = jax.tree.map(lambda part: lax.all_gather(part, axis), value)
    if backward:
        pieces = jax.tree.map(lambda part: part[::-1], pieces)
        mine = count - 1 - mine
    total = jax.tree.map(
        lambda part, zero: jnp.full_like(part, 0) + jnp.asarray(zero, part.dtype), value, neutral
    )

    def hop(position, total):
        longer = join(total, jax.tree.map(lambda part: part[position], pieces))
        return jax.tree.map(lambda new, old: jnp.where(position < mine, new, old), longer, total)

    return lax.fori_loop(0, count - 1, hop, total)


def prepare(mix_ext, seg_ext, conv_weight):
    margin = conv_weight.shape[0] - 1
    positions = mix_ext.shape[0] - margin
    current = seg_ext[margin:]
    summed = jnp.zeros((positions, mix_ext.shape[1]), jnp.float32)
    for tap_index in range(margin + 1):
        same_doc = (seg_ext[tap_index : tap_index + positions] == current).astype(jnp.float32)
        summed = (
            summed
            + conv_weight[tap_index][None, :]
            * mix_ext[tap_index : tap_index + positions]
            * same_doc[:, None]
        )
    activated = jax.nn.silu(summed)
    split_at = HK * DK
    queries = activated[:, :split_at].reshape(positions, HK, DK)
    keyset = activated[:, split_at : 2 * split_at].reshape(positions, HK, DK)
    values = activated[:, 2 * split_at :].reshape(positions, HV, DV)
    queries = (
        queries
        / jnp.sqrt(jnp.sum(queries * queries, axis=-1, keepdims=True) + 1e-06)
        / math.sqrt(DK)
    )
    keyset = keyset / jnp.sqrt(jnp.sum(keyset * keyset, axis=-1, keepdims=True) + 1e-06)
    repeats = HV // HK
    return (jnp.repeat(queries, repeats, axis=1), jnp.repeat(keyset, repeats, axis=1), values)


def unit_lower_inverse(strict_part):
    positions = strict_part.shape[-1]
    identity_matrix = jnp.eye(positions, dtype=jnp.float32)[None]
    result = identity_matrix - strict_part
    power = strict_part
    reach = 2
    while reach < positions:
        power = jnp.einsum("hij,hjk->hik", power, power, precision=HIGHEST)
        result = jnp.einsum("hij,hjk->hik", result, identity_matrix + power, precision=HIGHEST)
        reach = reach * 2
    return result


def block_parts(queries, keyset, values, log_decay, write_rate, segments, seg_before):
    positions = queries.shape[0]
    cumulative = jnp.cumsum(log_decay, axis=0)
    keep_state = (segments == seg_before).astype(jnp.float32)
    entering = jnp.exp(cumulative) * keep_state[:, None]
    token_position = lax.iota(jnp.int32, positions)
    same_doc = segments[:, None] == segments[None, :]
    strict = same_doc & (token_position[:, None] > token_position[None, :])
    causal = same_doc & (token_position[:, None] >= token_position[None, :])
    spread = cumulative.T[:, :, None] - cumulative.T[:, None, :]
    strict_decay = jnp.where(strict[None], jnp.exp(jnp.where(strict[None], spread, 0.0)), 0.0)
    causal_decay = jnp.where(causal[None], jnp.exp(jnp.where(causal[None], spread, 0.0)), 0.0)
    key_inner = jnp.einsum("ihd,jhd->hij", keyset, keyset, precision=HIGHEST)
    inverse = unit_lower_inverse(write_rate.T[:, :, None] * key_inner * strict_decay)
    targets = jnp.concatenate(
        [keyset * (write_rate * entering)[:, :, None], values * write_rate[:, :, None]], axis=2
    )
    solved = jnp.einsum("hij,hjd->hid", inverse, targets.transpose(1, 0, 2), precision=HIGHEST)
    write_keys = solved[:, :, :DK]
    write_values = solved[:, :, DK:]
    scores = jnp.einsum("ihd,jhd->hij", queries, keyset, precision=HIGHEST) * causal_decay
    final_sum = cumulative[-1]
    tail_decay = (
        jnp.exp(final_sum[None, :] - cumulative)
        * (segments == segments[-1]).astype(jnp.float32)[:, None]
    )
    carried = jnp.exp(final_sum) * keep_state[-1]
    tail_keys = (keyset * tail_decay[:, :, None]).transpose(1, 0, 2)
    queried = (queries * entering[:, :, None]).transpose(1, 0, 2)
    return (write_keys, write_values, scores, tail_keys, queried, carried)


@jax.custom_vjp
def lower_inverse(strict_part):
    return unit_lower_inverse_fast(strict_part)


def lower_inverse_forward(strict_part):
    inverse = unit_lower_inverse_fast(strict_part)
    return inverse, inverse


def lower_inverse_backward(inverse, grad_inverse):
    flipped = jnp.swapaxes(inverse, -1, -2)
    inner = jnp.einsum("hij,hjk->hik", flipped, grad_inverse, precision=HIGHEST)
    return (-jnp.einsum("hij,hjk->hik", inner, flipped, precision=HIGHEST),)


lower_inverse.defvjp(lower_inverse_forward, lower_inverse_backward)


def block_parts_heads(queries, keyset, values, log_decay, write_rate, segments, seg_before):
    positions = queries.shape[0]
    cumulative = jnp.cumsum(log_decay, axis=0)
    keep_state = (segments == seg_before).astype(jnp.float32)
    entering = jnp.exp(cumulative) * keep_state[:, None]
    token_position = lax.iota(jnp.int32, positions)
    same_doc = segments[:, None] == segments[None, :]
    strict = same_doc & (token_position[:, None] > token_position[None, :])
    causal = same_doc & (token_position[:, None] >= token_position[None, :])
    spread = cumulative.T[:, :, None] - cumulative.T[:, None, :]
    strict_decay = jnp.where(strict[None], jnp.exp(jnp.where(strict[None], spread, 0.0)), 0.0)
    causal_decay = jnp.where(causal[None], jnp.exp(jnp.where(causal[None], spread, 0.0)), 0.0)
    key_inner = jnp.einsum("ihd,jhd->hij", keyset, keyset, precision=HIGHEST)
    inverse = lower_inverse(write_rate.T[:, :, None] * key_inner * strict_decay)
    targets = jnp.concatenate(
        [keyset * (write_rate * entering)[:, :, None], values * write_rate[:, :, None]], axis=2
    )
    solved = jnp.einsum("hij,hjd->hid", inverse, targets.transpose(1, 0, 2), precision=HIGHEST)
    write_keys = solved[:, :, :DK]
    write_values = solved[:, :, DK:]
    scores = jnp.einsum("ihd,jhd->hij", queries, keyset, precision=HIGHEST) * causal_decay
    final_sum = cumulative[-1]
    tail_decay = (
        jnp.exp(final_sum[None, :] - cumulative)
        * (segments == segments[-1]).astype(jnp.float32)[:, None]
    )
    carried = jnp.exp(final_sum) * keep_state[-1]
    tail_keys = (keyset * tail_decay[:, :, None]).transpose(1, 0, 2)
    queried = (queries * entering[:, :, None]).transpose(1, 0, 2)
    return (write_keys, write_values, scores, tail_keys, queried, carried)


def inverse_kernel(strict_ref, out_ref):
    strict_part = strict_ref[...]
    size = strict_part.shape[-1]
    rows_at = lax.broadcasted_iota(jnp.int32, strict_part.shape, 1)
    cols_at = lax.broadcasted_iota(jnp.int32, strict_part.shape, 2)
    identity_matrix = (rows_at == cols_at).astype(jnp.float32)
    dims = (((2,), (1,)), ((0,), (0,)))
    result = identity_matrix - strict_part
    power = strict_part
    reach = 2
    while reach < size:
        power = lax.dot_general(
            power, power, dims, precision=HIGHEST, preferred_element_type=jnp.float32
        )
        result = lax.dot_general(
            result, identity_matrix + power, dims, precision=HIGHEST,
            preferred_element_type=jnp.float32,
        )
        reach = reach * 2
    out_ref[...] = result


def kernel_inverse(strict_part):
    count, size = strict_part.shape[0], strict_part.shape[-1]
    steps = max(1, (size - 1).bit_length() - 1)
    return pl.pallas_call(
        inverse_kernel,
        out_shape=jax.ShapeDtypeStruct(strict_part.shape, jnp.float32),
        in_specs=[pl.BlockSpec(memory_space=pltpu.VMEM)],
        out_specs=pl.BlockSpec(memory_space=pltpu.VMEM),
        cost_estimate=pl.CostEstimate(
            flops=12 * 2 * steps * count * size**3,
            transcendentals=0,
            bytes_accessed=2 * 4 * count * size * size,
        ),
    )(strict_part)


@jax.custom_vjp
def batch_inverse(strict_part):
    return kernel_inverse(strict_part)


def batch_inverse_forward(strict_part):
    inverse = kernel_inverse(strict_part)
    return inverse, inverse


def batch_inverse_backward(inverse, grad_inverse):
    flipped = jnp.swapaxes(inverse, -1, -2)
    inner = jnp.einsum("hij,hjk->hik", flipped, grad_inverse, precision=HIGHEST)
    return (-jnp.einsum("hij,hjk->hik", inner, flipped, precision=HIGHEST),)


batch_inverse.defvjp(batch_inverse_forward, batch_inverse_backward)


def block_system(keyset, log_decay, write_rate, segments):
    positions = keyset.shape[0]
    cumulative = jnp.cumsum(log_decay, axis=0)
    token_position = lax.iota(jnp.int32, positions)
    same_doc = segments[:, None] == segments[None, :]
    strict = same_doc & (token_position[:, None] > token_position[None, :])
    spread = cumulative.T[:, :, None] - cumulative.T[:, None, :]
    strict_decay = jnp.where(strict[None], jnp.exp(jnp.where(strict[None], spread, 0.0)), 0.0)
    key_inner = jnp.einsum("ihd,jhd->hij", keyset, keyset, precision=HIGHEST)
    return write_rate.T[:, :, None] * key_inner * strict_decay


def block_rest(inverse, queries, keyset, values, log_decay, write_rate, segments, seg_before):
    positions = queries.shape[0]
    cumulative = jnp.cumsum(log_decay, axis=0)
    keep_state = (segments == seg_before).astype(jnp.float32)
    entering = jnp.exp(cumulative) * keep_state[:, None]
    token_position = lax.iota(jnp.int32, positions)
    same_doc = segments[:, None] == segments[None, :]
    causal = same_doc & (token_position[:, None] >= token_position[None, :])
    spread = cumulative.T[:, :, None] - cumulative.T[:, None, :]
    causal_decay = jnp.where(causal[None], jnp.exp(jnp.where(causal[None], spread, 0.0)), 0.0)
    targets = jnp.concatenate(
        [keyset * (write_rate * entering)[:, :, None], values * write_rate[:, :, None]], axis=2
    )
    solved = jnp.einsum("hij,hjd->hid", inverse, targets.transpose(1, 0, 2), precision=FAST)
    write_keys = solved[:, :, :DK]
    write_values = solved[:, :, DK:]
    scores = jnp.einsum("ihd,jhd->hij", queries, keyset, precision=FAST) * causal_decay
    final_sum = cumulative[-1]
    tail_decay = (
        jnp.exp(final_sum[None, :] - cumulative)
        * (segments == segments[-1]).astype(jnp.float32)[:, None]
    )
    carried = jnp.exp(final_sum) * keep_state[-1]
    tail_keys = (keyset * tail_decay[:, :, None]).transpose(1, 0, 2)
    queried = (queries * entering[:, :, None]).transpose(1, 0, 2)
    return (write_keys, write_values, scores, tail_keys, queried, carried)


def block_map(block_data):
    write_keys, write_values, scores, tail_keys, queried, carried = block_data
    identity_matrix = jnp.eye(DK, dtype=jnp.float32)
    transform = carried[:, None, None] * identity_matrix[None] - jnp.einsum(
        "hcd,hce->hde", tail_keys, write_keys, precision=HIGHEST
    )
    shift_term = jnp.einsum("hcd,hce->hde", tail_keys, write_values, precision=HIGHEST)
    return (transform, shift_term)


def block_apply(block_data, state_in):
    write_keys, write_values, scores, tail_keys, queried, carried = block_data
    fresh_values = write_values - jnp.einsum(
        "hcd,hde->hce", write_keys, state_in, precision=HIGHEST
    )
    output = jnp.einsum("hcd,hde->hce", queried, state_in, precision=HIGHEST)
    output = output + jnp.einsum("hij,hje->hie", scores, fresh_values, precision=HIGHEST)
    state_next = carried[:, None, None] * state_in + jnp.einsum(
        "hcd,hce->hde", tail_keys, fresh_values, precision=HIGHEST
    )
    return (output, state_next)

def unit_lower_inverse_fast(strict_part):
    positions = strict_part.shape[-1]
    identity_matrix = jnp.eye(positions, dtype=jnp.float32)[None]
    result = identity_matrix - strict_part
    power = strict_part
    reach = 2
    while reach < positions:
        power = jnp.einsum("hij,hjk->hik", power, power, precision=HIGHEST)
        result = jnp.einsum("hij,hjk->hik", result, identity_matrix + power, precision=HIGHEST)
        reach = reach * 2
    return result


def block_map_fast(block_data):
    write_keys, write_values, scores, tail_keys, queried, carried = block_data
    identity_matrix = jnp.eye(DK, dtype=jnp.float32)
    transform = carried[:, None, None] * identity_matrix[None] - jnp.einsum(
        "hcd,hce->hde", tail_keys, write_keys, precision=FAST
    )
    shift_term = jnp.einsum("hcd,hce->hde", tail_keys, write_values, precision=FAST)
    return (transform, shift_term)


def block_apply_fast(block_data, state_in):
    write_keys, write_values, scores, tail_keys, queried, carried = block_data
    fresh_values = write_values - jnp.einsum(
        "hcd,hde->hce", write_keys, state_in, precision=FAST
    )
    output = jnp.einsum("hcd,hde->hce", queried, state_in, precision=FAST)
    output = output + jnp.einsum("hij,hje->hie", scores, fresh_values, precision=FAST)
    state_next = carried[:, None, None] * state_in + jnp.einsum(
        "hcd,hce->hde", tail_keys, fresh_values, precision=FAST
    )
    return (output, state_next)


def section_one(mix_ext, conv_weight, log_decay, write_rate, seg_ext):
    queries, keyset, values = prepare(mix_ext, seg_ext, conv_weight)
    margin = conv_weight.shape[0] - 1
    positions = log_decay.shape[0]
    blocks = positions // BLOCK
    segments = seg_ext[margin:]
    before = seg_ext[margin - 1 : margin - 1 + positions : BLOCK]

    def blocked(tensor):
        return tensor.reshape((blocks, BLOCK) + tensor.shape[1:])

    return jax.vmap(block_parts)(
        blocked(queries),
        blocked(keyset),
        blocked(values),
        blocked(log_decay),
        blocked(write_rate),
        blocked(segments),
        before,
    )


def section_two(parts, state_in):

    def step_block(state_now, block_data):
        output, state_next = block_apply(block_data, state_now)
        return (state_next, output)

    state_out, outputs = lax.scan(step_block, state_in, parts)
    blocks = outputs.shape[0]
    return (outputs.transpose(0, 2, 1, 3).reshape(blocks * BLOCK, HV * DV), state_out)


def summarize(parts):
    identity_matrix = jnp.eye(DK, dtype=jnp.float32)
    initial = (
        jnp.broadcast_to(identity_matrix, (HV, DK, DK)),
        jnp.zeros((HV, DK, DV), jnp.float32),
    )

    def fold_block(carried_map, block_data):
        transform, shift_term = block_map(block_data)
        merged = jnp.einsum("hij,hjk->hik", transform, carried_map[0], precision=HIGHEST)
        moved = (
            jnp.einsum("hij,hjk->hik", transform, carried_map[1], precision=HIGHEST) + shift_term
        )
        return ((merged, moved), None)

    result, unused = lax.scan(fold_block, initial, parts)
    return result


def compose(earlier_map, later_map):
    merged = jnp.einsum("shij,shjk->shik", later_map[0], earlier_map[0], precision=HIGHEST)
    moved = (
        jnp.einsum("shij,shjk->shik", later_map[0], earlier_map[1], precision=HIGHEST)
        + later_map[1]
    )
    return (merged, moved)


def local(mixed, conv_weight, log_decay, write_rate, segment_ids, cotangent):
    margin = conv_weight.shape[0] - 1
    shifted_rows, shifted_segs = from_behind(
        (mixed[:, -margin:, :], segment_ids[:, -margin:].astype(jnp.bfloat16)), "ctx", 1
    )
    mix_ext = jnp.concatenate([shifted_rows, mixed], axis=1).astype(jnp.float32)
    seg_ext = jnp.concatenate([shifted_segs.astype(jnp.int32), segment_ids], axis=1)

    def first_section(mix_in, weight_in, decay_in, rate_in):
        return jax.vmap(section_one, in_axes=(0, None, 0, 0, 0))(
            mix_in, weight_in, decay_in, rate_in, seg_ext
        )

    parts, first_pull = jax.vjp(first_section, mix_ext, conv_weight, log_decay, write_rate)
    transform, shift_term = jax.vmap(summarize)(parts)
    identity_pair = (
        jnp.broadcast_to(jnp.eye(transform.shape[-1], dtype=jnp.float32), transform.shape),
        jnp.zeros_like(shift_term),
    )
    incoming = prefix((transform, shift_term), "ctx", compose, identity_pair, False)[1]
    (outputs, leaving), second_pull = jax.vjp(jax.vmap(section_two), parts, incoming)
    part_grads, local_term = second_pull((cotangent.astype(jnp.float32), jnp.zeros_like(leaving)))
    flipped = jnp.swapaxes(transform, -1, -2)
    departing = prefix((flipped, local_term), "ctx", compose, identity_pair, True)[1]
    more_grads, unused_grad = second_pull((jnp.zeros_like(outputs), departing))
    total_parts = jax.tree.map(jnp.add, part_grads, more_grads)
    grad_mix, grad_weight, grad_decay, grad_rate = first_pull(total_parts)
    returned = from_behind(grad_mix[:, :margin, :].astype(jnp.bfloat16), "ctx", -1).astype(
        jnp.float32
    )
    own_grad = grad_mix[:, margin:, :]
    own_grad = jnp.concatenate(
        [own_grad[:, :-margin, :], own_grad[:, -margin:, :] + returned], axis=1
    )
    total_conv = lax.psum(grad_weight, ("dp", "ctx"))
    tokens_all = mixed.shape[0] * lax.axis_size("dp") * mixed.shape[1] * lax.axis_size("ctx")
    return (
        outputs.astype(jnp.bfloat16),
        own_grad.astype(jnp.bfloat16),
        grad_decay,
        grad_rate,
        total_conv / math.sqrt(tokens_all),
    )


def tree_sum(value, axis):
    count = lax.axis_size(axis)
    if count & (count - 1):
        return lax.psum(value, axis)
    step = 1
    while step < count:
        value = value + lax.ppermute(value, axis, [(i, i ^ step) for i in range(count)])
        step = step * 2
    return value


def prepare_heads(mix_ext, seg_ext, conv_weight, key_heads, value_heads):
    margin = conv_weight.shape[0] - 1
    positions = mix_ext.shape[0] - margin
    current = seg_ext[margin:]
    summed = jnp.zeros((positions, mix_ext.shape[1]), jnp.float32)
    for tap_index in range(margin + 1):
        same_doc = (seg_ext[tap_index : tap_index + positions] == current).astype(jnp.float32)
        summed = (
            summed
            + conv_weight[tap_index][None, :]
            * mix_ext[tap_index : tap_index + positions]
            * same_doc[:, None]
        )
    activated = jax.nn.silu(summed)
    split_at = key_heads * DK
    queries = activated[:, :split_at].reshape(positions, key_heads, DK)
    keyset = activated[:, split_at : 2 * split_at].reshape(positions, key_heads, DK)
    values = activated[:, 2 * split_at :].reshape(positions, value_heads, DV)
    queries = (
        queries
        / jnp.sqrt(jnp.sum(queries * queries, axis=-1, keepdims=True) + 1e-06)
        / math.sqrt(DK)
    )
    keyset = keyset / jnp.sqrt(jnp.sum(keyset * keyset, axis=-1, keepdims=True) + 1e-06)
    repeats = value_heads // key_heads
    return (jnp.repeat(queries, repeats, axis=1), jnp.repeat(keyset, repeats, axis=1), values)


def combine_maps(earlier, later):
    merged = jnp.einsum("...ij,...jk->...ik", later[0], earlier[0], precision=HIGHEST)
    moved = jnp.einsum("...ij,...jk->...ik", later[0], earlier[1], precision=HIGHEST) + later[1]
    return (merged, moved)


def inclusive_states(transform, shift_term):
    blocks = transform.shape[0]
    reach = 1
    while reach < blocks:
        moved = jnp.einsum(
            "bhij,bhjk->bhik", transform[reach:], shift_term[:-reach], precision=FAST
        )
        shift_term = jnp.concatenate([shift_term[:reach], shift_term[reach:] + moved], axis=0)
        if 2 * reach < blocks:
            merged = jnp.einsum(
                "bhij,bhjk->bhik", transform[reach:], transform[:-reach], precision=FAST
            )
            transform = jnp.concatenate([transform[:reach], merged], axis=0)
        reach = reach * 2
    return shift_term


@jax.custom_vjp
def entering_states(transform, shift_term):
    return entering_forward(transform, shift_term)[0]


def entering_forward(transform, shift_term):
    eye = jnp.broadcast_to(jnp.eye(transform.shape[-1], dtype=transform.dtype), transform[:1].shape)
    shifted_maps = jnp.concatenate([eye, transform[:-1]], axis=0)
    shifted_terms = jnp.concatenate([jnp.zeros_like(shift_term[:1]), shift_term[:-1]], axis=0)
    states = inclusive_states(shifted_maps, shifted_terms)
    return states, (transform, states)


def entering_backward(saved, grad_states):
    transform, states = saved
    flipped = jnp.swapaxes(transform, -1, -2)[::-1]
    total = inclusive_states(flipped, grad_states[::-1])[::-1]
    later = total[1:]
    grad_shift = jnp.concatenate([later, jnp.zeros_like(later[:1])], axis=0)
    grad_map = jnp.einsum("bhik,bhjk->bhij", later, states[:-1], precision=FAST)
    grad_transform = jnp.concatenate([grad_map, jnp.zeros_like(transform[:1])], axis=0)
    return (grad_transform, grad_shift)


entering_states.defvjp(entering_forward, entering_backward)


def states_kernel(maps_ref, terms_ref, out_ref):
    blocks = maps_ref.shape[0]
    dims = (((2,), (1,)), ((0,), (0,)))
    state = jnp.zeros(terms_ref.shape[1:], jnp.float32)
    out_ref[0] = state
    for index in range(blocks - 1):
        state = (
            lax.dot_general(
                maps_ref[index], state, dims, precision=FAST, preferred_element_type=jnp.float32
            )
            + terms_ref[index]
        )
        out_ref[index + 1] = state


def adjoint_kernel(flipped_ref, grads_ref, out_ref):
    blocks = flipped_ref.shape[0]
    dims = (((2,), (1,)), ((0,), (0,)))
    total = grads_ref[blocks - 1]
    out_ref[blocks - 1] = total
    for index in range(blocks - 2, -1, -1):
        total = grads_ref[index] + lax.dot_general(
            flipped_ref[index], total, dims, precision=FAST, preferred_element_type=jnp.float32
        )
        out_ref[index] = total


def run_chain(kernel, maps, terms):
    blocks, heads, size = maps.shape[0], maps.shape[1], maps.shape[2]
    return pl.pallas_call(
        kernel,
        out_shape=jax.ShapeDtypeStruct(terms.shape, jnp.float32),
        in_specs=[pl.BlockSpec(memory_space=pltpu.VMEM)] * 2,
        out_specs=pl.BlockSpec(memory_space=pltpu.VMEM),
        cost_estimate=pl.CostEstimate(
            flops=6 * 2 * blocks * heads * size * size * terms.shape[-1],
            transcendentals=0,
            bytes_accessed=4 * (maps.size + 2 * terms.size),
        ),
    )(maps, terms)


@jax.custom_vjp
def chain_states(transform, shift_term):
    return run_chain(states_kernel, transform, shift_term)


def chain_forward(transform, shift_term):
    states = run_chain(states_kernel, transform, shift_term)
    return states, (transform, states)


def chain_backward(saved, grad_states):
    transform, states = saved
    flipped = jnp.swapaxes(transform, -1, -2)
    total = run_chain(adjoint_kernel, flipped, grad_states)
    later = total[1:]
    grad_shift = jnp.concatenate([later, jnp.zeros_like(later[:1])], axis=0)
    grad_map = jnp.einsum("bhik,bhjk->bhij", later, states[:-1], precision=FAST)
    grad_transform = jnp.concatenate([grad_map, jnp.zeros_like(transform[:1])], axis=0)
    return (grad_transform, grad_shift)


chain_states.defvjp(chain_forward, chain_backward)


def heads_forward(mix_in, weight_in, decay_in, rate_in, seg_ext, key_heads, value_heads):
    margin = weight_in.shape[0] - 1
    positions = decay_in.shape[0]
    blocks = positions // BLOCK
    mix_ext = jnp.concatenate([jnp.zeros((margin, mix_in.shape[1]), jnp.float32), mix_in], axis=0)
    queries, keyset, values = prepare_heads(mix_ext, seg_ext, weight_in, key_heads, value_heads)
    segments = seg_ext[margin:]
    before = seg_ext[margin - 1 : margin - 1 + positions : BLOCK]

    def blocked(tensor):
        return tensor.reshape((blocks, BLOCK) + tensor.shape[1:])

    system = jax.vmap(block_system)(
        blocked(keyset), blocked(decay_in), blocked(rate_in), blocked(segments)
    )
    inverse = batch_inverse(system.reshape((-1,) + system.shape[2:])).reshape(system.shape)
    parts = jax.vmap(block_rest)(
        inverse,
        blocked(queries),
        blocked(keyset),
        blocked(values),
        blocked(decay_in),
        blocked(rate_in),
        blocked(segments),
        before,
    )
    transform, shift_term = jax.vmap(block_map_fast)(parts)
    incoming = chain_states(transform, shift_term)
    outputs, unused = jax.vmap(block_apply_fast)(parts, incoming)
    return outputs.transpose(0, 2, 1, 3).reshape(positions, value_heads * DV)


def heads_local(mixed, conv_weight, log_decay, write_rate, segment_ids, cotangent):
    if mixed.shape[0] != 1:
        return local(mixed, conv_weight, log_decay, write_rate, segment_ids, cotangent)
    count = lax.axis_size("ctx")
    mine = lax.axis_index("ctx")
    value_heads = HV // count
    key_heads = value_heads * HK // HV
    margin = conv_weight.shape[0] - 1
    rows = mixed.shape[1]
    length = rows * count
    qk_width = key_heads * DK
    v_width = value_heads * DV

    def to_heads(array, width):
        grouped = array.reshape(rows, count, width)
        return lax.all_to_all(grouped, "ctx", 1, 0, tiled=True).reshape(length, width)

    def to_rows(array, width):
        grouped = array.reshape(count, rows, 1, width)
        return lax.all_to_all(grouped, "ctx", 0, 2, tiled=True).reshape(rows, count, width)

    own = mixed[0]
    width = 2 * qk_width + v_width
    packed = jnp.concatenate(
        [
            own[:, : HK * DK].reshape(rows, count, qk_width),
            own[:, HK * DK : 2 * HK * DK].reshape(rows, count, qk_width),
            own[:, 2 * HK * DK :].reshape(rows, count, v_width),
            cotangent[0].reshape(rows, count, v_width),
        ],
        axis=-1,
    )
    wide = to_heads(packed, width + v_width)
    mix_heads = wide[:, :width].astype(jnp.float32)
    cot_heads = wide[:, width:].astype(jnp.float32)
    seg_columns = jnp.broadcast_to(
        segment_ids[0].astype(jnp.float32)[:, None, None], (rows, count, 1)
    )
    small = jnp.concatenate(
        [
            log_decay[0].reshape(rows, count, value_heads),
            write_rate[0].reshape(rows, count, value_heads),
            seg_columns,
        ],
        axis=-1,
    )
    narrow = to_heads(small, 2 * value_heads + 1)
    decay_heads = narrow[:, :value_heads]
    rate_heads = narrow[:, value_heads : 2 * value_heads]
    segments = narrow[:, 2 * value_heads].astype(jnp.int32)
    seg_ext = jnp.concatenate([jnp.full((margin,), -1, jnp.int32), segments])

    weight_q = conv_weight[:, : HK * DK].reshape(-1, count, qk_width)[:, mine]
    weight_k = conv_weight[:, HK * DK : 2 * HK * DK].reshape(-1, count, qk_width)[:, mine]
    weight_v = conv_weight[:, 2 * HK * DK :].reshape(-1, count, v_width)[:, mine]
    weight_heads = jnp.concatenate([weight_q, weight_k, weight_v], axis=-1)

    def forward(mix_in, weight_in, decay_in, rate_in):
        return heads_forward(
            mix_in, weight_in, decay_in, rate_in, seg_ext, key_heads, value_heads
        )

    outputs, pullback = jax.vjp(forward, mix_heads, weight_heads, decay_heads, rate_heads)
    grad_mix, grad_weight, grad_decay, grad_rate = pullback(cot_heads)

    joined = jnp.concatenate([outputs.astype(jnp.bfloat16), grad_mix.astype(jnp.bfloat16)], axis=-1)
    back = to_rows(joined, v_width + width)
    core = back[:, :, :v_width].reshape(1, rows, HV * DV)
    grad_rows = jnp.concatenate(
        [
            back[:, :, v_width : v_width + qk_width].reshape(rows, HK * DK),
            back[:, :, v_width + qk_width : v_width + 2 * qk_width].reshape(rows, HK * DK),
            back[:, :, v_width + 2 * qk_width :].reshape(rows, HV * DV),
        ],
        axis=-1,
    )[None]
    taps = conv_weight.shape[0]
    sequences = lax.axis_size("dp")
    mine_dp = lax.axis_index("dp")
    row_grads = jnp.concatenate([grad_decay, grad_rate], axis=-1).reshape(count, rows * 2 * value_heads)
    pieces = jnp.concatenate(
        [
            jnp.broadcast_to(row_grads[None], (sequences,) + row_grads.shape),
            jnp.broadcast_to(
                grad_weight.reshape(1, 1, taps * width), (sequences, count, taps * width)
            ),
        ],
        axis=-1,
    ).reshape(sequences * count, 1, rows * 2 * value_heads + taps * width)
    everything = lax.all_to_all(pieces, ("dp", "ctx"), 0, 1, tiled=True)[0]
    everything = everything.reshape(sequences, count, rows * 2 * value_heads + taps * width)
    weight_sum = everything[0, :, rows * 2 * value_heads :]
    for index in range(1, sequences):
        weight_sum = weight_sum + everything[index, :, rows * 2 * value_heads :]
    returned = jnp.concatenate(
        [lax.dynamic_index_in_dim(everything, mine_dp, 0, keepdims=False)[:, : rows * 2 * value_heads], weight_sum],
        axis=-1,
    )
    grads_small = returned[:, : rows * 2 * value_heads].reshape(count, rows, 2 * value_heads)
    grads_small = grads_small.transpose(1, 0, 2)
    decay_rows = grads_small[:, :, :value_heads].reshape(1, rows, HV)
    rate_rows = grads_small[:, :, value_heads:].reshape(1, rows, HV)
    conv_parts = returned[:, rows * 2 * value_heads :].reshape(count, taps, width).transpose(1, 0, 2)
    total_conv = jnp.concatenate(
        [
            conv_parts[:, :, :qk_width].reshape(taps, HK * DK),
            conv_parts[:, :, qk_width : 2 * qk_width].reshape(taps, HK * DK),
            conv_parts[:, :, 2 * qk_width :].reshape(taps, HV * DV),
        ],
        axis=-1,
    )
    tokens_all = mixed.shape[0] * sequences * length
    return (core, grad_rows, decay_rows, rate_rows, total_conv / math.sqrt(tokens_all))


def solution(mesh):
    in_specs = (
        P("dp", "ctx", None),
        P(),
        P("dp", "ctx", None),
        P("dp", "ctx", None),
        P("dp", "ctx"),
        P("dp", "ctx", None),
    )
    out_specs = (
        P("dp", "ctx", None),
        P("dp", "ctx", None),
        P("dp", "ctx", None),
        P("dp", "ctx", None),
        P(),
    )
    count = mesh.shape["ctx"]
    per_device = HV // count if HV % count == 0 else 0
    chosen = heads_local if per_device and (per_device * HK) % HV == 0 else local
    return jax.shard_map(chosen, mesh=mesh, in_specs=in_specs, out_specs=out_specs, check_vma=False)
```

```python
import math

import jax
import jax.numpy as jnp
from jax import lax
from jax.experimental import pallas as pl
from jax.experimental.pallas import tpu as pltpu
from jax.sharding import PartitionSpec as P

HK = 8
HV = 16
DK = 128
DV = 128
BLOCK = 64


HIGHEST = lax.Precision.HIGHEST
FAST = lax.Precision.HIGH


def from_behind(x, axis, by):
    size = lax.axis_size(axis)
    pairs = [(i, i + by) for i in range(size) if 0 <= i + by < size]
    return lax.ppermute(x, axis, pairs)


def prefix(value, axis, join, neutral, backward):
    count, mine = (lax.axis_size(axis), lax.axis_index(axis))
    pieces = jax.tree.map(lambda part: lax.all_gather(part, axis), value)
    if backward:
        pieces = jax.tree.map(lambda part: part[::-1], pieces)
        mine = count - 1 - mine
    total = jax.tree.map(
        lambda part, zero: jnp.full_like(part, 0) + jnp.asarray(zero, part.dtype), value, neutral
    )

    def hop(position, total):
        longer = join(total, jax.tree.map(lambda part: part[position], pieces))
        return jax.tree.map(lambda new, old: jnp.where(position < mine, new, old), longer, total)

    return lax.fori_loop(0, count - 1, hop, total)


def prepare(mix_ext, seg_ext, conv_weight):
    margin = conv_weight.shape[0] - 1
    positions = mix_ext.shape[0] - margin
    current = seg_ext[margin:]
    summed = jnp.zeros((positions, mix_ext.shape[1]), jnp.float32)
    for tap_index in range(margin + 1):
        same_doc = (seg_ext[tap_index : tap_index + positions] == current).astype(jnp.float32)
        summed = (
            summed
            + conv_weight[tap_index][None, :]
            * mix_ext[tap_index : tap_index + positions]
            * same_doc[:, None]
        )
    activated = jax.nn.silu(summed)
    split_at = HK * DK
    queries = activated[:, :split_at].reshape(positions, HK, DK)
    keyset = activated[:, split_at : 2 * split_at].reshape(positions, HK, DK)
    values = activated[:, 2 * split_at :].reshape(positions, HV, DV)
    queries = (
        queries
        / jnp.sqrt(jnp.sum(queries * queries, axis=-1, keepdims=True) + 1e-06)
        / math.sqrt(DK)
    )
    keyset = keyset / jnp.sqrt(jnp.sum(keyset * keyset, axis=-1, keepdims=True) + 1e-06)
    repeats = HV // HK
    return (jnp.repeat(queries, repeats, axis=1), jnp.repeat(keyset, repeats, axis=1), values)


def unit_lower_inverse(strict_part):
    positions = strict_part.shape[-1]
    identity_matrix = jnp.eye(positions, dtype=jnp.float32)[None]
    result = identity_matrix - strict_part
    power = strict_part
    reach = 2
    while reach < positions:
        power = jnp.einsum("hij,hjk->hik", power, power, precision=HIGHEST)
        result = jnp.einsum("hij,hjk->hik", result, identity_matrix + power, precision=HIGHEST)
        reach = reach * 2
    return result


def block_parts(queries, keyset, values, log_decay, write_rate, segments, seg_before):
    positions = queries.shape[0]
    cumulative = jnp.cumsum(log_decay, axis=0)
    keep_state = (segments == seg_before).astype(jnp.float32)
    entering = jnp.exp(cumulative) * keep_state[:, None]
    token_position = lax.iota(jnp.int32, positions)
    same_doc = segments[:, None] == segments[None, :]
    strict = same_doc & (token_position[:, None] > token_position[None, :])
    causal = same_doc & (token_position[:, None] >= token_position[None, :])
    spread = cumulative.T[:, :, None] - cumulative.T[:, None, :]
    strict_decay = jnp.where(strict[None], jnp.exp(jnp.where(strict[None], spread, 0.0)), 0.0)
    causal_decay = jnp.where(causal[None], jnp.exp(jnp.where(causal[None], spread, 0.0)), 0.0)
    key_inner = jnp.einsum("ihd,jhd->hij", keyset, keyset, precision=HIGHEST)
    inverse = unit_lower_inverse(write_rate.T[:, :, None] * key_inner * strict_decay)
    targets = jnp.concatenate(
        [keyset * (write_rate * entering)[:, :, None], values * write_rate[:, :, None]], axis=2
    )
    solved = jnp.einsum("hij,hjd->hid", inverse, targets.transpose(1, 0, 2), precision=HIGHEST)
    write_keys = solved[:, :, :DK]
    write_values = solved[:, :, DK:]
    scores = jnp.einsum("ihd,jhd->hij", queries, keyset, precision=HIGHEST) * causal_decay
    final_sum = cumulative[-1]
    tail_decay = (
        jnp.exp(final_sum[None, :] - cumulative)
        * (segments == segments[-1]).astype(jnp.float32)[:, None]
    )
    carried = jnp.exp(final_sum) * keep_state[-1]
    tail_keys = (keyset * tail_decay[:, :, None]).transpose(1, 0, 2)
    queried = (queries * entering[:, :, None]).transpose(1, 0, 2)
    return (write_keys, write_values, scores, tail_keys, queried, carried)


@jax.custom_vjp
def lower_inverse(strict_part):
    return unit_lower_inverse_fast(strict_part)


def lower_inverse_forward(strict_part):
    inverse = unit_lower_inverse_fast(strict_part)
    return inverse, inverse


def lower_inverse_backward(inverse, grad_inverse):
    flipped = jnp.swapaxes(inverse, -1, -2)
    inner = jnp.einsum("hij,hjk->hik", flipped, grad_inverse, precision=HIGHEST)
    return (-jnp.einsum("hij,hjk->hik", inner, flipped, precision=HIGHEST),)


lower_inverse.defvjp(lower_inverse_forward, lower_inverse_backward)


def block_parts_heads(queries, keyset, values, log_decay, write_rate, segments, seg_before):
    positions = queries.shape[0]
    cumulative = jnp.cumsum(log_decay, axis=0)
    keep_state = (segments == seg_before).astype(jnp.float32)
    entering = jnp.exp(cumulative) * keep_state[:, None]
    token_position = lax.iota(jnp.int32, positions)
    same_doc = segments[:, None] == segments[None, :]
    strict = same_doc & (token_position[:, None] > token_position[None, :])
    causal = same_doc & (token_position[:, None] >= token_position[None, :])
    spread = cumulative.T[:, :, None] - cumulative.T[:, None, :]
    strict_decay = jnp.where(strict[None], jnp.exp(jnp.where(strict[None], spread, 0.0)), 0.0)
    causal_decay = jnp.where(causal[None], jnp.exp(jnp.where(causal[None], spread, 0.0)), 0.0)
    key_inner = jnp.einsum("ihd,jhd->hij", keyset, keyset, precision=HIGHEST)
    inverse = lower_inverse(write_rate.T[:, :, None] * key_inner * strict_decay)
    targets = jnp.concatenate(
        [keyset * (write_rate * entering)[:, :, None], values * write_rate[:, :, None]], axis=2
    )
    solved = jnp.einsum("hij,hjd->hid", inverse, targets.transpose(1, 0, 2), precision=HIGHEST)
    write_keys = solved[:, :, :DK]
    write_values = solved[:, :, DK:]
    scores = jnp.einsum("ihd,jhd->hij", queries, keyset, precision=HIGHEST) * causal_decay
    final_sum = cumulative[-1]
    tail_decay = (
        jnp.exp(final_sum[None, :] - cumulative)
        * (segments == segments[-1]).astype(jnp.float32)[:, None]
    )
    carried = jnp.exp(final_sum) * keep_state[-1]
    tail_keys = (keyset * tail_decay[:, :, None]).transpose(1, 0, 2)
    queried = (queries * entering[:, :, None]).transpose(1, 0, 2)
    return (write_keys, write_values, scores, tail_keys, queried, carried)


def inverse_kernel(strict_ref, out_ref):
    strict_part = strict_ref[...]
    size = strict_part.shape[-1]
    rows_at = lax.broadcasted_iota(jnp.int32, strict_part.shape, 1)
    cols_at = lax.broadcasted_iota(jnp.int32, strict_part.shape, 2)
    identity_matrix = (rows_at == cols_at).astype(jnp.float32)
    dims = (((2,), (1,)), ((0,), (0,)))
    result = identity_matrix - strict_part
    power = strict_part
    reach = 2
    while reach < size:
        power = lax.dot_general(
            power, power, dims, precision=HIGHEST, preferred_element_type=jnp.float32
        )
        result = lax.dot_general(
            result, identity_matrix + power, dims, precision=HIGHEST,
            preferred_element_type=jnp.float32,
        )
        reach = reach * 2
    out_ref[...] = result


def kernel_inverse(strict_part):
    count, size = strict_part.shape[0], strict_part.shape[-1]
    steps = max(1, (size - 1).bit_length() - 1)
    return pl.pallas_call(
        inverse_kernel,
        out_shape=jax.ShapeDtypeStruct(strict_part.shape, jnp.float32),
        in_specs=[pl.BlockSpec(memory_space=pltpu.VMEM)],
        out_specs=pl.BlockSpec(memory_space=pltpu.VMEM),
        cost_estimate=pl.CostEstimate(
            flops=12 * 2 * steps * count * size**3,
            transcendentals=0,
            bytes_accessed=2 * 4 * count * size * size,
        ),
    )(strict_part)


@jax.custom_vjp
def batch_inverse(strict_part):
    return kernel_inverse(strict_part)


def batch_inverse_forward(strict_part):
    inverse = kernel_inverse(strict_part)
    return inverse, inverse


def batch_inverse_backward(inverse, grad_inverse):
    flipped = jnp.swapaxes(inverse, -1, -2)
    inner = jnp.einsum("hij,hjk->hik", flipped, grad_inverse, precision=HIGHEST)
    return (-jnp.einsum("hij,hjk->hik", inner, flipped, precision=HIGHEST),)


batch_inverse.defvjp(batch_inverse_forward, batch_inverse_backward)


def block_system(keyset, log_decay, write_rate, segments):
    positions = keyset.shape[0]
    cumulative = jnp.cumsum(log_decay, axis=0)
    token_position = lax.iota(jnp.int32, positions)
    same_doc = segments[:, None] == segments[None, :]
    strict = same_doc & (token_position[:, None] > token_position[None, :])
    spread = cumulative.T[:, :, None] - cumulative.T[:, None, :]
    strict_decay = jnp.where(strict[None], jnp.exp(jnp.where(strict[None], spread, 0.0)), 0.0)
    key_inner = jnp.einsum("ihd,jhd->hij", keyset, keyset, precision=HIGHEST)
    return (write_rate.T[:, :, None] * key_inner * strict_decay, strict_decay)


def block_rest(inverse, strict_decay, queries, keyset, values, log_decay, write_rate, segments, seg_before):
    positions = queries.shape[0]
    cumulative = jnp.cumsum(log_decay, axis=0)
    keep_state = (segments == seg_before).astype(jnp.float32)
    entering = jnp.exp(cumulative) * keep_state[:, None]
    token_position = lax.iota(jnp.int32, positions)
    same_doc = segments[:, None] == segments[None, :]
    spread = cumulative.T[:, :, None] - cumulative.T[:, None, :]
    causal_decay = strict_decay + jnp.eye(positions, dtype=jnp.float32)[None]
    targets = jnp.concatenate(
        [keyset * (write_rate * entering)[:, :, None], values * write_rate[:, :, None]], axis=2
    )
    solved = jnp.einsum("hij,hjd->hid", inverse, targets.transpose(1, 0, 2), precision=FAST)
    write_keys = solved[:, :, :DK]
    write_values = solved[:, :, DK:]
    scores = jnp.einsum("ihd,jhd->hij", queries, keyset, precision=FAST) * causal_decay
    final_sum = cumulative[-1]
    tail_decay = (
        jnp.exp(final_sum[None, :] - cumulative)
        * (segments == segments[-1]).astype(jnp.float32)[:, None]
    )
    carried = jnp.exp(final_sum) * keep_state[-1]
    tail_keys = (keyset * tail_decay[:, :, None]).transpose(1, 0, 2)
    queried = (queries * entering[:, :, None]).transpose(1, 0, 2)
    return (write_keys, write_values, scores, tail_keys, queried, carried)


def block_map(block_data):
    write_keys, write_values, scores, tail_keys, queried, carried = block_data
    identity_matrix = jnp.eye(DK, dtype=jnp.float32)
    transform = carried[:, None, None] * identity_matrix[None] - jnp.einsum(
        "hcd,hce->hde", tail_keys, write_keys, precision=HIGHEST
    )
    shift_term = jnp.einsum("hcd,hce->hde", tail_keys, write_values, precision=HIGHEST)
    return (transform, shift_term)


def block_apply(block_data, state_in):
    write_keys, write_values, scores, tail_keys, queried, carried = block_data
    fresh_values = write_values - jnp.einsum(
        "hcd,hde->hce", write_keys, state_in, precision=HIGHEST
    )
    output = jnp.einsum("hcd,hde->hce", queried, state_in, precision=HIGHEST)
    output = output + jnp.einsum("hij,hje->hie", scores, fresh_values, precision=HIGHEST)
    state_next = carried[:, None, None] * state_in + jnp.einsum(
        "hcd,hce->hde", tail_keys, fresh_values, precision=HIGHEST
    )
    return (output, state_next)

def unit_lower_inverse_fast(strict_part):
    positions = strict_part.shape[-1]
    identity_matrix = jnp.eye(positions, dtype=jnp.float32)[None]
    result = identity_matrix - strict_part
    power = strict_part
    reach = 2
    while reach < positions:
        power = jnp.einsum("hij,hjk->hik", power, power, precision=HIGHEST)
        result = jnp.einsum("hij,hjk->hik", result, identity_matrix + power, precision=HIGHEST)
        reach = reach * 2
    return result


def block_map_fast(block_data):
    write_keys, write_values, scores, tail_keys, queried, carried = block_data
    identity_matrix = jnp.eye(DK, dtype=jnp.float32)
    transform = carried[:, None, None] * identity_matrix[None] - jnp.einsum(
        "hcd,hce->hde", tail_keys, write_keys, precision=FAST
    )
    shift_term = jnp.einsum("hcd,hce->hde", tail_keys, write_values, precision=FAST)
    return (transform, shift_term)


def block_apply_fast(block_data, state_in):
    write_keys, write_values, scores, tail_keys, queried, carried = block_data
    fresh_values = write_values - jnp.einsum(
        "hcd,hde->hce", write_keys, state_in, precision=FAST
    )
    output = jnp.einsum("hcd,hde->hce", queried, state_in, precision=FAST)
    output = output + jnp.einsum("hij,hje->hie", scores, fresh_values, precision=FAST)
    state_next = carried[:, None, None] * state_in + jnp.einsum(
        "hcd,hce->hde", tail_keys, fresh_values, precision=FAST
    )
    return (output, state_next)


def section_one(mix_ext, conv_weight, log_decay, write_rate, seg_ext):
    queries, keyset, values = prepare(mix_ext, seg_ext, conv_weight)
    margin = conv_weight.shape[0] - 1
    positions = log_decay.shape[0]
    blocks = positions // BLOCK
    segments = seg_ext[margin:]
    before = seg_ext[margin - 1 : margin - 1 + positions : BLOCK]

    def blocked(tensor):
        return tensor.reshape((blocks, BLOCK) + tensor.shape[1:])

    return jax.vmap(block_parts)(
        blocked(queries),
        blocked(keyset),
        blocked(values),
        blocked(log_decay),
        blocked(write_rate),
        blocked(segments),
        before,
    )


def section_two(parts, state_in):

    def step_block(state_now, block_data):
        output, state_next = block_apply(block_data, state_now)
        return (state_next, output)

    state_out, outputs = lax.scan(step_block, state_in, parts)
    blocks = outputs.shape[0]
    return (outputs.transpose(0, 2, 1, 3).reshape(blocks * BLOCK, HV * DV), state_out)


def summarize(parts):
    identity_matrix = jnp.eye(DK, dtype=jnp.float32)
    initial = (
        jnp.broadcast_to(identity_matrix, (HV, DK, DK)),
        jnp.zeros((HV, DK, DV), jnp.float32),
    )

    def fold_block(carried_map, block_data):
        transform, shift_term = block_map(block_data)
        merged = jnp.einsum("hij,hjk->hik", transform, carried_map[0], precision=HIGHEST)
        moved = (
            jnp.einsum("hij,hjk->hik", transform, carried_map[1], precision=HIGHEST) + shift_term
        )
        return ((merged, moved), None)

    result, unused = lax.scan(fold_block, initial, parts)
    return result


def compose(earlier_map, later_map):
    merged = jnp.einsum("shij,shjk->shik", later_map[0], earlier_map[0], precision=HIGHEST)
    moved = (
        jnp.einsum("shij,shjk->shik", later_map[0], earlier_map[1], precision=HIGHEST)
        + later_map[1]
    )
    return (merged, moved)


def local(mixed, conv_weight, log_decay, write_rate, segment_ids, cotangent):
    margin = conv_weight.shape[0] - 1
    shifted_rows, shifted_segs = from_behind(
        (mixed[:, -margin:, :], segment_ids[:, -margin:].astype(jnp.bfloat16)), "ctx", 1
    )
    mix_ext = jnp.concatenate([shifted_rows, mixed], axis=1).astype(jnp.float32)
    seg_ext = jnp.concatenate([shifted_segs.astype(jnp.int32), segment_ids], axis=1)

    def first_section(mix_in, weight_in, decay_in, rate_in):
        return jax.vmap(section_one, in_axes=(0, None, 0, 0, 0))(
            mix_in, weight_in, decay_in, rate_in, seg_ext
        )

    parts, first_pull = jax.vjp(first_section, mix_ext, conv_weight, log_decay, write_rate)
    transform, shift_term = jax.vmap(summarize)(parts)
    identity_pair = (
        jnp.broadcast_to(jnp.eye(transform.shape[-1], dtype=jnp.float32), transform.shape),
        jnp.zeros_like(shift_term),
    )
    incoming = prefix((transform, shift_term), "ctx", compose, identity_pair, False)[1]
    (outputs, leaving), second_pull = jax.vjp(jax.vmap(section_two), parts, incoming)
    part_grads, local_term = second_pull((cotangent.astype(jnp.float32), jnp.zeros_like(leaving)))
    flipped = jnp.swapaxes(transform, -1, -2)
    departing = prefix((flipped, local_term), "ctx", compose, identity_pair, True)[1]
    more_grads, unused_grad = second_pull((jnp.zeros_like(outputs), departing))
    total_parts = jax.tree.map(jnp.add, part_grads, more_grads)
    grad_mix, grad_weight, grad_decay, grad_rate = first_pull(total_parts)
    returned = from_behind(grad_mix[:, :margin, :].astype(jnp.bfloat16), "ctx", -1).astype(
        jnp.float32
    )
    own_grad = grad_mix[:, margin:, :]
    own_grad = jnp.concatenate(
        [own_grad[:, :-margin, :], own_grad[:, -margin:, :] + returned], axis=1
    )
    total_conv = lax.psum(grad_weight, ("dp", "ctx"))
    tokens_all = mixed.shape[0] * lax.axis_size("dp") * mixed.shape[1] * lax.axis_size("ctx")
    return (
        outputs.astype(jnp.bfloat16),
        own_grad.astype(jnp.bfloat16),
        grad_decay,
        grad_rate,
        total_conv / math.sqrt(tokens_all),
    )


def tree_sum(value, axis):
    count = lax.axis_size(axis)
    if count & (count - 1):
        return lax.psum(value, axis)
    step = 1
    while step < count:
        value = value + lax.ppermute(value, axis, [(i, i ^ step) for i in range(count)])
        step = step * 2
    return value


def prepare_heads(mix_ext, seg_ext, conv_weight, key_heads, value_heads):
    margin = conv_weight.shape[0] - 1
    positions = mix_ext.shape[0] - margin
    current = seg_ext[margin:]
    summed = jnp.zeros((positions, mix_ext.shape[1]), jnp.float32)
    for tap_index in range(margin + 1):
        same_doc = (seg_ext[tap_index : tap_index + positions] == current).astype(jnp.float32)
        summed = (
            summed
            + conv_weight[tap_index][None, :]
            * mix_ext[tap_index : tap_index + positions]
            * same_doc[:, None]
        )
    activated = jax.nn.silu(summed)
    split_at = key_heads * DK
    queries = activated[:, :split_at].reshape(positions, key_heads, DK)
    keyset = activated[:, split_at : 2 * split_at].reshape(positions, key_heads, DK)
    values = activated[:, 2 * split_at :].reshape(positions, value_heads, DV)
    queries = (
        queries
        / jnp.sqrt(jnp.sum(queries * queries, axis=-1, keepdims=True) + 1e-06)
        / math.sqrt(DK)
    )
    keyset = keyset / jnp.sqrt(jnp.sum(keyset * keyset, axis=-1, keepdims=True) + 1e-06)
    repeats = value_heads // key_heads
    return (jnp.repeat(queries, repeats, axis=1), jnp.repeat(keyset, repeats, axis=1), values)


def combine_maps(earlier, later):
    merged = jnp.einsum("...ij,...jk->...ik", later[0], earlier[0], precision=HIGHEST)
    moved = jnp.einsum("...ij,...jk->...ik", later[0], earlier[1], precision=HIGHEST) + later[1]
    return (merged, moved)


def inclusive_states(transform, shift_term):
    blocks = transform.shape[0]
    reach = 1
    while reach < blocks:
        moved = jnp.einsum(
            "bhij,bhjk->bhik", transform[reach:], shift_term[:-reach], precision=FAST
        )
        shift_term = jnp.concatenate([shift_term[:reach], shift_term[reach:] + moved], axis=0)
        if 2 * reach < blocks:
            merged = jnp.einsum(
                "bhij,bhjk->bhik", transform[reach:], transform[:-reach], precision=FAST
            )
            transform = jnp.concatenate([transform[:reach], merged], axis=0)
        reach = reach * 2
    return shift_term


@jax.custom_vjp
def entering_states(transform, shift_term):
    return entering_forward(transform, shift_term)[0]


def entering_forward(transform, shift_term):
    eye = jnp.broadcast_to(jnp.eye(transform.shape[-1], dtype=transform.dtype), transform[:1].shape)
    shifted_maps = jnp.concatenate([eye, transform[:-1]], axis=0)
    shifted_terms = jnp.concatenate([jnp.zeros_like(shift_term[:1]), shift_term[:-1]], axis=0)
    states = inclusive_states(shifted_maps, shifted_terms)
    return states, (transform, states)


def entering_backward(saved, grad_states):
    transform, states = saved
    flipped = jnp.swapaxes(transform, -1, -2)[::-1]
    total = inclusive_states(flipped, grad_states[::-1])[::-1]
    later = total[1:]
    grad_shift = jnp.concatenate([later, jnp.zeros_like(later[:1])], axis=0)
    grad_map = jnp.einsum("bhik,bhjk->bhij", later, states[:-1], precision=FAST)
    grad_transform = jnp.concatenate([grad_map, jnp.zeros_like(transform[:1])], axis=0)
    return (grad_transform, grad_shift)


entering_states.defvjp(entering_forward, entering_backward)


def states_kernel(maps_ref, terms_ref, out_ref):
    blocks = maps_ref.shape[0]
    dims = (((2,), (1,)), ((0,), (0,)))
    state = jnp.zeros(terms_ref.shape[1:], jnp.float32)
    out_ref[0] = state
    for index in range(blocks - 1):
        state = (
            lax.dot_general(
                maps_ref[index], state, dims, precision=FAST, preferred_element_type=jnp.float32
            )
            + terms_ref[index]
        )
        out_ref[index + 1] = state


def adjoint_kernel(flipped_ref, grads_ref, out_ref):
    blocks = flipped_ref.shape[0]
    dims = (((2,), (1,)), ((0,), (0,)))
    total = grads_ref[blocks - 1]
    out_ref[blocks - 1] = total
    for index in range(blocks - 2, -1, -1):
        total = grads_ref[index] + lax.dot_general(
            flipped_ref[index], total, dims, precision=FAST, preferred_element_type=jnp.float32
        )
        out_ref[index] = total


def run_chain(kernel, maps, terms):
    blocks, heads, size = maps.shape[0], maps.shape[1], maps.shape[2]
    return pl.pallas_call(
        kernel,
        out_shape=jax.ShapeDtypeStruct(terms.shape, jnp.float32),
        in_specs=[pl.BlockSpec(memory_space=pltpu.VMEM)] * 2,
        out_specs=pl.BlockSpec(memory_space=pltpu.VMEM),
        cost_estimate=pl.CostEstimate(
            flops=6 * 2 * blocks * heads * size * size * terms.shape[-1],
            transcendentals=0,
            bytes_accessed=4 * (maps.size + 2 * terms.size),
        ),
    )(maps, terms)


@jax.custom_vjp
def chain_states(transform, shift_term):
    return run_chain(states_kernel, transform, shift_term)


def chain_forward(transform, shift_term):
    states = run_chain(states_kernel, transform, shift_term)
    return states, (transform, states)


def chain_backward(saved, grad_states):
    transform, states = saved
    flipped = jnp.swapaxes(transform, -1, -2)
    total = run_chain(adjoint_kernel, flipped, grad_states)
    later = total[1:]
    grad_shift = jnp.concatenate([later, jnp.zeros_like(later[:1])], axis=0)
    grad_map = jnp.einsum("bhik,bhjk->bhij", later, states[:-1], precision=FAST)
    grad_transform = jnp.concatenate([grad_map, jnp.zeros_like(transform[:1])], axis=0)
    return (grad_transform, grad_shift)


chain_states.defvjp(chain_forward, chain_backward)


def heads_forward(mix_in, weight_in, decay_in, rate_in, seg_ext, key_heads, value_heads):
    margin = weight_in.shape[0] - 1
    positions = decay_in.shape[0]
    blocks = positions // BLOCK
    mix_ext = jnp.concatenate([jnp.zeros((margin, mix_in.shape[1]), jnp.float32), mix_in], axis=0)
    queries, keyset, values = prepare_heads(mix_ext, seg_ext, weight_in, key_heads, value_heads)
    segments = seg_ext[margin:]
    before = seg_ext[margin - 1 : margin - 1 + positions : BLOCK]

    def blocked(tensor):
        return tensor.reshape((blocks, BLOCK) + tensor.shape[1:])

    system, strict_decay = jax.vmap(block_system)(
        blocked(keyset), blocked(decay_in), blocked(rate_in), blocked(segments)
    )
    inverse = batch_inverse(system.reshape((-1,) + system.shape[2:])).reshape(system.shape)
    parts = jax.vmap(block_rest)(
        inverse,
        strict_decay,
        blocked(queries),
        blocked(keyset),
        blocked(values),
        blocked(decay_in),
        blocked(rate_in),
        blocked(segments),
        before,
    )
    transform, shift_term = jax.vmap(block_map_fast)(parts)
    incoming = chain_states(transform, shift_term)
    outputs, unused = jax.vmap(block_apply_fast)(parts, incoming)
    return outputs.transpose(0, 2, 1, 3).reshape(positions, value_heads * DV)


def heads_local(mixed, conv_weight, log_decay, write_rate, segment_ids, cotangent):
    if mixed.shape[0] != 1:
        return local(mixed, conv_weight, log_decay, write_rate, segment_ids, cotangent)
    count = lax.axis_size("ctx")
    mine = lax.axis_index("ctx")
    value_heads = HV // count
    key_heads = value_heads * HK // HV
    margin = conv_weight.shape[0] - 1
    rows = mixed.shape[1]
    length = rows * count
    qk_width = key_heads * DK
    v_width = value_heads * DV

    def to_heads(array, width):
        grouped = array.reshape(rows, count, width)
        return lax.all_to_all(grouped, "ctx", 1, 0, tiled=True).reshape(length, width)

    def to_rows(array, width):
        grouped = array.reshape(count, rows, 1, width)
        return lax.all_to_all(grouped, "ctx", 0, 2, tiled=True).reshape(rows, count, width)

    own = mixed[0]
    width = 2 * qk_width + v_width
    packed = jnp.concatenate(
        [
            own[:, : HK * DK].reshape(rows, count, qk_width),
            own[:, HK * DK : 2 * HK * DK].reshape(rows, count, qk_width),
            own[:, 2 * HK * DK :].reshape(rows, count, v_width),
            cotangent[0].reshape(rows, count, v_width),
        ],
        axis=-1,
    )
    wide = to_heads(packed, width + v_width)
    mix_heads = wide[:, :width].astype(jnp.float32)
    cot_heads = wide[:, width:].astype(jnp.float32)
    seg_columns = jnp.broadcast_to(
        segment_ids[0].astype(jnp.float32)[:, None, None], (rows, count, 1)
    )
    small = jnp.concatenate(
        [
            log_decay[0].reshape(rows, count, value_heads),
            write_rate[0].reshape(rows, count, value_heads),
            seg_columns,
        ],
        axis=-1,
    )
    narrow = to_heads(small, 2 * value_heads + 1)
    decay_heads = narrow[:, :value_heads]
    rate_heads = narrow[:, value_heads : 2 * value_heads]
    segments = narrow[:, 2 * value_heads].astype(jnp.int32)
    seg_ext = jnp.concatenate([jnp.full((margin,), -1, jnp.int32), segments])

    weight_q = conv_weight[:, : HK * DK].reshape(-1, count, qk_width)[:, mine]
    weight_k = conv_weight[:, HK * DK : 2 * HK * DK].reshape(-1, count, qk_width)[:, mine]
    weight_v = conv_weight[:, 2 * HK * DK :].reshape(-1, count, v_width)[:, mine]
    weight_heads = jnp.concatenate([weight_q, weight_k, weight_v], axis=-1)

    def forward(mix_in, weight_in, decay_in, rate_in):
        return heads_forward(
            mix_in, weight_in, decay_in, rate_in, seg_ext, key_heads, value_heads
        )

    outputs, pullback = jax.vjp(forward, mix_heads, weight_heads, decay_heads, rate_heads)
    grad_mix, grad_weight, grad_decay, grad_rate = pullback(cot_heads)

    joined = jnp.concatenate([outputs.astype(jnp.bfloat16), grad_mix.astype(jnp.bfloat16)], axis=-1)
    back = to_rows(joined, v_width + width)
    core = back[:, :, :v_width].reshape(1, rows, HV * DV)
    grad_rows = jnp.concatenate(
        [
            back[:, :, v_width : v_width + qk_width].reshape(rows, HK * DK),
            back[:, :, v_width + qk_width : v_width + 2 * qk_width].reshape(rows, HK * DK),
            back[:, :, v_width + 2 * qk_width :].reshape(rows, HV * DV),
        ],
        axis=-1,
    )[None]
    taps = conv_weight.shape[0]
    sequences = lax.axis_size("dp")
    mine_dp = lax.axis_index("dp")
    row_grads = jnp.concatenate([grad_decay, grad_rate], axis=-1).reshape(count, rows * 2 * value_heads)
    pieces = jnp.concatenate(
        [
            jnp.broadcast_to(row_grads[None], (sequences,) + row_grads.shape),
            jnp.broadcast_to(
                grad_weight.reshape(1, 1, taps * width), (sequences, count, taps * width)
            ),
        ],
        axis=-1,
    ).reshape(sequences * count, 1, rows * 2 * value_heads + taps * width)
    everything = lax.all_to_all(pieces, ("dp", "ctx"), 0, 1, tiled=True)[0]
    everything = everything.reshape(sequences, count, rows * 2 * value_heads + taps * width)
    weight_sum = everything[0, :, rows * 2 * value_heads :]
    for index in range(1, sequences):
        weight_sum = weight_sum + everything[index, :, rows * 2 * value_heads :]
    returned = jnp.concatenate(
        [lax.dynamic_index_in_dim(everything, mine_dp, 0, keepdims=False)[:, : rows * 2 * value_heads], weight_sum],
        axis=-1,
    )
    grads_small = returned[:, : rows * 2 * value_heads].reshape(count, rows, 2 * value_heads)
    grads_small = grads_small.transpose(1, 0, 2)
    decay_rows = grads_small[:, :, :value_heads].reshape(1, rows, HV)
    rate_rows = grads_small[:, :, value_heads:].reshape(1, rows, HV)
    conv_parts = returned[:, rows * 2 * value_heads :].reshape(count, taps, width).transpose(1, 0, 2)
    total_conv = jnp.concatenate(
        [
            conv_parts[:, :, :qk_width].reshape(taps, HK * DK),
            conv_parts[:, :, qk_width : 2 * qk_width].reshape(taps, HK * DK),
            conv_parts[:, :, 2 * qk_width :].reshape(taps, HV * DV),
        ],
        axis=-1,
    )
    tokens_all = mixed.shape[0] * sequences * length
    return (core, grad_rows, decay_rows, rate_rows, total_conv / math.sqrt(tokens_all))


def solution(mesh):
    in_specs = (
        P("dp", "ctx", None),
        P(),
        P("dp", "ctx", None),
        P("dp", "ctx", None),
        P("dp", "ctx"),
        P("dp", "ctx", None),
    )
    out_specs = (
        P("dp", "ctx", None),
        P("dp", "ctx", None),
        P("dp", "ctx", None),
        P("dp", "ctx", None),
        P(),
    )
    count = mesh.shape["ctx"]
    per_device = HV // count if HV % count == 0 else 0
    chosen = heads_local if per_device and (per_device * HK) % HV == 0 else local
    return jax.shard_map(chosen, mesh=mesh, in_specs=in_specs, out_specs=out_specs, check_vma=False)
```
